128 devices in a mesh: gx: 16 (over y, z_lo, core), gy: 2 (over z_hi), gz: 4 (over x).
Axes of the slice: x: 4, y: 4, z: 4 (z_hi: 2, z_lo: 2; z = z_hi * 2 + z_lo), core: 2. Of those that a mesh axis runs over, the one named last changes fastest.
Arguments:
- check_pops: float32 [27, 64, 32, 512], P(None, 'gx', 'gy', 'gz'), as said below
- adjoint_end: float32 [27, 64, 32, 512], P(None, 'gx', 'gy', 'gz'), may hold values from -6 to 6
- relax_rate: float32 [64, 32, 512], P('gx', 'gy', 'gz'), may hold values from 0.6 to 1.7
- wall_flag: int32 [64, 32, 512], P('gx', 'gy', 'gz'), may hold values from 0 to 1
- patch_of_cell: int32 [64, 32, 512], P('gx', 'gy', 'gz'), may hold values from 0 to 1023, as said below
- porosity: float32 [1024], replicated, may hold values from 0.1 to 0.9
- patch_slot: int32 [1024], replicated, may hold values from 0 to 1023, each once
Outputs:
- adjoint_start: float32 [27, 64, 32, 512], P(None, 'gx', 'gy', 'gz')
- patch_sens: float32 [1024], P(('gx', 'gy', 'gz'))
The draws below stay inside these ranges and needn't reach their ends.
Inputs may be any that keep to these rules, and one draw needn't show every extreme that they name: `patch_of_cell`: the cells of one patch form one box of 2 x 16/2 x 128/2 cells, boxes shifted by 1 cells along the first dimension (periodically); every patch id is used. `check_pops`: all populations are positive.
All inputs are finite; a program needn't handle non-finite values.
Results may differ from the reference program's by a relative error of at most 0.0003.
Values sent between devices are 32-bit elements; how exact they have to be, the bound alone decides.
No kernel may reach another device: no remote copies, remote signals or barrier semaphores. Data moves between devices by JAX's collectives and lax.ppermute only.
A program may use at most 64 MiB of HBM per device.

```python
import jax
import jax.numpy as jnp
import numpy as np
from jax import lax

BX = 4
BY = 16
BZ = 128
POPS = 27
NX = 64
NY = 32
NZ = 512
PATCHES = 1024


def lattice_weights():
    steps = np.array([[first, second, third] for first in (-1, 0, 1) for second in (-1, 0, 1) for third in (-1, 0, 1)], dtype=np.int64)
    moved = np.abs(steps).sum(axis=1)
    weights = np.array([8.0 / 27.0, 2.0 / 27.0, 1.0 / 54.0, 1.0 / 216.0])[moved]
    return (steps, weights)


def draw_check_pops(key, part):
    keys = jax.random.split(jax.random.fold_in(key, 11), 3)
    steps, weights = lattice_weights()
    density = 1.0 + 0.05 * jax.random.normal(keys[0], (NX, NY, NZ), jnp.float32)
    flow = 0.05 * jax.random.normal(keys[1], (3, NX, NY, NZ), jnp.float32)
    noise = jax.random.uniform(keys[2], (27, NX, NY, NZ), jnp.float32, -0.2, 0.2)
    cx = jnp.asarray(steps[:, 0], jnp.float32)[:, None, None, None]
    cy = jnp.asarray(steps[:, 1], jnp.float32)[:, None, None, None]
    cz = jnp.asarray(steps[:, 2], jnp.float32)[:, None, None, None]
    wts = jnp.asarray(weights, jnp.float32)[:, None, None, None]
    along = cx * flow[0] + cy * flow[1] + cz * flow[2]
    speed = flow[0] * flow[0] + flow[1] * flow[1] + flow[2] * flow[2]
    equil = wts * density * (1.0 + 3.0 * along + 4.5 * along * along - 1.5 * speed)
    return equil * (1.0 + noise)


def draw_wall_flag(key, part):
    rows = jax.lax.broadcasted_iota(jnp.int32, (NX, NY, NZ), 1)
    picks = jax.random.randint(jax.random.fold_in(key, 23), (NX, NY, NZ), 0, NY)
    return (picks <= rows).astype(jnp.int32)


def draw_patch_of_cell(key, part):
    first = jax.lax.broadcasted_iota(jnp.int32, (NX, NY, NZ), 0)
    second = jax.lax.broadcasted_iota(jnp.int32, (NX, NY, NZ), 1)
    third = jax.lax.broadcasted_iota(jnp.int32, (NX, NY, NZ), 2)
    tiles_x = NX // (BX // 2)
    tiles_y = NY // (BY // 2)
    tiles_z = NZ // (BZ // 2)
    tile_x = (first + BX // 4) // (BX // 2) % tiles_x
    tile_y = second // (BY // 2)
    tile_z = third // (BZ // 2)
    tile = (tile_x * tiles_y + tile_y) * tiles_z + tile_z
    labels = jax.random.permutation(jax.random.fold_in(key, 37), PATCHES).astype(jnp.int32)
    return labels[tile]


def steps_of(rng, shape, pieces, least, largest):
    factor_of, own = 1.0, jax.random.fold_in(rng, 6)
    for dim, shards_of in pieces:
        heights = jnp.exp(jax.random.uniform(jax.random.fold_in(own, dim), (shards_of,), jnp.float32, least / len(pieces), largest / len(pieces)))
        factor_of = factor_of * jnp.repeat(heights, shape[dim] // shards_of).reshape([-1 if axis == dim else 1 for axis in range(len(shape))])
    return factor_of


def bell_draw(stream_key, extent, scale, most, cuts=(), kind=jnp.bfloat16):
    values = scale * jax.random.normal(stream_key, extent, jnp.float32)
    if cuts:
        values = values * steps_of(stream_key, extent, cuts, -0.22, 0.18)
    return jnp.clip(values, -most, most).astype(kind)


def setup_inputs(seed: int = 0) -> dict:
    key_of = jax.random.split(jax.random.key(seed), 8)
    return {
        "check_pops": draw_check_pops(jax.random.fold_in(key_of[7], 71), 0),
        "adjoint_end": bell_draw(key_of[1], (POPS, NX, NY, NZ), 1.0, 6.0, ((1, 16), (2, 2), (3, 4)), jnp.float32),
        "relax_rate": jnp.clip(0.6 + 1.1 * jax.random.uniform(key_of[2], (NX, NY, NZ), jnp.float32) ** steps_of(key_of[2], (NX, NY, NZ), ((0, 16), (1, 2), (2, 4)), -0.2, 0.2), 0.6, 1.7),
        "wall_flag": draw_wall_flag(jax.random.fold_in(key_of[7], 71), 0),
        "patch_of_cell": draw_patch_of_cell(jax.random.fold_in(key_of[7], 71), 0),
        "porosity": jnp.clip(jax.random.uniform(key_of[5], (PATCHES,), jnp.float32, 0.1, 0.9), 0.1, 0.9),
        "patch_slot": jax.random.permutation(key_of[6], PATCHES).astype(jnp.int32),
    }


def lattice_table():
    steps = np.array([[first, second, third] for first in (-1, 0, 1) for second in (-1, 0, 1) for third in (-1, 0, 1)], dtype=np.int64)
    moved = np.abs(steps).sum(axis=1)
    weights = np.array([8.0 / 27.0, 2.0 / 27.0, 1.0 / 54.0, 1.0 / 216.0])[moved]
    return (steps, weights)

def collide(pops, rate, gamma):
    steps, weights = lattice_table()
    cube = pops.reshape((3, 3, 3) + pops.shape[1:])
    density = lax.optimization_barrier(jnp.sum(pops, axis=0))
    mom_x = lax.optimization_barrier(jnp.sum(cube[2], axis=(0, 1))) - lax.optimization_barrier(jnp.sum(cube[0], axis=(0, 1)))
    mom_y = lax.optimization_barrier(jnp.sum(cube[:, 2], axis=(0, 1))) - lax.optimization_barrier(jnp.sum(cube[:, 0], axis=(0, 1)))
    mom_z = lax.optimization_barrier(jnp.sum(cube[:, :, 2], axis=(0, 1))) - lax.optimization_barrier(jnp.sum(cube[:, :, 0], axis=(0, 1)))
    vel_x = mom_x / density
    vel_y = mom_y / density
    vel_z = mom_z / density
    cx = jnp.asarray(steps[:, 0], jnp.float32)[:, None, None, None]
    cy = jnp.asarray(steps[:, 1], jnp.float32)[:, None, None, None]
    cz = jnp.asarray(steps[:, 2], jnp.float32)[:, None, None, None]
    wts = jnp.asarray(weights, jnp.float32)[:, None, None, None]
    along = cx * vel_x + cy * vel_y + cz * vel_z
    speed = vel_x * vel_x + vel_y * vel_y + vel_z * vel_z
    equil = wts * density * (1.0 + 3.0 * along + 4.5 * along * along - 1.5 * speed)
    relaxed = pops - rate * (pops - equil)
    flipped = pops[::-1]
    return ((1.0 - gamma) * relaxed + gamma * flipped, flipped - relaxed)

def adjoint_collide(pops, rate, gamma, adj_post):

    def forward(values):
        return collide(values, rate, gamma)
    post, pullback, deriv = jax.vjp(forward, pops, has_aux=True)
    adj_pre, = pullback(adj_post)
    return (adj_pre, lax.optimization_barrier(jnp.sum(adj_post * deriv, axis=0)))

def stream(pops, sign):
    steps, _ = lattice_table()
    moved = []
    for index in range(27):
        offset = (int(sign * steps[index, 0]), int(sign * steps[index, 1]), int(sign * steps[index, 2]))
        moved.append(jnp.roll(pops[index], offset, axis=(0, 1, 2)))
    return jnp.stack(moved, 0)

def reference(check_pops, adjoint_end, relax_rate, wall_flag, patch_of_cell, porosity, patch_slot):
    walls = wall_flag.astype(jnp.float32)
    gamma = walls * porosity[patch_of_cell]
    post_now, _ = collide(check_pops, relax_rate, gamma)
    pops_next = stream(post_now, 1)
    post_adj_next = stream(adjoint_end, -1)
    adj_next, sens_next = adjoint_collide(pops_next, relax_rate, gamma, post_adj_next)
    post_adj = stream(adj_next, -1)
    adjoint_start, sens_now = adjoint_collide(check_pops, relax_rate, gamma, post_adj)
    density = walls * (sens_next + sens_now)
    totals = jax.ops.segment_sum(density.reshape(-1), patch_of_cell.reshape(-1).astype(jnp.int32), num_segments=PATCHES)
    patch_sens = jnp.zeros((PATCHES,), jnp.float32).at[patch_slot].set(totals)
    return (adjoint_start, patch_sens)
```

```python
import jax
import jax.numpy as jnp
import numpy as np
from jax import lax
from jax.sharding import PartitionSpec as P


def lattice_table():
    steps = np.array(
        [
            [first, second, third]
            for first in (-1, 0, 1)
            for second in (-1, 0, 1)
            for third in (-1, 0, 1)
        ],
        dtype=np.int64,
    )
    moved = np.abs(steps).sum(axis=1)
    weights = np.array([8.0 / 27.0, 2.0 / 27.0, 1.0 / 54.0, 1.0 / 216.0])[moved]
    return (steps, weights)


def collide(pops, rate, gamma):
    steps, weights = lattice_table()
    cube = pops.reshape((3, 3, 3) + pops.shape[1:])
    density = jnp.sum(pops, axis=0)
    mom_x = jnp.sum(cube[2], axis=(0, 1)) - jnp.sum(cube[0], axis=(0, 1))
    mom_y = jnp.sum(cube[:, 2], axis=(0, 1)) - jnp.sum(cube[:, 0], axis=(0, 1))
    mom_z = jnp.sum(cube[:, :, 2], axis=(0, 1)) - jnp.sum(cube[:, :, 0], axis=(0, 1))
    vel_x = mom_x / density
    vel_y = mom_y / density
    vel_z = mom_z / density
    cx = jnp.asarray(steps[:, 0], jnp.float32)[:, None, None, None]
    cy = jnp.asarray(steps[:, 1], jnp.float32)[:, None, None, None]
    cz = jnp.asarray(steps[:, 2], jnp.float32)[:, None, None, None]
    wts = jnp.asarray(weights, jnp.float32)[:, None, None, None]
    along = cx * vel_x + cy * vel_y + cz * vel_z
    speed = vel_x * vel_x + vel_y * vel_y + vel_z * vel_z
    equil = wts * density * (1.0 + 3.0 * along + 4.5 * along * along - 1.5 * speed)
    relaxed = pops - rate * (pops - equil)
    flipped = pops[::-1]
    return ((1.0 - gamma) * relaxed + gamma * flipped, flipped - relaxed)


def adjoint_collide(pops, rate, gamma, adj_post):

    def forward(values):
        return collide(values, rate, gamma)

    post, pullback, deriv = jax.vjp(forward, pops, has_aux=True)
    (adj_pre,) = pullback(adj_post)
    return (adj_pre, jnp.sum(adj_post * deriv, axis=0))


def halo_exchange(up, down, axis):
    size = lax.axis_size(axis)
    if size == 1:
        return up, down
    if size == 2:
        both = lax.ppermute(jnp.stack([up, down]), axis, [(0, 1), (1, 0)])
        return both[0], both[1]
    lo = lax.ppermute(up, axis, [(i, (i + 1) % size) for i in range(size)])
    hi = lax.ppermute(down, axis, [(i, (i - 1) % size) for i in range(size)])
    return lo, hi


def move_axis(cubes, signs, axis, d):
    n = cubes[0].shape[3 + d]
    ups, downs = [], []
    for cube, sign in zip(cubes, signs):
        plus = lax.index_in_dim(cube, 1 + sign, axis=d, keepdims=False)
        minus = lax.index_in_dim(cube, 1 - sign, axis=d, keepdims=False)
        ups.append(lax.slice_in_dim(plus, n - 1, n, axis=2 + d))
        downs.append(lax.slice_in_dim(minus, 0, 1, axis=2 + d))
    lo, hi = halo_exchange(jnp.stack(ups), jnp.stack(downs), axis)
    out = []
    for k, (cube, sign) in enumerate(zip(cubes, signs)):
        plus = lax.index_in_dim(cube, 1 + sign, axis=d, keepdims=False)
        minus = lax.index_in_dim(cube, 1 - sign, axis=d, keepdims=False)
        still = lax.index_in_dim(cube, 1, axis=d, keepdims=False)
        plus = jnp.concatenate([lo[k], lax.slice_in_dim(plus, 0, n - 1, axis=2 + d)], axis=2 + d)
        minus = jnp.concatenate([lax.slice_in_dim(minus, 1, n, axis=2 + d), hi[k]], axis=2 + d)
        groups = [None, still, None]
        groups[1 + sign] = plus
        groups[1 - sign] = minus
        out.append(jnp.stack(groups, axis=d))
    return out


def propagate(fields, signs):
    cubes = [field.reshape((3, 3, 3) + field.shape[1:]) for field in fields]
    for d, axis in enumerate(("gx", "gy", "gz")):
        cubes = move_axis(cubes, signs, axis, d)
    return [cube.reshape(field.shape) for cube, field in zip(cubes, fields)]


def shards(check_pops, adjoint_end, relax_rate, wall_flag, patch_of_cell, porosity, patch_slot):
    sx, sy, sz = relax_rate.shape
    rows = np.array([0, 1, sx - 1])
    row_of = np.array([0] + [1] * (sx - 2) + [2])
    ids = patch_of_cell[rows][:, np.array([0, sy // 2])][:, :, np.array([0, sz // 2])]
    solid = porosity[ids][row_of]
    solid = jnp.broadcast_to(solid[:, :, None, :, None], (sx, 2, sy // 2, 2, sz // 2)).reshape(sx, sy, sz)
    walls = wall_flag.astype(jnp.float32)
    gamma = walls * solid
    post_now, _ = collide(check_pops, relax_rate, gamma)
    pops_next, post_adj_next = propagate([post_now, adjoint_end], [1, -1])
    adj_next, sens_next = adjoint_collide(pops_next, relax_rate, gamma, post_adj_next)
    (post_adj,) = propagate([adj_next], [-1])
    adjoint_start, sens_now = adjoint_collide(check_pops, relax_rate, gamma, post_adj)
    density = walls * (sens_next + sens_now)
    boxes = density.reshape(sx, 2, sy // 2, 2, sz // 2).sum(axis=(2, 4))
    parts = jnp.stack([boxes[0], boxes[1 : sx - 1].sum(axis=0), boxes[sx - 1]])
    count = porosity.shape[0]
    devices = lax.axis_size(("gx", "gy", "gz"))
    slots = patch_slot[ids].reshape(-1)
    hits = (slots[:, None] == jnp.arange(count, dtype=slots.dtype)[None, :]).astype(jnp.float32)
    placed = jnp.sum(parts.reshape(-1)[:, None] * hits, axis=0)
    got = lax.all_to_all(placed.reshape(devices, count // devices), ("gx", "gy", "gz"), 0, 0, tiled=True)
    patch_sens = jnp.sum(got, axis=0)
    return (adjoint_start, patch_sens)


def solution(mesh):
    in_specs = (
        P(None, "gx", "gy", "gz"),
        P(None, "gx", "gy", "gz"),
        P("gx", "gy", "gz"),
        P("gx", "gy", "gz"),
        P("gx", "gy", "gz"),
        P(),
        P(),
    )
    out_specs = (P(None, "gx", "gy", "gz"), P(("gx", "gy", "gz")))
    return jax.shard_map(shards, mesh=mesh, in_specs=in_specs, out_specs=out_specs, check_vma=False)
```

```python
import jax
import jax.numpy as jnp
import numpy as np
from jax import lax
from jax.sharding import PartitionSpec as P


def lattice_table():
    steps = np.array(
        [
            [first, second, third]
            for first in (-1, 0, 1)
            for second in (-1, 0, 1)
            for third in (-1, 0, 1)
        ],
        dtype=np.int64,
    )
    moved = np.abs(steps).sum(axis=1)
    weights = np.array([8.0 / 27.0, 2.0 / 27.0, 1.0 / 54.0, 1.0 / 216.0])[moved]
    return (steps, weights)


def collide(pops, rate, gamma):
    steps, weights = lattice_table()
    cube = pops.reshape((3, 3, 3) + pops.shape[1:])
    density = jnp.sum(pops, axis=0)
    mom_x = jnp.sum(cube[2], axis=(0, 1)) - jnp.sum(cube[0], axis=(0, 1))
    mom_y = jnp.sum(cube[:, 2], axis=(0, 1)) - jnp.sum(cube[:, 0], axis=(0, 1))
    mom_z = jnp.sum(cube[:, :, 2], axis=(0, 1)) - jnp.sum(cube[:, :, 0], axis=(0, 1))
    vel_x = mom_x / density
    vel_y = mom_y / density
    vel_z = mom_z / density
    cx = jnp.asarray(steps[:, 0], jnp.float32)[:, None, None, None]
    cy = jnp.asarray(steps[:, 1], jnp.float32)[:, None, None, None]
    cz = jnp.asarray(steps[:, 2], jnp.float32)[:, None, None, None]
    wts = jnp.asarray(weights, jnp.float32)[:, None, None, None]
    along = cx * vel_x + cy * vel_y + cz * vel_z
    speed = vel_x * vel_x + vel_y * vel_y + vel_z * vel_z
    equil = wts * density * (1.0 + 3.0 * along + 4.5 * along * along - 1.5 * speed)
    relaxed = pops - rate * (pops - equil)
    flipped = pops[::-1]
    return ((1.0 - gamma) * relaxed + gamma * flipped, flipped - relaxed)


def adjoint_collide(pops, rate, gamma, adj_post):

    def forward(values):
        return collide(values, rate, gamma)

    post, pullback, deriv = jax.vjp(forward, pops, has_aux=True)
    (adj_pre,) = pullback(adj_post)
    return (adj_pre, jnp.sum(adj_post * deriv, axis=0))


def halo_exchange(up, down, axis):
    size = lax.axis_size(axis)
    if size == 1:
        return up, down
    if size == 2:
        both = lax.ppermute(jnp.stack([up, down]), axis, [(0, 1), (1, 0)])
        return both[0], both[1]
    lo = lax.ppermute(up, axis, [(i, (i + 1) % size) for i in range(size)])
    hi = lax.ppermute(down, axis, [(i, (i - 1) % size) for i in range(size)])
    return lo, hi


def move_axis(cubes, signs, axis, d):
    n = cubes[0].shape[3 + d]
    ups, downs = [], []
    for cube, sign in zip(cubes, signs):
        plus = lax.index_in_dim(cube, 1 + sign, axis=d, keepdims=False)
        minus = lax.index_in_dim(cube, 1 - sign, axis=d, keepdims=False)
        ups.append(lax.slice_in_dim(plus, n - 1, n, axis=2 + d))
        downs.append(lax.slice_in_dim(minus, 0, 1, axis=2 + d))
    lo, hi = halo_exchange(jnp.stack(ups), jnp.stack(downs), axis)
    out = []
    for k, (cube, sign) in enumerate(zip(cubes, signs)):
        plus = lax.index_in_dim(cube, 1 + sign, axis=d, keepdims=False)
        minus = lax.index_in_dim(cube, 1 - sign, axis=d, keepdims=False)
        still = lax.index_in_dim(cube, 1, axis=d, keepdims=False)
        plus = jnp.concatenate([lo[k], lax.slice_in_dim(plus, 0, n - 1, axis=2 + d)], axis=2 + d)
        minus = jnp.concatenate([lax.slice_in_dim(minus, 1, n, axis=2 + d), hi[k]], axis=2 + d)
        groups = [None, still, None]
        groups[1 + sign] = plus
        groups[1 - sign] = minus
        out.append(jnp.stack(groups, axis=d))
    return out


def propagate(fields, signs):
    cubes = [field.reshape((3, 3, 3) + field.shape[1:]) for field in fields]
    for d, axis in enumerate(("gx", "gy", "gz")):
        cubes = move_axis(cubes, signs, axis, d)
    return [cube.reshape(field.shape) for cube, field in zip(cubes, fields)]


def shards(check_pops, adjoint_end, relax_rate, wall_flag, patch_of_cell, porosity, patch_slot):
    sx, sy, sz = relax_rate.shape
    ids = patch_of_cell[:, :: sy // 2, :: sz // 2]
    table = jnp.stack([porosity, patch_slot.astype(jnp.float32)], axis=1)
    looked = table[ids]
    solid = jnp.broadcast_to(looked[:, :, None, :, None, 0], (sx, 2, sy // 2, 2, sz // 2)).reshape(sx, sy, sz)
    walls = wall_flag.astype(jnp.float32)
    gamma = walls * solid
    post_now, _ = collide(check_pops, relax_rate, gamma)
    pops_next, post_adj_next = propagate([post_now, adjoint_end], [1, -1])
    adj_next, sens_next = adjoint_collide(pops_next, relax_rate, gamma, post_adj_next)
    (post_adj,) = propagate([adj_next], [-1])
    adjoint_start, sens_now = adjoint_collide(check_pops, relax_rate, gamma, post_adj)
    density = walls * (sens_next + sens_now)
    boxes = density.reshape(sx, 2, sy // 2, 2, sz // 2).sum(axis=(2, 4))
    parts = jnp.stack([boxes[0], boxes[1 : sx - 1].sum(axis=0), boxes[sx - 1]])
    count = porosity.shape[0]
    devices = lax.axis_size(("gx", "gy", "gz"))
    slots = jnp.stack([looked[0, :, :, 1], looked[1, :, :, 1], looked[sx - 1, :, :, 1]]).reshape(-1)
    hits = (slots[:, None] == jnp.arange(count, dtype=jnp.float32)[None, :]).astype(jnp.float32)
    placed = jnp.sum(parts.reshape(-1)[:, None] * hits, axis=0)
    got = lax.all_to_all(placed.reshape(devices, count // devices), ("gx", "gy", "gz"), 0, 0, tiled=True)
    patch_sens = jnp.sum(got, axis=0)
    return (adjoint_start, patch_sens)


def solution(mesh):
    in_specs = (
        P(None, "gx", "gy", "gz"),
        P(None, "gx", "gy", "gz"),
        P("gx", "gy", "gz"),
        P("gx", "gy", "gz"),
        P("gx", "gy", "gz"),
        P(),
        P(),
    )
    out_specs = (P(None, "gx", "gy", "gz"), P(("gx", "gy", "gz")))
    return jax.shard_map(shards, mesh=mesh, in_specs=in_specs, out_specs=out_specs, check_vma=False)
```

```python
import jax
import jax.numpy as jnp
import numpy as np
from jax import lax
from jax.experimental import pallas as pl
from jax.experimental.pallas import tpu as pltpu
from jax.sharding import PartitionSpec as P


def lattice_table():
    steps = np.array(
        [
            [first, second, third]
            for first in (-1, 0, 1)
            for second in (-1, 0, 1)
            for third in (-1, 0, 1)
        ],
        dtype=np.int64,
    )
    moved = np.abs(steps).sum(axis=1)
    weights = np.array([8.0 / 27.0, 2.0 / 27.0, 1.0 / 54.0, 1.0 / 216.0])[moved]
    return (steps, weights)


STEPS, WEIGHTS = lattice_table()


def collide(pops, rate, gamma):
    steps, weights = lattice_table()
    cube = pops.reshape((3, 3, 3) + pops.shape[1:])
    density = jnp.sum(pops, axis=0)
    mom_x = jnp.sum(cube[2], axis=(0, 1)) - jnp.sum(cube[0], axis=(0, 1))
    mom_y = jnp.sum(cube[:, 2], axis=(0, 1)) - jnp.sum(cube[:, 0], axis=(0, 1))
    mom_z = jnp.sum(cube[:, :, 2], axis=(0, 1)) - jnp.sum(cube[:, :, 0], axis=(0, 1))
    vel_x = mom_x / density
    vel_y = mom_y / density
    vel_z = mom_z / density
    cx = jnp.asarray(steps[:, 0], jnp.float32)[:, None, None, None]
    cy = jnp.asarray(steps[:, 1], jnp.float32)[:, None, None, None]
    cz = jnp.asarray(steps[:, 2], jnp.float32)[:, None, None, None]
    wts = jnp.asarray(weights, jnp.float32)[:, None, None, None]
    along = cx * vel_x + cy * vel_y + cz * vel_z
    speed = vel_x * vel_x + vel_y * vel_y + vel_z * vel_z
    equil = wts * density * (1.0 + 3.0 * along + 4.5 * along * along - 1.5 * speed)
    relaxed = pops - rate * (pops - equil)
    flipped = pops[::-1]
    return ((1.0 - gamma) * relaxed + gamma * flipped, flipped - relaxed)


def halo_exchange(up, down, axis):
    size = lax.axis_size(axis)
    if size == 1:
        return up, down
    if size == 2:
        both = lax.ppermute(jnp.stack([up, down]), axis, [(0, 1), (1, 0)])
        return both[0], both[1]
    lo = lax.ppermute(up, axis, [(i, (i + 1) % size) for i in range(size)])
    hi = lax.ppermute(down, axis, [(i, (i - 1) % size) for i in range(size)])
    return lo, hi


def shifted(cube, lo, hi, d, sign):
    n = cube.shape[3 + d]
    plus = lax.index_in_dim(cube, 1 + sign, axis=d, keepdims=False)
    minus = lax.index_in_dim(cube, 1 - sign, axis=d, keepdims=False)
    still = lax.index_in_dim(cube, 1, axis=d, keepdims=False)
    plus = jnp.concatenate([lo, lax.slice_in_dim(plus, 0, n - 1, axis=2 + d)], axis=2 + d)
    minus = jnp.concatenate([lax.slice_in_dim(minus, 1, n, axis=2 + d), hi], axis=2 + d)
    groups = [None, still, None]
    groups[1 + sign] = plus
    groups[1 - sign] = minus
    return jnp.stack(groups, axis=d)


def faces(cube, sign, d):
    n = cube.shape[3 + d]
    plus = lax.index_in_dim(cube, 1 + sign, axis=d, keepdims=False)
    minus = lax.index_in_dim(cube, 1 - sign, axis=d, keepdims=False)
    return lax.slice_in_dim(plus, n - 1, n, axis=2 + d), lax.slice_in_dim(minus, 0, 1, axis=2 + d)


def halos(fields, signs):
    cubes = [f.reshape((3, 3, 3) + f.shape[1:]) for f in fields]
    sx, sy, sz = cubes[0].shape[3:]
    x_up, x_dn = zip(*[faces(c, s, 0) for c, s in zip(cubes, signs)])
    xlo, xhi = halo_exchange(jnp.stack(x_up), jnp.stack(x_dn), "gx")
    y_up, y_dn = [], []
    for k, (c, s) in enumerate(zip(cubes, signs)):
        top = shifted(c[:, :, :, :, sy - 1 : sy], xlo[k][:, :, :, sy - 1 : sy], xhi[k][:, :, :, sy - 1 : sy], 0, s)
        bot = shifted(c[:, :, :, :, 0:1], xlo[k][:, :, :, 0:1], xhi[k][:, :, :, 0:1], 0, s)
        y_up.append(lax.index_in_dim(top, 1 + s, axis=1, keepdims=False))
        y_dn.append(lax.index_in_dim(bot, 1 - s, axis=1, keepdims=False))
    ylo, yhi = halo_exchange(jnp.stack(y_up), jnp.stack(y_dn), "gy")
    z_up, z_dn = [], []
    for k, (c, s) in enumerate(zip(cubes, signs)):
        cols = []
        for z0 in (sz - 1, 0):
            col = shifted(c[..., z0 : z0 + 1], xlo[k][..., z0 : z0 + 1], xhi[k][..., z0 : z0 + 1], 0, s)
            col = shifted(col, ylo[k][..., z0 : z0 + 1], yhi[k][..., z0 : z0 + 1], 1, s)
            cols.append(col)
        z_up.append(lax.index_in_dim(cols[0], 1 + s, axis=2, keepdims=False))
        z_dn.append(lax.index_in_dim(cols[1], 1 - s, axis=2, keepdims=False))
    zlo, zhi = halo_exchange(jnp.stack(z_up), jnp.stack(z_dn), "gz")
    out = []
    for k in range(len(cubes)):
        out.append(
            (
                xlo[k].reshape(9, sy, sz),
                xhi[k].reshape(9, sy, sz),
                ylo[k].reshape(9, sx, sz),
                yhi[k].reshape(9, sx, sz),
                zlo[k].reshape(9, sx, sy, 1),
                zhi[k].reshape(9, sx, sy, 1),
            )
        )
    return out


def move_into(dst, src, hal, sign):
    xlo, xhi, ylo, yhi, zlo, zhi = hal
    _, sx, sy, sz = src.shape
    rows = lax.broadcasted_iota(jnp.int32, (sy, sz), 0)
    lanes = lax.broadcasted_iota(jnp.int32, (sy, sz), 1)
    for q in range(27):
        cx, cy, cz = (int(v) for v in STEPS[q])
        vx, vy, vz = sign * cx, sign * cy, sign * cz
        for i in range(sx):
            j = i - vx
            if j < 0:
                t = xlo[(cy + 1) * 3 + cz + 1]
            elif j >= sx:
                t = xhi[(cy + 1) * 3 + cz + 1]
            else:
                t = src[q, j]
            if vy == 1:
                t = jnp.where(rows == 0, ylo[(cx + 1) * 3 + cz + 1, pl.ds(i, 1), :], pltpu.roll(t, 1, 0))
            elif vy == -1:
                t = jnp.where(rows == sy - 1, yhi[(cx + 1) * 3 + cz + 1, pl.ds(i, 1), :], pltpu.roll(t, sy - 1, 0))
            if vz == 1:
                t = jnp.where(lanes == 0, zlo[(cx + 1) * 3 + cy + 1, i], pltpu.roll(t, 1, 1))
            elif vz == -1:
                t = jnp.where(lanes == sz - 1, zhi[(cx + 1) * 3 + cy + 1, i], pltpu.roll(t, sz - 1, 1))
            dst[q, i] = t


def adjoint_rows(F, A, om, ga):
    rho = sum(F)
    mom = []
    for axis in range(3):
        pos = [F[q] for q in range(27) if STEPS[q, axis] == 1]
        neg = [F[q] for q in range(27) if STEPS[q, axis] == -1]
        mom.append(sum(pos) - sum(neg))
    vel = (mom[0] / rho, mom[1] / rho, mom[2] / rho)
    uu = vel[0] * vel[0] + vel[1] * vel[1] + vel[2] * vel[2]
    sens = 0.0
    e_rho = 0.0
    s0 = 0.0
    sm = [0.0, 0.0, 0.0]
    for q in range(27):
        c = STEPS[q]
        w = float(WEIGHTS[q])
        cu = None
        for axis in range(3):
            if c[axis] == 1:
                cu = vel[axis] if cu is None else cu + vel[axis]
            elif c[axis] == -1:
                cu = -vel[axis] if cu is None else cu - vel[axis]
        if cu is None:
            eq = w * rho * (1.0 - 1.5 * uu)
        else:
            eq = w * rho * (1.0 + 3.0 * cu + 4.5 * cu * cu - 1.5 * uu)
        bgk = F[q] - om * (F[q] - eq)
        sens = sens + A[q] * (F[26 - q] - bgk)
        aw = A[q] * w
        s0 = s0 + aw
        if cu is None:
            e_rho = e_rho + aw * (1.0 + 1.5 * uu)
        else:
            e_rho = e_rho + aw * (1.0 - 4.5 * cu * cu + 1.5 * uu)
            t = aw * (1.0 + 3.0 * cu)
            for axis in range(3):
                if c[axis] == 1:
                    sm[axis] = sm[axis] + t
                elif c[axis] == -1:
                    sm[axis] = sm[axis] - t
    em = [3.0 * sm[axis] - 3.0 * vel[axis] * s0 for axis in range(3)]
    keep = 1.0 - ga
    out = []
    for p in range(27):
        c = STEPS[p]
        g = e_rho
        for axis in range(3):
            if c[axis] == 1:
                g = g + em[axis]
            elif c[axis] == -1:
                g = g - em[axis]
        out.append(keep * ((1.0 - om) * A[p] + om * g) + ga * A[26 - p])
    return out, sens


def chunked_adjoint(f_ref, a_ref, rate_ref, gamma_ref, out_ref, sens_ref):
    _, sx, sy, sz = out_ref.shape
    halves = sy // 8

    def body(step, carry):
        i = step // halves
        h = pl.multiple_of((step % halves) * 8, 8)
        F = [f_ref[q, i, pl.ds(h, 8), :] for q in range(27)]
        A = [a_ref[q, i, pl.ds(h, 8), :] for q in range(27)]
        om = rate_ref[i, pl.ds(h, 8), :]
        ga = gamma_ref[i, pl.ds(h, 8), :]
        adj, sens = adjoint_rows(F, A, om, ga)
        for q in range(27):
            out_ref[q, i, pl.ds(h, 8), :] = adj[q]
        sens_ref[i, pl.ds(h, 8), :] = sens
        return carry

    lax.fori_loop(0, sx * halves, body, 0)


def next_kernel(cf_ref, ae_ref, *refs):
    hal_f = refs[0:6]
    hal_a = refs[6:12]
    rate_ref, gamma_ref, out_ref, sens_ref, fs, as_ = refs[12:]
    move_into(fs, cf_ref, hal_f, 1)
    move_into(as_, ae_ref, hal_a, -1)
    chunked_adjoint(fs, as_, rate_ref, gamma_ref, out_ref, sens_ref)


def now_kernel(an_ref, f_ref, *refs):
    hal = refs[0:6]
    rate_ref, gamma_ref, out_ref, sens_ref, as_ = refs[6:]
    move_into(as_, an_ref, hal, -1)
    chunked_adjoint(f_ref, as_, rate_ref, gamma_ref, out_ref, sens_ref)


def run_stage(kernel, args, shape, scratch):
    _, sx, sy, sz = shape
    return pl.pallas_call(
        kernel,
        out_shape=(
            jax.ShapeDtypeStruct(shape, jnp.float32),
            jax.ShapeDtypeStruct((sx, sy, sz), jnp.float32),
        ),
        scratch_shapes=[pltpu.VMEM(shape, jnp.float32) for _ in range(scratch)],
    )(*args)


def shards(check_pops, adjoint_end, relax_rate, wall_flag, patch_of_cell, porosity, patch_slot):
    sx, sy, sz = relax_rate.shape
    ids = patch_of_cell[:, :: sy // 2, :: sz // 2]
    table = jnp.stack([porosity, patch_slot.astype(jnp.float32)], axis=1)
    looked = table[ids]
    solid = jnp.broadcast_to(looked[:, :, None, :, None, 0], (sx, 2, sy // 2, 2, sz // 2)).reshape(sx, sy, sz)
    walls = wall_flag.astype(jnp.float32)
    gamma = walls * solid
    post_now, _ = collide(check_pops, relax_rate, gamma)
    hal_f, hal_a = halos([post_now, adjoint_end], [1, -1])
    shape = check_pops.shape
    adj_next, sens_next = run_stage(
        next_kernel, (post_now, adjoint_end) + hal_f + hal_a + (relax_rate, gamma), shape, 2
    )
    (hal_n,) = halos([adj_next], [-1])
    adjoint_start, sens_now = run_stage(now_kernel, (adj_next, check_pops) + hal_n + (relax_rate, gamma), shape, 1)
    density = walls * (sens_next + sens_now)
    boxes = density.reshape(sx, 2, sy // 2, 2, sz // 2).sum(axis=(2, 4))
    parts = jnp.stack([boxes[0], boxes[1 : sx - 1].sum(axis=0), boxes[sx - 1]])
    count = porosity.shape[0]
    devices = lax.axis_size(("gx", "gy", "gz"))
    slots = jnp.stack([looked[0, :, :, 1], looked[1, :, :, 1], looked[sx - 1, :, :, 1]]).reshape(-1)
    hits = (slots[:, None] == jnp.arange(count, dtype=jnp.float32)[None, :]).astype(jnp.float32)
    placed = jnp.sum(parts.reshape(-1)[:, None] * hits, axis=0)
    got = lax.all_to_all(placed.reshape(devices, count // devices), ("gx", "gy", "gz"), 0, 0, tiled=True)
    patch_sens = jnp.sum(got, axis=0)
    return (adjoint_start, patch_sens)


def solution(mesh):
    in_specs = (
        P(None, "gx", "gy", "gz"),
        P(None, "gx", "gy", "gz"),
        P("gx", "gy", "gz"),
        P("gx", "gy", "gz"),
        P("gx", "gy", "gz"),
        P(),
        P(),
    )
    out_specs = (P(None, "gx", "gy", "gz"), P(("gx", "gy", "gz")))
    return jax.shard_map(shards, mesh=mesh, in_specs=in_specs, out_specs=out_specs, check_vma=False)
```

```python
import jax
import jax.numpy as jnp
import numpy as np
from jax import lax
from jax.experimental import pallas as pl
from jax.experimental.pallas import tpu as pltpu
from jax.sharding import PartitionSpec as P


def lattice_table():
    steps = np.array(
        [
            [first, second, third]
            for first in (-1, 0, 1)
            for second in (-1, 0, 1)
            for third in (-1, 0, 1)
        ],
        dtype=np.int64,
    )
    moved = np.abs(steps).sum(axis=1)
    weights = np.array([8.0 / 27.0, 2.0 / 27.0, 1.0 / 54.0, 1.0 / 216.0])[moved]
    return (steps, weights)


STEPS, WEIGHTS = lattice_table()


def collide(pops, rate, gamma):
    steps, weights = lattice_table()
    cube = pops.reshape((3, 3, 3) + pops.shape[1:])
    density = jnp.sum(pops, axis=0)
    mom_x = jnp.sum(cube[2], axis=(0, 1)) - jnp.sum(cube[0], axis=(0, 1))
    mom_y = jnp.sum(cube[:, 2], axis=(0, 1)) - jnp.sum(cube[:, 0], axis=(0, 1))
    mom_z = jnp.sum(cube[:, :, 2], axis=(0, 1)) - jnp.sum(cube[:, :, 0], axis=(0, 1))
    vel_x = mom_x / density
    vel_y = mom_y / density
    vel_z = mom_z / density
    cx = jnp.asarray(steps[:, 0], jnp.float32)[:, None, None, None]
    cy = jnp.asarray(steps[:, 1], jnp.float32)[:, None, None, None]
    cz = jnp.asarray(steps[:, 2], jnp.float32)[:, None, None, None]
    wts = jnp.asarray(weights, jnp.float32)[:, None, None, None]
    along = cx * vel_x + cy * vel_y + cz * vel_z
    speed = vel_x * vel_x + vel_y * vel_y + vel_z * vel_z
    equil = wts * density * (1.0 + 3.0 * along + 4.5 * along * along - 1.5 * speed)
    relaxed = pops - rate * (pops - equil)
    flipped = pops[::-1]
    return ((1.0 - gamma) * relaxed + gamma * flipped, flipped - relaxed)


def halo_exchange(up, down, axis):
    size = lax.axis_size(axis)
    if size == 1:
        return up, down
    if size == 2:
        both = lax.ppermute(jnp.stack([up, down]), axis, [(0, 1), (1, 0)])
        return both[0], both[1]
    lo = lax.ppermute(up, axis, [(i, (i + 1) % size) for i in range(size)])
    hi = lax.ppermute(down, axis, [(i, (i - 1) % size) for i in range(size)])
    return lo, hi


def shifted(cube, lo, hi, d, sign):
    n = cube.shape[3 + d]
    plus = lax.index_in_dim(cube, 1 + sign, axis=d, keepdims=False)
    minus = lax.index_in_dim(cube, 1 - sign, axis=d, keepdims=False)
    still = lax.index_in_dim(cube, 1, axis=d, keepdims=False)
    plus = jnp.concatenate([lo, lax.slice_in_dim(plus, 0, n - 1, axis=2 + d)], axis=2 + d)
    minus = jnp.concatenate([lax.slice_in_dim(minus, 1, n, axis=2 + d), hi], axis=2 + d)
    groups = [None, still, None]
    groups[1 + sign] = plus
    groups[1 - sign] = minus
    return jnp.stack(groups, axis=d)


def faces(cube, sign, d):
    n = cube.shape[3 + d]
    plus = lax.index_in_dim(cube, 1 + sign, axis=d, keepdims=False)
    minus = lax.index_in_dim(cube, 1 - sign, axis=d, keepdims=False)
    return lax.slice_in_dim(plus, n - 1, n, axis=2 + d), lax.slice_in_dim(minus, 0, 1, axis=2 + d)


def halos(fields, signs):
    cubes = [f.reshape((3, 3, 3) + f.shape[1:]) for f in fields]
    sx, sy, sz = cubes[0].shape[3:]
    x_up, x_dn = zip(*[faces(c, s, 0) for c, s in zip(cubes, signs)])
    xlo, xhi = halo_exchange(jnp.stack(x_up), jnp.stack(x_dn), "gx")
    y_up, y_dn = [], []
    for k, (c, s) in enumerate(zip(cubes, signs)):
        top = shifted(c[:, :, :, :, sy - 1 : sy], xlo[k][:, :, :, sy - 1 : sy], xhi[k][:, :, :, sy - 1 : sy], 0, s)
        bot = shifted(c[:, :, :, :, 0:1], xlo[k][:, :, :, 0:1], xhi[k][:, :, :, 0:1], 0, s)
        y_up.append(lax.index_in_dim(top, 1 + s, axis=1, keepdims=False))
        y_dn.append(lax.index_in_dim(bot, 1 - s, axis=1, keepdims=False))
    ylo, yhi = halo_exchange(jnp.stack(y_up), jnp.stack(y_dn), "gy")
    z_up, z_dn = [], []
    for k, (c, s) in enumerate(zip(cubes, signs)):
        cols = []
        for z0 in (sz - 1, 0):
            col = shifted(c[..., z0 : z0 + 1], xlo[k][..., z0 : z0 + 1], xhi[k][..., z0 : z0 + 1], 0, s)
            col = shifted(col, ylo[k][..., z0 : z0 + 1], yhi[k][..., z0 : z0 + 1], 1, s)
            cols.append(col)
        z_up.append(jnp.swapaxes(lax.index_in_dim(cols[0], 1 + s, axis=2, keepdims=False)[..., 0], -1, -2))
        z_dn.append(jnp.swapaxes(lax.index_in_dim(cols[1], 1 - s, axis=2, keepdims=False)[..., 0], -1, -2))
    zlo, zhi = halo_exchange(jnp.stack(z_up), jnp.stack(z_dn), "gz")
    out = []
    for k in range(len(cubes)):
        out.append(
            (
                xlo[k].reshape(9, sy, sz),
                xhi[k].reshape(9, sy, sz),
                ylo[k].reshape(9, sx, sz),
                yhi[k].reshape(9, sx, sz),
                zlo[k].reshape(9, sy, sx),
                zhi[k].reshape(9, sy, sx),
            )
        )
    return out


def move_into(dst, src, hal, sign):
    xlo, xhi, ylo, yhi, zlo, zhi = hal
    _, sx, sy, sz = src.shape
    rows = lax.broadcasted_iota(jnp.int32, (sy, sz), 0)
    lanes = lax.broadcasted_iota(jnp.int32, (sy, sz), 1)
    for q in range(27):
        cx, cy, cz = (int(v) for v in STEPS[q])
        vx, vy, vz = sign * cx, sign * cy, sign * cz
        if vz == 1:
            zcol = zlo[(cx + 1) * 3 + cy + 1]
        elif vz == -1:
            zcol = zhi[(cx + 1) * 3 + cy + 1]
        for i in range(sx):
            j = i - vx
            if j < 0:
                t = xlo[(cy + 1) * 3 + cz + 1]
            elif j >= sx:
                t = xhi[(cy + 1) * 3 + cz + 1]
            else:
                t = src[q, j]
            if vy == 1:
                t = jnp.where(rows == 0, ylo[(cx + 1) * 3 + cz + 1, pl.ds(i, 1), :], pltpu.roll(t, 1, 0))
            elif vy == -1:
                t = jnp.where(rows == sy - 1, yhi[(cx + 1) * 3 + cz + 1, pl.ds(i, 1), :], pltpu.roll(t, sy - 1, 0))
            if vz == 1:
                t = jnp.where(lanes == 0, zcol[:, i : i + 1], pltpu.roll(t, 1, 1))
            elif vz == -1:
                t = jnp.where(lanes == sz - 1, zcol[:, i : i + 1], pltpu.roll(t, sz - 1, 1))
            dst[q, i] = t


def adjoint_rows(F, A, om, ga):
    rho = sum(F)
    mom = []
    for axis in range(3):
        pos = [F[q] for q in range(27) if STEPS[q, axis] == 1]
        neg = [F[q] for q in range(27) if STEPS[q, axis] == -1]
        mom.append(sum(pos) - sum(neg))
    vel = (mom[0] / rho, mom[1] / rho, mom[2] / rho)
    uu = vel[0] * vel[0] + vel[1] * vel[1] + vel[2] * vel[2]
    sens = 0.0
    e_rho = 0.0
    s0 = 0.0
    sm = [0.0, 0.0, 0.0]
    for q in range(27):
        c = STEPS[q]
        w = float(WEIGHTS[q])
        cu = None
        for axis in range(3):
            if c[axis] == 1:
                cu = vel[axis] if cu is None else cu + vel[axis]
            elif c[axis] == -1:
                cu = -vel[axis] if cu is None else cu - vel[axis]
        if cu is None:
            eq = w * rho * (1.0 - 1.5 * uu)
        else:
            eq = w * rho * (1.0 + 3.0 * cu + 4.5 * cu * cu - 1.5 * uu)
        bgk = F[q] - om * (F[q] - eq)
        sens = sens + A[q] * (F[26 - q] - bgk)
        aw = A[q] * w
        s0 = s0 + aw
        if cu is None:
            e_rho = e_rho + aw * (1.0 + 1.5 * uu)
        else:
            e_rho = e_rho + aw * (1.0 - 4.5 * cu * cu + 1.5 * uu)
            t = aw * (1.0 + 3.0 * cu)
            for axis in range(3):
                if c[axis] == 1:
                    sm[axis] = sm[axis] + t
                elif c[axis] == -1:
                    sm[axis] = sm[axis] - t
    em = [3.0 * sm[axis] - 3.0 * vel[axis] * s0 for axis in range(3)]
    keep = 1.0 - ga
    out = []
    for p in range(27):
        c = STEPS[p]
        g = e_rho
        for axis in range(3):
            if c[axis] == 1:
                g = g + em[axis]
            elif c[axis] == -1:
                g = g - em[axis]
        out.append(keep * ((1.0 - om) * A[p] + om * g) + ga * A[26 - p])
    return out, sens


def chunked_adjoint(f_ref, a_ref, rate_ref, gamma_ref, out_ref, sens_ref):
    _, sx, sy, sz = out_ref.shape
    halves = sy // 8

    def body(step, carry):
        i = step // halves
        h = pl.multiple_of((step % halves) * 8, 8)
        F = [f_ref[q, i, pl.ds(h, 8), :] for q in range(27)]
        A = [a_ref[q, i, pl.ds(h, 8), :] for q in range(27)]
        om = rate_ref[i, pl.ds(h, 8), :]
        ga = gamma_ref[i, pl.ds(h, 8), :]
        adj, sens = adjoint_rows(F, A, om, ga)
        for q in range(27):
            out_ref[q, i, pl.ds(h, 8), :] = adj[q]
        sens_ref[i, pl.ds(h, 8), :] = sens
        return carry

    lax.fori_loop(0, sx * halves, body, 0)


def next_kernel(cf_ref, ae_ref, *refs):
    hal_f = refs[0:6]
    hal_a = refs[6:12]
    rate_ref, gamma_ref, out_ref, sens_ref, fs, as_ = refs[12:]
    move_into(fs, cf_ref, hal_f, 1)
    move_into(as_, ae_ref, hal_a, -1)
    chunked_adjoint(fs, as_, rate_ref, gamma_ref, out_ref, sens_ref)


def now_kernel(an_ref, f_ref, *refs):
    hal = refs[0:6]
    rate_ref, gamma_ref, out_ref, sens_ref, as_ = refs[6:]
    move_into(as_, an_ref, hal, -1)
    chunked_adjoint(f_ref, as_, rate_ref, gamma_ref, out_ref, sens_ref)


def run_stage(kernel, args, shape, scratch):
    _, sx, sy, sz = shape
    return pl.pallas_call(
        kernel,
        out_shape=(
            jax.ShapeDtypeStruct(shape, jnp.float32),
            jax.ShapeDtypeStruct((sx, sy, sz), jnp.float32),
        ),
        scratch_shapes=[pltpu.VMEM(shape, jnp.float32) for _ in range(scratch)],
    )(*args)


def shards(check_pops, adjoint_end, relax_rate, wall_flag, patch_of_cell, porosity, patch_slot):
    sx, sy, sz = relax_rate.shape
    ids = patch_of_cell[:, :: sy // 2, :: sz // 2]
    table = jnp.stack([porosity, patch_slot.astype(jnp.float32)], axis=1)
    looked = table[ids]
    solid = jnp.broadcast_to(looked[:, :, None, :, None, 0], (sx, 2, sy // 2, 2, sz // 2)).reshape(sx, sy, sz)
    walls = wall_flag.astype(jnp.float32)
    gamma = walls * solid
    post_now, _ = collide(check_pops, relax_rate, gamma)
    hal_f, hal_a = halos([post_now, adjoint_end], [1, -1])
    shape = check_pops.shape
    adj_next, sens_next = run_stage(
        next_kernel, (post_now, adjoint_end) + hal_f + hal_a + (relax_rate, gamma), shape, 2
    )
    (hal_n,) = halos([adj_next], [-1])
    adjoint_start, sens_now = run_stage(now_kernel, (adj_next, check_pops) + hal_n + (relax_rate, gamma), shape, 1)
    density = walls * (sens_next + sens_now)
    boxes = density.reshape(sx, 2, sy // 2, 2, sz // 2).sum(axis=(2, 4))
    parts = jnp.stack([boxes[0], boxes[1 : sx - 1].sum(axis=0), boxes[sx - 1]])
    count = porosity.shape[0]
    devices = lax.axis_size(("gx", "gy", "gz"))
    slots = jnp.stack([looked[0, :, :, 1], looked[1, :, :, 1], looked[sx - 1, :, :, 1]]).reshape(-1)
    hits = (slots[:, None] == jnp.arange(count, dtype=jnp.float32)[None, :]).astype(jnp.float32)
    placed = jnp.sum(parts.reshape(-1)[:, None] * hits, axis=0)
    got = lax.all_to_all(placed.reshape(devices, count // devices), ("gx", "gy", "gz"), 0, 0, tiled=True)
    patch_sens = jnp.sum(got, axis=0)
    return (adjoint_start, patch_sens)


def solution(mesh):
    in_specs = (
        P(None, "gx", "gy", "gz"),
        P(None, "gx", "gy", "gz"),
        P("gx", "gy", "gz"),
        P("gx", "gy", "gz"),
        P("gx", "gy", "gz"),
        P(),
        P(),
    )
    out_specs = (P(None, "gx", "gy", "gz"), P(("gx", "gy", "gz")))
    return jax.shard_map(shards, mesh=mesh, in_specs=in_specs, out_specs=out_specs, check_vma=False)
```

```python
import jax
import jax.numpy as jnp
import numpy as np
from jax import lax
from jax.experimental import pallas as pl
from jax.experimental.pallas import tpu as pltpu
from jax.sharding import PartitionSpec as P


def lattice_table():
    steps = np.array(
        [
            [first, second, third]
            for first in (-1, 0, 1)
            for second in (-1, 0, 1)
            for third in (-1, 0, 1)
        ],
        dtype=np.int64,
    )
    moved = np.abs(steps).sum(axis=1)
    weights = np.array([8.0 / 27.0, 2.0 / 27.0, 1.0 / 54.0, 1.0 / 216.0])[moved]
    return (steps, weights)


STEPS, WEIGHTS = lattice_table()


def collide(pops, rate, gamma):
    steps, weights = lattice_table()
    cube = pops.reshape((3, 3, 3) + pops.shape[1:])
    density = jnp.sum(pops, axis=0)
    mom_x = jnp.sum(cube[2], axis=(0, 1)) - jnp.sum(cube[0], axis=(0, 1))
    mom_y = jnp.sum(cube[:, 2], axis=(0, 1)) - jnp.sum(cube[:, 0], axis=(0, 1))
    mom_z = jnp.sum(cube[:, :, 2], axis=(0, 1)) - jnp.sum(cube[:, :, 0], axis=(0, 1))
    vel_x = mom_x / density
    vel_y = mom_y / density
    vel_z = mom_z / density
    cx = jnp.asarray(steps[:, 0], jnp.float32)[:, None, None, None]
    cy = jnp.asarray(steps[:, 1], jnp.float32)[:, None, None, None]
    cz = jnp.asarray(steps[:, 2], jnp.float32)[:, None, None, None]
    wts = jnp.asarray(weights, jnp.float32)[:, None, None, None]
    along = cx * vel_x + cy * vel_y + cz * vel_z
    speed = vel_x * vel_x + vel_y * vel_y + vel_z * vel_z
    equil = wts * density * (1.0 + 3.0 * along + 4.5 * along * along - 1.5 * speed)
    relaxed = pops - rate * (pops - equil)
    flipped = pops[::-1]
    return ((1.0 - gamma) * relaxed + gamma * flipped, flipped - relaxed)


def halo_exchange(up, down, axis):
    size = lax.axis_size(axis)
    if size == 1:
        return up, down
    if size == 2:
        both = lax.ppermute(jnp.stack([up, down]), axis, [(0, 1), (1, 0)])
        return both[0], both[1]
    lo = lax.ppermute(up, axis, [(i, (i + 1) % size) for i in range(size)])
    hi = lax.ppermute(down, axis, [(i, (i - 1) % size) for i in range(size)])
    return lo, hi


def shifted(cube, lo, hi, d, sign):
    n = cube.shape[3 + d]
    plus = lax.index_in_dim(cube, 1 + sign, axis=d, keepdims=False)
    minus = lax.index_in_dim(cube, 1 - sign, axis=d, keepdims=False)
    still = lax.index_in_dim(cube, 1, axis=d, keepdims=False)
    plus = jnp.concatenate([lo, lax.slice_in_dim(plus, 0, n - 1, axis=2 + d)], axis=2 + d)
    minus = jnp.concatenate([lax.slice_in_dim(minus, 1, n, axis=2 + d), hi], axis=2 + d)
    groups = [None, still, None]
    groups[1 + sign] = plus
    groups[1 - sign] = minus
    return jnp.stack(groups, axis=d)


def faces(cube, sign, d):
    n = cube.shape[3 + d]
    plus = lax.index_in_dim(cube, 1 + sign, axis=d, keepdims=False)
    minus = lax.index_in_dim(cube, 1 - sign, axis=d, keepdims=False)
    return lax.slice_in_dim(plus, n - 1, n, axis=2 + d), lax.slice_in_dim(minus, 0, 1, axis=2 + d)


def halos(fields, signs):
    cubes = [f.reshape((3, 3, 3) + f.shape[1:]) for f in fields]
    sx, sy, sz = cubes[0].shape[3:]
    x_up, x_dn = zip(*[faces(c, s, 0) for c, s in zip(cubes, signs)])
    xlo, xhi = halo_exchange(jnp.stack(x_up), jnp.stack(x_dn), "gx")
    both = jnp.stack(cubes)
    rows = jnp.concatenate([both[..., sy - 1 : sy, :], both[..., 0:1, :]], axis=5)
    cols = jnp.concatenate([both[..., sz - 1 : sz], both[..., 0:1]], axis=6)
    y_up, y_dn = [], []
    for k, s in enumerate(signs):
        top = shifted(rows[k][..., 0:1, :], xlo[k][:, :, :, sy - 1 : sy], xhi[k][:, :, :, sy - 1 : sy], 0, s)
        bot = shifted(rows[k][..., 1:2, :], xlo[k][:, :, :, 0:1], xhi[k][:, :, :, 0:1], 0, s)
        y_up.append(lax.index_in_dim(top, 1 + s, axis=1, keepdims=False))
        y_dn.append(lax.index_in_dim(bot, 1 - s, axis=1, keepdims=False))
    ylo, yhi = halo_exchange(jnp.stack(y_up), jnp.stack(y_dn), "gy")
    z_up, z_dn = [], []
    for k, s in enumerate(signs):
        picked = []
        for at, z0 in ((0, sz - 1), (1, 0)):
            col = cols[k][..., at : at + 1]
            col = shifted(col, xlo[k][..., z0 : z0 + 1], xhi[k][..., z0 : z0 + 1], 0, s)
            col = shifted(col, ylo[k][..., z0 : z0 + 1], yhi[k][..., z0 : z0 + 1], 1, s)
            picked.append(col)
        z_up.append(jnp.swapaxes(lax.index_in_dim(picked[0], 1 + s, axis=2, keepdims=False)[..., 0], -1, -2))
        z_dn.append(jnp.swapaxes(lax.index_in_dim(picked[1], 1 - s, axis=2, keepdims=False)[..., 0], -1, -2))
    zlo, zhi = halo_exchange(jnp.stack(z_up), jnp.stack(z_dn), "gz")
    out = []
    for k in range(len(cubes)):
        out.append(
            (
                xlo[k].reshape(9, sy, sz),
                xhi[k].reshape(9, sy, sz),
                ylo[k].reshape(9, sx, sz),
                yhi[k].reshape(9, sx, sz),
                zlo[k].reshape(9, sy, sx),
                zhi[k].reshape(9, sy, sx),
            )
        )
    return out


def move_into(dst, src, hal, sign):
    xlo, xhi, ylo, yhi, zlo, zhi = hal
    _, sx, sy, sz = src.shape
    rows = lax.broadcasted_iota(jnp.int32, (sy, sz), 0)
    lanes = lax.broadcasted_iota(jnp.int32, (sy, sz), 1)
    for q in range(27):
        cx, cy, cz = (int(v) for v in STEPS[q])
        vx, vy, vz = sign * cx, sign * cy, sign * cz
        if vz == 1:
            zcol = zlo[(cx + 1) * 3 + cy + 1]
        elif vz == -1:
            zcol = zhi[(cx + 1) * 3 + cy + 1]
        for i in range(sx):
            j = i - vx
            if j < 0:
                t = xlo[(cy + 1) * 3 + cz + 1]
            elif j >= sx:
                t = xhi[(cy + 1) * 3 + cz + 1]
            else:
                t = src[q, j]
            if vy == 1:
                t = jnp.where(rows == 0, ylo[(cx + 1) * 3 + cz + 1, pl.ds(i, 1), :], pltpu.roll(t, 1, 0))
            elif vy == -1:
                t = jnp.where(rows == sy - 1, yhi[(cx + 1) * 3 + cz + 1, pl.ds(i, 1), :], pltpu.roll(t, sy - 1, 0))
            if vz == 1:
                t = jnp.where(lanes == 0, zcol[:, i : i + 1], pltpu.roll(t, 1, 1))
            elif vz == -1:
                t = jnp.where(lanes == sz - 1, zcol[:, i : i + 1], pltpu.roll(t, sz - 1, 1))
            dst[q, i] = t


def adjoint_rows(F, A, om, ga):
    rho = sum(F)
    mom = []
    for axis in range(3):
        pos = [F[q] for q in range(27) if STEPS[q, axis] == 1]
        neg = [F[q] for q in range(27) if STEPS[q, axis] == -1]
        mom.append(sum(pos) - sum(neg))
    vel = (mom[0] / rho, mom[1] / rho, mom[2] / rho)
    uu = vel[0] * vel[0] + vel[1] * vel[1] + vel[2] * vel[2]
    sens = 0.0
    e_rho = 0.0
    s0 = 0.0
    sm = [0.0, 0.0, 0.0]
    for q in range(27):
        c = STEPS[q]
        w = float(WEIGHTS[q])
        cu = None
        for axis in range(3):
            if c[axis] == 1:
                cu = vel[axis] if cu is None else cu + vel[axis]
            elif c[axis] == -1:
                cu = -vel[axis] if cu is None else cu - vel[axis]
        if cu is None:
            eq = w * rho * (1.0 - 1.5 * uu)
        else:
            eq = w * rho * (1.0 + 3.0 * cu + 4.5 * cu * cu - 1.5 * uu)
        bgk = F[q] - om * (F[q] - eq)
        sens = sens + A[q] * (F[26 - q] - bgk)
        aw = A[q] * w
        s0 = s0 + aw
        if cu is None:
            e_rho = e_rho + aw * (1.0 + 1.5 * uu)
        else:
            e_rho = e_rho + aw * (1.0 - 4.5 * cu * cu + 1.5 * uu)
            t = aw * (1.0 + 3.0 * cu)
            for axis in range(3):
                if c[axis] == 1:
                    sm[axis] = sm[axis] + t
                elif c[axis] == -1:
                    sm[axis] = sm[axis] - t
    em = [3.0 * sm[axis] - 3.0 * vel[axis] * s0 for axis in range(3)]
    keep = 1.0 - ga
    out = []
    for p in range(27):
        c = STEPS[p]
        g = e_rho
        for axis in range(3):
            if c[axis] == 1:
                g = g + em[axis]
            elif c[axis] == -1:
                g = g - em[axis]
        out.append(keep * ((1.0 - om) * A[p] + om * g) + ga * A[26 - p])
    return out, sens


def chunked_adjoint(f_ref, a_ref, rate_ref, gamma_ref, out_ref, sens_ref):
    _, sx, sy, sz = out_ref.shape
    halves = sy // 8

    def body(step, carry):
        i = step // halves
        h = pl.multiple_of((step % halves) * 8, 8)
        F = [f_ref[q, i, pl.ds(h, 8), :] for q in range(27)]
        A = [a_ref[q, i, pl.ds(h, 8), :] for q in range(27)]
        om = rate_ref[i, pl.ds(h, 8), :]
        ga = gamma_ref[i, pl.ds(h, 8), :]
        adj, sens = adjoint_rows(F, A, om, ga)
        for q in range(27):
            out_ref[q, i, pl.ds(h, 8), :] = adj[q]
        sens_ref[i, pl.ds(h, 8), :] = sens
        return carry

    lax.fori_loop(0, sx * halves, body, 0)


def next_kernel(cf_ref, ae_ref, *refs):
    hal_f = refs[0:6]
    hal_a = refs[6:12]
    rate_ref, gamma_ref, out_ref, sens_ref, fs, as_ = refs[12:]
    move_into(fs, cf_ref, hal_f, 1)
    move_into(as_, ae_ref, hal_a, -1)
    chunked_adjoint(fs, as_, rate_ref, gamma_ref, out_ref, sens_ref)


def now_kernel(an_ref, f_ref, *refs):
    hal = refs[0:6]
    rate_ref, gamma_ref, out_ref, sens_ref, as_ = refs[6:]
    move_into(as_, an_ref, hal, -1)
    chunked_adjoint(f_ref, as_, rate_ref, gamma_ref, out_ref, sens_ref)


def run_stage(kernel, args, shape, scratch):
    _, sx, sy, sz = shape
    return pl.pallas_call(
        kernel,
        out_shape=(
            jax.ShapeDtypeStruct(shape, jnp.float32),
            jax.ShapeDtypeStruct((sx, sy, sz), jnp.float32),
        ),
        scratch_shapes=[pltpu.VMEM(shape, jnp.float32) for _ in range(scratch)],
    )(*args)


def shards(check_pops, adjoint_end, relax_rate, wall_flag, patch_of_cell, porosity, patch_slot):
    sx, sy, sz = relax_rate.shape
    ids = patch_of_cell[:, :: sy // 2, :: sz // 2]
    table = jnp.stack([porosity, patch_slot.astype(jnp.float32)], axis=1)
    looked = table[ids]
    solid = jnp.broadcast_to(looked[:, :, None, :, None, 0], (sx, 2, sy // 2, 2, sz // 2)).reshape(sx, sy, sz)
    walls = wall_flag.astype(jnp.float32)
    gamma = walls * solid
    post_now, _ = collide(check_pops, relax_rate, gamma)
    hal_f, hal_a = halos([post_now, adjoint_end], [1, -1])
    shape = check_pops.shape
    adj_next, sens_next = run_stage(
        next_kernel, (post_now, adjoint_end) + hal_f + hal_a + (relax_rate, gamma), shape, 2
    )
    (hal_n,) = halos([adj_next], [-1])
    adjoint_start, sens_now = run_stage(now_kernel, (adj_next, check_pops) + hal_n + (relax_rate, gamma), shape, 1)
    density = walls * (sens_next + sens_now)
    boxes = density.reshape(sx, 2, sy // 2, 2, sz // 2).sum(axis=(2, 4))
    parts = jnp.stack([boxes[0], boxes[1 : sx - 1].sum(axis=0), boxes[sx - 1]])
    count = porosity.shape[0]
    devices = lax.axis_size(("gx", "gy", "gz"))
    slots = jnp.stack([looked[0, :, :, 1], looked[1, :, :, 1], looked[sx - 1, :, :, 1]]).reshape(-1)
    hits = (slots[:, None] == jnp.arange(count, dtype=jnp.float32)[None, :]).astype(jnp.float32)
    placed = jnp.sum(parts.reshape(-1)[:, None] * hits, axis=0)
    got = lax.all_to_all(placed.reshape(devices, count // devices), ("gx", "gy", "gz"), 0, 0, tiled=True)
    patch_sens = jnp.sum(got, axis=0)
    return (adjoint_start, patch_sens)


def solution(mesh):
    in_specs = (
        P(None, "gx", "gy", "gz"),
        P(None, "gx", "gy", "gz"),
        P("gx", "gy", "gz"),
        P("gx", "gy", "gz"),
        P("gx", "gy", "gz"),
        P(),
        P(),
    )
    out_specs = (P(None, "gx", "gy", "gz"), P(("gx", "gy", "gz")))
    return jax.shard_map(shards, mesh=mesh, in_specs=in_specs, out_specs=out_specs, check_vma=False)
```

```python
import jax
import jax.numpy as jnp
import numpy as np
from jax import lax
from jax.experimental import pallas as pl
from jax.experimental.pallas import tpu as pltpu
from jax.sharding import PartitionSpec as P


def lattice_table():
    steps = np.array(
        [
            [first, second, third]
            for first in (-1, 0, 1)
            for second in (-1, 0, 1)
            for third in (-1, 0, 1)
        ],
        dtype=np.int64,
    )
    moved = np.abs(steps).sum(axis=1)
    weights = np.array([8.0 / 27.0, 2.0 / 27.0, 1.0 / 54.0, 1.0 / 216.0])[moved]
    return (steps, weights)


STEPS, WEIGHTS = lattice_table()


def collide(pops, rate, gamma):
    steps, weights = lattice_table()
    cube = pops.reshape((3, 3, 3) + pops.shape[1:])
    density = jnp.sum(pops, axis=0)
    mom_x = jnp.sum(cube[2], axis=(0, 1)) - jnp.sum(cube[0], axis=(0, 1))
    mom_y = jnp.sum(cube[:, 2], axis=(0, 1)) - jnp.sum(cube[:, 0], axis=(0, 1))
    mom_z = jnp.sum(cube[:, :, 2], axis=(0, 1)) - jnp.sum(cube[:, :, 0], axis=(0, 1))
    vel_x = mom_x / density
    vel_y = mom_y / density
    vel_z = mom_z / density
    cx = jnp.asarray(steps[:, 0], jnp.float32)[:, None, None, None]
    cy = jnp.asarray(steps[:, 1], jnp.float32)[:, None, None, None]
    cz = jnp.asarray(steps[:, 2], jnp.float32)[:, None, None, None]
    wts = jnp.asarray(weights, jnp.float32)[:, None, None, None]
    along = cx * vel_x + cy * vel_y + cz * vel_z
    speed = vel_x * vel_x + vel_y * vel_y + vel_z * vel_z
    equil = wts * density * (1.0 + 3.0 * along + 4.5 * along * along - 1.5 * speed)
    relaxed = pops - rate * (pops - equil)
    flipped = pops[::-1]
    return ((1.0 - gamma) * relaxed + gamma * flipped, flipped - relaxed)


def halo_exchange(up, down, axis):
    size = lax.axis_size(axis)
    if size == 1:
        return up, down
    if size == 2:
        both = lax.ppermute(jnp.stack([up, down]), axis, [(0, 1), (1, 0)])
        return both[0], both[1]
    lo = lax.ppermute(up, axis, [(i, (i + 1) % size) for i in range(size)])
    hi = lax.ppermute(down, axis, [(i, (i - 1) % size) for i in range(size)])
    return lo, hi


def shifted(cube, lo, hi, d, sign):
    n = cube.shape[3 + d]
    plus = lax.index_in_dim(cube, 1 + sign, axis=d, keepdims=False)
    minus = lax.index_in_dim(cube, 1 - sign, axis=d, keepdims=False)
    still = lax.index_in_dim(cube, 1, axis=d, keepdims=False)
    plus = jnp.concatenate([lo, lax.slice_in_dim(plus, 0, n - 1, axis=2 + d)], axis=2 + d)
    minus = jnp.concatenate([lax.slice_in_dim(minus, 1, n, axis=2 + d), hi], axis=2 + d)
    groups = [None, still, None]
    groups[1 + sign] = plus
    groups[1 - sign] = minus
    return jnp.stack(groups, axis=d)


def faces(cube, sign, d):
    n = cube.shape[3 + d]
    plus = lax.index_in_dim(cube, 1 + sign, axis=d, keepdims=False)
    minus = lax.index_in_dim(cube, 1 - sign, axis=d, keepdims=False)
    return lax.slice_in_dim(plus, n - 1, n, axis=2 + d), lax.slice_in_dim(minus, 0, 1, axis=2 + d)


def halos(fields, signs):
    cubes = [f.reshape((3, 3, 3) + f.shape[1:]) for f in fields]
    sx, sy, sz = cubes[0].shape[3:]
    x_up, x_dn = zip(*[faces(c, s, 0) for c, s in zip(cubes, signs)])
    xlo, xhi = halo_exchange(jnp.stack(x_up), jnp.stack(x_dn), "gx")
    both = jnp.stack(cubes)
    rows = jnp.stack([both[..., sy - 1, :], both[..., 0, :]])
    cols = jnp.stack([both[..., sz - 1], both[..., 0]])
    y_up, y_dn = [], []
    for k, s in enumerate(signs):
        top = shifted(rows[0, k], xlo[k][:, :, :, sy - 1, :], xhi[k][:, :, :, sy - 1, :], 0, s)
        bot = shifted(rows[1, k], xlo[k][:, :, :, 0, :], xhi[k][:, :, :, 0, :], 0, s)
        y_up.append(lax.index_in_dim(top, 1 + s, axis=1, keepdims=False))
        y_dn.append(lax.index_in_dim(bot, 1 - s, axis=1, keepdims=False))
    ylo, yhi = halo_exchange(jnp.stack(y_up), jnp.stack(y_dn), "gy")
    z_up, z_dn = [], []
    for k, s in enumerate(signs):
        picked = []
        for at, z0 in ((0, sz - 1), (1, 0)):
            col = shifted(cols[at, k], xlo[k][..., z0], xhi[k][..., z0], 0, s)
            col = shifted(col, ylo[k][..., z0][..., None], yhi[k][..., z0][..., None], 1, s)
            picked.append(col)
        z_up.append(jnp.swapaxes(lax.index_in_dim(picked[0], 1 + s, axis=2, keepdims=False), -1, -2))
        z_dn.append(jnp.swapaxes(lax.index_in_dim(picked[1], 1 - s, axis=2, keepdims=False), -1, -2))
    zlo, zhi = halo_exchange(jnp.stack(z_up), jnp.stack(z_dn), "gz")
    out = []
    for k in range(len(cubes)):
        out.append(
            (
                xlo[k].reshape(9, sy, sz),
                xhi[k].reshape(9, sy, sz),
                ylo[k].reshape(9, sx, sz),
                yhi[k].reshape(9, sx, sz),
                zlo[k].reshape(9, sy, sx),
                zhi[k].reshape(9, sy, sx),
            )
        )
    return out


def move_into(dst, src, hal, sign):
    xlo, xhi, ylo, yhi, zlo, zhi = hal
    _, sx, sy, sz = src.shape
    rows = lax.broadcasted_iota(jnp.int32, (sy, sz), 0)
    lanes = lax.broadcasted_iota(jnp.int32, (sy, sz), 1)
    for q in range(27):
        cx, cy, cz = (int(v) for v in STEPS[q])
        vx, vy, vz = sign * cx, sign * cy, sign * cz
        if vz == 1:
            zcol = zlo[(cx + 1) * 3 + cy + 1]
        elif vz == -1:
            zcol = zhi[(cx + 1) * 3 + cy + 1]
        for i in range(sx):
            j = i - vx
            if j < 0:
                t = xlo[(cy + 1) * 3 + cz + 1]
            elif j >= sx:
                t = xhi[(cy + 1) * 3 + cz + 1]
            else:
                t = src[q, j]
            if vy == 1:
                t = jnp.where(rows == 0, ylo[(cx + 1) * 3 + cz + 1, pl.ds(i, 1), :], pltpu.roll(t, 1, 0))
            elif vy == -1:
                t = jnp.where(rows == sy - 1, yhi[(cx + 1) * 3 + cz + 1, pl.ds(i, 1), :], pltpu.roll(t, sy - 1, 0))
            if vz == 1:
                t = jnp.where(lanes == 0, zcol[:, i : i + 1], pltpu.roll(t, 1, 1))
            elif vz == -1:
                t = jnp.where(lanes == sz - 1, zcol[:, i : i + 1], pltpu.roll(t, sz - 1, 1))
            dst[q, i] = t


def adjoint_rows(F, A, om, ga):
    rho = sum(F)
    mom = []
    for axis in range(3):
        pos = [F[q] for q in range(27) if STEPS[q, axis] == 1]
        neg = [F[q] for q in range(27) if STEPS[q, axis] == -1]
        mom.append(sum(pos) - sum(neg))
    vel = (mom[0] / rho, mom[1] / rho, mom[2] / rho)
    uu = vel[0] * vel[0] + vel[1] * vel[1] + vel[2] * vel[2]
    sens = 0.0
    e_rho = 0.0
    s0 = 0.0
    sm = [0.0, 0.0, 0.0]
    for q in range(27):
        c = STEPS[q]
        w = float(WEIGHTS[q])
        cu = None
        for axis in range(3):
            if c[axis] == 1:
                cu = vel[axis] if cu is None else cu + vel[axis]
            elif c[axis] == -1:
                cu = -vel[axis] if cu is None else cu - vel[axis]
        if cu is None:
            eq = w * rho * (1.0 - 1.5 * uu)
        else:
            eq = w * rho * (1.0 + 3.0 * cu + 4.5 * cu * cu - 1.5 * uu)
        bgk = F[q] - om * (F[q] - eq)
        sens = sens + A[q] * (F[26 - q] - bgk)
        aw = A[q] * w
        s0 = s0 + aw
        if cu is None:
            e_rho = e_rho + aw * (1.0 + 1.5 * uu)
        else:
            e_rho = e_rho + aw * (1.0 - 4.5 * cu * cu + 1.5 * uu)
            t = aw * (1.0 + 3.0 * cu)
            for axis in range(3):
                if c[axis] == 1:
                    sm[axis] = sm[axis] + t
                elif c[axis] == -1:
                    sm[axis] = sm[axis] - t
    em = [3.0 * sm[axis] - 3.0 * vel[axis] * s0 for axis in range(3)]
    keep = 1.0 - ga
    out = []
    for p in range(27):
        c = STEPS[p]
        g = e_rho
        for axis in range(3):
            if c[axis] == 1:
                g = g + em[axis]
            elif c[axis] == -1:
                g = g - em[axis]
        out.append(keep * ((1.0 - om) * A[p] + om * g) + ga * A[26 - p])
    return out, sens


def chunked_adjoint(f_ref, a_ref, rate_ref, gamma_ref, out_ref, sens_ref):
    _, sx, sy, sz = out_ref.shape
    halves = sy // 8

    def body(step, carry):
        i = step // halves
        h = pl.multiple_of((step % halves) * 8, 8)
        F = [f_ref[q, i, pl.ds(h, 8), :] for q in range(27)]
        A = [a_ref[q, i, pl.ds(h, 8), :] for q in range(27)]
        om = rate_ref[i, pl.ds(h, 8), :]
        ga = gamma_ref[i, pl.ds(h, 8), :]
        adj, sens = adjoint_rows(F, A, om, ga)
        for q in range(27):
            out_ref[q, i, pl.ds(h, 8), :] = adj[q]
        sens_ref[i, pl.ds(h, 8), :] = sens
        return carry

    lax.fori_loop(0, sx * halves, body, 0)


def next_kernel(cf_ref, ae_ref, *refs):
    hal_f = refs[0:6]
    hal_a = refs[6:12]
    rate_ref, gamma_ref, out_ref, sens_ref, fs, as_ = refs[12:]
    move_into(fs, cf_ref, hal_f, 1)
    move_into(as_, ae_ref, hal_a, -1)
    chunked_adjoint(fs, as_, rate_ref, gamma_ref, out_ref, sens_ref)


def now_kernel(an_ref, f_ref, *refs):
    hal = refs[0:6]
    rate_ref, gamma_ref, out_ref, sens_ref, as_ = refs[6:]
    move_into(as_, an_ref, hal, -1)
    chunked_adjoint(f_ref, as_, rate_ref, gamma_ref, out_ref, sens_ref)


def run_stage(kernel, args, shape, scratch):
    _, sx, sy, sz = shape
    return pl.pallas_call(
        kernel,
        out_shape=(
            jax.ShapeDtypeStruct(shape, jnp.float32),
            jax.ShapeDtypeStruct((sx, sy, sz), jnp.float32),
        ),
        scratch_shapes=[pltpu.VMEM(shape, jnp.float32) for _ in range(scratch)],
    )(*args)


def shards(check_pops, adjoint_end, relax_rate, wall_flag, patch_of_cell, porosity, patch_slot):
    sx, sy, sz = relax_rate.shape
    ids = patch_of_cell[:, :: sy // 2, :: sz // 2]
    table = jnp.stack([porosity, patch_slot.astype(jnp.float32)], axis=1)
    looked = table[ids]
    solid = jnp.broadcast_to(looked[:, :, None, :, None, 0], (sx, 2, sy // 2, 2, sz // 2)).reshape(sx, sy, sz)
    walls = wall_flag.astype(jnp.float32)
    gamma = walls * solid
    post_now, _ = collide(check_pops, relax_rate, gamma)
    hal_f, hal_a = halos([post_now, adjoint_end], [1, -1])
    shape = check_pops.shape
    adj_next, sens_next = run_stage(
        next_kernel, (post_now, adjoint_end) + hal_f + hal_a + (relax_rate, gamma), shape, 2
    )
    (hal_n,) = halos([adj_next], [-1])
    adjoint_start, sens_now = run_stage(now_kernel, (adj_next, check_pops) + hal_n + (relax_rate, gamma), shape, 1)
    density = walls * (sens_next + sens_now)
    boxes = density.reshape(sx, 2, sy // 2, 2, sz // 2).sum(axis=(2, 4))
    parts = jnp.stack([boxes[0], boxes[1 : sx - 1].sum(axis=0), boxes[sx - 1]])
    count = porosity.shape[0]
    devices = lax.axis_size(("gx", "gy", "gz"))
    slots = jnp.stack([looked[0, :, :, 1], looked[1, :, :, 1], looked[sx - 1, :, :, 1]]).reshape(-1)
    hits = (slots[:, None] == jnp.arange(count, dtype=jnp.float32)[None, :]).astype(jnp.float32)
    placed = jnp.sum(parts.reshape(-1)[:, None] * hits, axis=0)
    got = lax.all_to_all(placed.reshape(devices, count // devices), ("gx", "gy", "gz"), 0, 0, tiled=True)
    patch_sens = jnp.sum(got, axis=0)
    return (adjoint_start, patch_sens)


def solution(mesh):
    in_specs = (
        P(None, "gx", "gy", "gz"),
        P(None, "gx", "gy", "gz"),
        P("gx", "gy", "gz"),
        P("gx", "gy", "gz"),
        P("gx", "gy", "gz"),
        P(),
        P(),
    )
    out_specs = (P(None, "gx", "gy", "gz"), P(("gx", "gy", "gz")))
    return jax.shard_map(shards, mesh=mesh, in_specs=in_specs, out_specs=out_specs, check_vma=False)
```

```python
import jax
import jax.numpy as jnp
import numpy as np
from jax import lax
from jax.experimental import pallas as pl
from jax.experimental.pallas import tpu as pltpu
from jax.sharding import PartitionSpec as P


def lattice_table():
    steps = np.array(
        [
            [first, second, third]
            for first in (-1, 0, 1)
            for second in (-1, 0, 1)
            for third in (-1, 0, 1)
        ],
        dtype=np.int64,
    )
    moved = np.abs(steps).sum(axis=1)
    weights = np.array([8.0 / 27.0, 2.0 / 27.0, 1.0 / 54.0, 1.0 / 216.0])[moved]
    return (steps, weights)


STEPS, WEIGHTS = lattice_table()


def collide(pops, rate, gamma):
    steps, weights = lattice_table()
    cube = pops.reshape((3, 3, 3) + pops.shape[1:])
    density = jnp.sum(pops, axis=0)
    mom_x = jnp.sum(cube[2], axis=(0, 1)) - jnp.sum(cube[0], axis=(0, 1))
    mom_y = jnp.sum(cube[:, 2], axis=(0, 1)) - jnp.sum(cube[:, 0], axis=(0, 1))
    mom_z = jnp.sum(cube[:, :, 2], axis=(0, 1)) - jnp.sum(cube[:, :, 0], axis=(0, 1))
    vel_x = mom_x / density
    vel_y = mom_y / density
    vel_z = mom_z / density
    cx = jnp.asarray(steps[:, 0], jnp.float32)[:, None, None, None]
    cy = jnp.asarray(steps[:, 1], jnp.float32)[:, None, None, None]
    cz = jnp.asarray(steps[:, 2], jnp.float32)[:, None, None, None]
    wts = jnp.asarray(weights, jnp.float32)[:, None, None, None]
    along = cx * vel_x + cy * vel_y + cz * vel_z
    speed = vel_x * vel_x + vel_y * vel_y + vel_z * vel_z
    equil = wts * density * (1.0 + 3.0 * along + 4.5 * along * along - 1.5 * speed)
    relaxed = pops - rate * (pops - equil)
    flipped = pops[::-1]
    return ((1.0 - gamma) * relaxed + gamma * flipped, flipped - relaxed)


def halo_exchange(up, down, axis):
    size = lax.axis_size(axis)
    if size == 1:
        return up, down
    if size == 2:
        both = lax.ppermute(jnp.stack([up, down]), axis, [(0, 1), (1, 0)])
        return both[0], both[1]
    lo = lax.ppermute(up, axis, [(i, (i + 1) % size) for i in range(size)])
    hi = lax.ppermute(down, axis, [(i, (i - 1) % size) for i in range(size)])
    return lo, hi


def shifted(cube, lo, hi, d, sign):
    n = cube.shape[3 + d]
    plus = lax.index_in_dim(cube, 1 + sign, axis=d, keepdims=False)
    minus = lax.index_in_dim(cube, 1 - sign, axis=d, keepdims=False)
    still = lax.index_in_dim(cube, 1, axis=d, keepdims=False)
    plus = jnp.concatenate([lo, lax.slice_in_dim(plus, 0, n - 1, axis=2 + d)], axis=2 + d)
    minus = jnp.concatenate([lax.slice_in_dim(minus, 1, n, axis=2 + d), hi], axis=2 + d)
    groups = [None, still, None]
    groups[1 + sign] = plus
    groups[1 - sign] = minus
    return jnp.stack(groups, axis=d)


def faces(cube, sign, d):
    n = cube.shape[3 + d]
    plus = lax.index_in_dim(cube, 1 + sign, axis=d, keepdims=False)
    minus = lax.index_in_dim(cube, 1 - sign, axis=d, keepdims=False)
    return lax.slice_in_dim(plus, n - 1, n, axis=2 + d), lax.slice_in_dim(minus, 0, 1, axis=2 + d)


def halos(fields, signs):
    cubes = [f.reshape((3, 3, 3) + f.shape[1:]) for f in fields]
    sx, sy, sz = cubes[0].shape[3:]
    x_up, x_dn = zip(*[faces(c, s, 0) for c, s in zip(cubes, signs)])
    xlo, xhi = halo_exchange(jnp.stack(x_up), jnp.stack(x_dn), "gx")
    both = jnp.stack(cubes)
    rows = jnp.concatenate([both[..., sy - 1 : sy, :], both[..., 0:1, :]], axis=5)
    cols = jnp.concatenate([both[..., sz - 1 : sz], both[..., 0:1]], axis=6)
    y_up, y_dn = [], []
    for k, s in enumerate(signs):
        top = shifted(rows[k][..., 0:1, :], xlo[k][:, :, :, sy - 1 : sy], xhi[k][:, :, :, sy - 1 : sy], 0, s)
        bot = shifted(rows[k][..., 1:2, :], xlo[k][:, :, :, 0:1], xhi[k][:, :, :, 0:1], 0, s)
        y_up.append(lax.index_in_dim(top, 1 + s, axis=1, keepdims=False))
        y_dn.append(lax.index_in_dim(bot, 1 - s, axis=1, keepdims=False))
    ylo, yhi = halo_exchange(jnp.stack(y_up), jnp.stack(y_dn), "gy")
    z_up, z_dn = [], []
    for k, s in enumerate(signs):
        picked = []
        for at, z0 in ((0, sz - 1), (1, 0)):
            col = cols[k][..., at : at + 1]
            col = shifted(col, xlo[k][..., z0 : z0 + 1], xhi[k][..., z0 : z0 + 1], 0, s)
            col = shifted(col, ylo[k][..., z0 : z0 + 1], yhi[k][..., z0 : z0 + 1], 1, s)
            picked.append(col)
        z_up.append(jnp.swapaxes(lax.index_in_dim(picked[0], 1 + s, axis=2, keepdims=False)[..., 0], -1, -2))
        z_dn.append(jnp.swapaxes(lax.index_in_dim(picked[1], 1 - s, axis=2, keepdims=False)[..., 0], -1, -2))
    zlo, zhi = halo_exchange(jnp.stack(z_up), jnp.stack(z_dn), "gz")
    out = []
    for k in range(len(cubes)):
        out.append(
            (
                xlo[k].reshape(9, sy, sz),
                xhi[k].reshape(9, sy, sz),
                ylo[k].reshape(9, sx, sz),
                yhi[k].reshape(9, sx, sz),
                zlo[k].reshape(9, sy, sx),
                zhi[k].reshape(9, sy, sx),
            )
        )
    return out


def move_into(dst, src, hal, sign):
    xlo, xhi, ylo, yhi, zlo, zhi = hal
    _, sx, sy, sz = src.shape
    rows = lax.broadcasted_iota(jnp.int32, (sy, sz), 0)
    lanes = lax.broadcasted_iota(jnp.int32, (sy, sz), 1)
    for q in range(27):
        cx, cy, cz = (int(v) for v in STEPS[q])
        vx, vy, vz = sign * cx, sign * cy, sign * cz
        if vz == 1:
            zcol = zlo[(cx + 1) * 3 + cy + 1]
        elif vz == -1:
            zcol = zhi[(cx + 1) * 3 + cy + 1]
        for i in range(sx):
            j = i - vx
            if j < 0:
                t = xlo[(cy + 1) * 3 + cz + 1]
            elif j >= sx:
                t = xhi[(cy + 1) * 3 + cz + 1]
            else:
                t = src[q, j]
            if vy == 1:
                t = jnp.where(rows == 0, ylo[(cx + 1) * 3 + cz + 1, pl.ds(i, 1), :], pltpu.roll(t, 1, 0))
            elif vy == -1:
                t = jnp.where(rows == sy - 1, yhi[(cx + 1) * 3 + cz + 1, pl.ds(i, 1), :], pltpu.roll(t, sy - 1, 0))
            if vz == 1:
                t = jnp.where(lanes == 0, zcol[:, i : i + 1], pltpu.roll(t, 1, 1))
            elif vz == -1:
                t = jnp.where(lanes == sz - 1, zcol[:, i : i + 1], pltpu.roll(t, sz - 1, 1))
            dst[q, i] = t


def adjoint_rows(F, A, om, ga):
    rho = sum(F)
    mom = []
    for axis in range(3):
        pos = [F[q] for q in range(27) if STEPS[q, axis] == 1]
        neg = [F[q] for q in range(27) if STEPS[q, axis] == -1]
        mom.append(sum(pos) - sum(neg))
    vel = (mom[0] / rho, mom[1] / rho, mom[2] / rho)
    uu = vel[0] * vel[0] + vel[1] * vel[1] + vel[2] * vel[2]
    sens = 0.0
    e_rho = 0.0
    s0 = 0.0
    sm = [0.0, 0.0, 0.0]
    for q in range(27):
        c = STEPS[q]
        w = float(WEIGHTS[q])
        cu = None
        for axis in range(3):
            if c[axis] == 1:
                cu = vel[axis] if cu is None else cu + vel[axis]
            elif c[axis] == -1:
                cu = -vel[axis] if cu is None else cu - vel[axis]
        if cu is None:
            eq = w * rho * (1.0 - 1.5 * uu)
        else:
            eq = w * rho * (1.0 + 3.0 * cu + 4.5 * cu * cu - 1.5 * uu)
        bgk = F[q] - om * (F[q] - eq)
        sens = sens + A[q] * (F[26 - q] - bgk)
        aw = A[q] * w
        s0 = s0 + aw
        if cu is None:
            e_rho = e_rho + aw * (1.0 + 1.5 * uu)
        else:
            e_rho = e_rho + aw * (1.0 - 4.5 * cu * cu + 1.5 * uu)
            t = aw * (1.0 + 3.0 * cu)
            for axis in range(3):
                if c[axis] == 1:
                    sm[axis] = sm[axis] + t
                elif c[axis] == -1:
                    sm[axis] = sm[axis] - t
    em = [3.0 * sm[axis] - 3.0 * vel[axis] * s0 for axis in range(3)]
    keep = 1.0 - ga
    out = []
    for p in range(27):
        c = STEPS[p]
        g = e_rho
        for axis in range(3):
            if c[axis] == 1:
                g = g + em[axis]
            elif c[axis] == -1:
                g = g - em[axis]
        out.append(keep * ((1.0 - om) * A[p] + om * g) + ga * A[26 - p])
    return out, sens


def chunked_adjoint(f_ref, a_ref, rate_ref, gamma_ref, out_ref, sens_ref):
    _, sx, sy, sz = out_ref.shape
    halves = sy // 8

    def body(step, carry):
        i = step // halves
        h = pl.multiple_of((step % halves) * 8, 8)
        F = [f_ref[q, i, pl.ds(h, 8), :] for q in range(27)]
        A = [a_ref[q, i, pl.ds(h, 8), :] for q in range(27)]
        om = rate_ref[i, pl.ds(h, 8), :]
        ga = gamma_ref[i, pl.ds(h, 8), :]
        adj, sens = adjoint_rows(F, A, om, ga)
        for q in range(27):
            out_ref[q, i, pl.ds(h, 8), :] = adj[q]
        sens_ref[i, pl.ds(h, 8), :] = sens
        return carry

    lax.fori_loop(0, sx * halves, body, 0)


def collide_rows(F, om, ga):
    rho = sum(F)
    mom = []
    for axis in range(3):
        pos = [F[q] for q in range(27) if STEPS[q, axis] == 1]
        neg = [F[q] for q in range(27) if STEPS[q, axis] == -1]
        mom.append(sum(pos) - sum(neg))
    vel = (mom[0] / rho, mom[1] / rho, mom[2] / rho)
    uu = vel[0] * vel[0] + vel[1] * vel[1] + vel[2] * vel[2]
    out = []
    for q in range(27):
        c = STEPS[q]
        w = float(WEIGHTS[q])
        cu = None
        for axis in range(3):
            if c[axis] == 1:
                cu = vel[axis] if cu is None else cu + vel[axis]
            elif c[axis] == -1:
                cu = -vel[axis] if cu is None else cu - vel[axis]
        if cu is None:
            eq = w * rho * (1.0 - 1.5 * uu)
        else:
            eq = w * rho * (1.0 + 3.0 * cu + 4.5 * cu * cu - 1.5 * uu)
        bgk = F[q] - om * (F[q] - eq)
        out.append((1.0 - ga) * bgk + ga * F[26 - q])
    return out


def collide_kernel(f_ref, rate_ref, gamma_ref, out_ref):
    _, sx, sy, sz = out_ref.shape
    halves = sy // 8

    def body(step, carry):
        i = step // halves
        h = pl.multiple_of((step % halves) * 8, 8)
        F = [f_ref[q, i, pl.ds(h, 8), :] for q in range(27)]
        post = collide_rows(F, rate_ref[i, pl.ds(h, 8), :], gamma_ref[i, pl.ds(h, 8), :])
        for q in range(27):
            out_ref[q, i, pl.ds(h, 8), :] = post[q]
        return carry

    lax.fori_loop(0, sx * halves, body, 0)


def next_kernel(cf_ref, ae_ref, *refs):
    hal_f = refs[0:6]
    hal_a = refs[6:12]
    rate_ref, gamma_ref, out_ref, sens_ref, fs, as_ = refs[12:]
    move_into(fs, cf_ref, hal_f, 1)
    move_into(as_, ae_ref, hal_a, -1)
    chunked_adjoint(fs, as_, rate_ref, gamma_ref, out_ref, sens_ref)


def now_kernel(an_ref, f_ref, *refs):
    hal = refs[0:6]
    rate_ref, gamma_ref, out_ref, sens_ref, as_ = refs[6:]
    move_into(as_, an_ref, hal, -1)
    chunked_adjoint(f_ref, as_, rate_ref, gamma_ref, out_ref, sens_ref)


def run_stage(kernel, args, shape, scratch):
    _, sx, sy, sz = shape
    return pl.pallas_call(
        kernel,
        out_shape=(
            jax.ShapeDtypeStruct(shape, jnp.float32),
            jax.ShapeDtypeStruct((sx, sy, sz), jnp.float32),
        ),
        scratch_shapes=[pltpu.VMEM(shape, jnp.float32) for _ in range(scratch)],
    )(*args)


def shards(check_pops, adjoint_end, relax_rate, wall_flag, patch_of_cell, porosity, patch_slot):
    sx, sy, sz = relax_rate.shape
    ids = patch_of_cell[:, :: sy // 2, :: sz // 2]
    table = jnp.stack([porosity, patch_slot.astype(jnp.float32)], axis=1)
    looked = table[ids]
    solid = jnp.broadcast_to(looked[:, :, None, :, None, 0], (sx, 2, sy // 2, 2, sz // 2)).reshape(sx, sy, sz)
    walls = wall_flag.astype(jnp.float32)
    gamma = walls * solid
    post_now = pl.pallas_call(collide_kernel, out_shape=jax.ShapeDtypeStruct(check_pops.shape, jnp.float32))(
        check_pops, relax_rate, gamma
    )
    hal_f, hal_a = halos([post_now, adjoint_end], [1, -1])
    shape = check_pops.shape
    adj_next, sens_next = run_stage(
        next_kernel, (post_now, adjoint_end) + hal_f + hal_a + (relax_rate, gamma), shape, 2
    )
    (hal_n,) = halos([adj_next], [-1])
    adjoint_start, sens_now = run_stage(now_kernel, (adj_next, check_pops) + hal_n + (relax_rate, gamma), shape, 1)
    density = walls * (sens_next + sens_now)
    boxes = density.reshape(sx, 2, sy // 2, 2, sz // 2).sum(axis=(2, 4))
    parts = jnp.stack([boxes[0], boxes[1 : sx - 1].sum(axis=0), boxes[sx - 1]])
    count = porosity.shape[0]
    devices = lax.axis_size(("gx", "gy", "gz"))
    slots = jnp.stack([looked[0, :, :, 1], looked[1, :, :, 1], looked[sx - 1, :, :, 1]]).reshape(-1)
    hits = (slots[:, None] == jnp.arange(count, dtype=jnp.float32)[None, :]).astype(jnp.float32)
    placed = jnp.sum(parts.reshape(-1)[:, None] * hits, axis=0)
    got = lax.all_to_all(placed.reshape(devices, count // devices), ("gx", "gy", "gz"), 0, 0, tiled=True)
    patch_sens = jnp.sum(got, axis=0)
    return (adjoint_start, patch_sens)


def solution(mesh):
    in_specs = (
        P(None, "gx", "gy", "gz"),
        P(None, "gx", "gy", "gz"),
        P("gx", "gy", "gz"),
        P("gx", "gy", "gz"),
        P("gx", "gy", "gz"),
        P(),
        P(),
    )
    out_specs = (P(None, "gx", "gy", "gz"), P(("gx", "gy", "gz")))
    return jax.shard_map(shards, mesh=mesh, in_specs=in_specs, out_specs=out_specs, check_vma=False)
```

```python
import jax
import jax.numpy as jnp
import numpy as np
from jax import lax
from jax.experimental import pallas as pl
from jax.experimental.pallas import tpu as pltpu
from jax.sharding import PartitionSpec as P


def lattice_table():
    steps = np.array(
        [
            [first, second, third]
            for first in (-1, 0, 1)
            for second in (-1, 0, 1)
            for third in (-1, 0, 1)
        ],
        dtype=np.int64,
    )
    moved = np.abs(steps).sum(axis=1)
    weights = np.array([8.0 / 27.0, 2.0 / 27.0, 1.0 / 54.0, 1.0 / 216.0])[moved]
    return (steps, weights)


STEPS, WEIGHTS = lattice_table()


def collide(pops, rate, gamma):
    steps, weights = lattice_table()
    cube = pops.reshape((3, 3, 3) + pops.shape[1:])
    density = jnp.sum(pops, axis=0)
    mom_x = jnp.sum(cube[2], axis=(0, 1)) - jnp.sum(cube[0], axis=(0, 1))
    mom_y = jnp.sum(cube[:, 2], axis=(0, 1)) - jnp.sum(cube[:, 0], axis=(0, 1))
    mom_z = jnp.sum(cube[:, :, 2], axis=(0, 1)) - jnp.sum(cube[:, :, 0], axis=(0, 1))
    vel_x = mom_x / density
    vel_y = mom_y / density
    vel_z = mom_z / density
    cx = jnp.asarray(steps[:, 0], jnp.float32)[:, None, None, None]
    cy = jnp.asarray(steps[:, 1], jnp.float32)[:, None, None, None]
    cz = jnp.asarray(steps[:, 2], jnp.float32)[:, None, None, None]
    wts = jnp.asarray(weights, jnp.float32)[:, None, None, None]
    along = cx * vel_x + cy * vel_y + cz * vel_z
    speed = vel_x * vel_x + vel_y * vel_y + vel_z * vel_z
    equil = wts * density * (1.0 + 3.0 * along + 4.5 * along * along - 1.5 * speed)
    relaxed = pops - rate * (pops - equil)
    flipped = pops[::-1]
    return ((1.0 - gamma) * relaxed + gamma * flipped, flipped - relaxed)


def halo_exchange(up, down, axis):
    size = lax.axis_size(axis)
    if size == 1:
        return up, down
    if size == 2:
        both = lax.ppermute(jnp.stack([up, down]), axis, [(0, 1), (1, 0)])
        return both[0], both[1]
    lo = lax.ppermute(up, axis, [(i, (i + 1) % size) for i in range(size)])
    hi = lax.ppermute(down, axis, [(i, (i - 1) % size) for i in range(size)])
    return lo, hi


def shifted(cube, lo, hi, d, sign):
    n = cube.shape[3 + d]
    plus = lax.index_in_dim(cube, 1 + sign, axis=d, keepdims=False)
    minus = lax.index_in_dim(cube, 1 - sign, axis=d, keepdims=False)
    still = lax.index_in_dim(cube, 1, axis=d, keepdims=False)
    plus = jnp.concatenate([lo, lax.slice_in_dim(plus, 0, n - 1, axis=2 + d)], axis=2 + d)
    minus = jnp.concatenate([lax.slice_in_dim(minus, 1, n, axis=2 + d), hi], axis=2 + d)
    groups = [None, still, None]
    groups[1 + sign] = plus
    groups[1 - sign] = minus
    return jnp.stack(groups, axis=d)


def faces(cube, sign, d):
    n = cube.shape[3 + d]
    plus = lax.index_in_dim(cube, 1 + sign, axis=d, keepdims=False)
    minus = lax.index_in_dim(cube, 1 - sign, axis=d, keepdims=False)
    return lax.slice_in_dim(plus, n - 1, n, axis=2 + d), lax.slice_in_dim(minus, 0, 1, axis=2 + d)


def halos(fields, signs):
    cubes = [f.reshape((3, 3, 3) + f.shape[1:]) for f in fields]
    sx, sy, sz = cubes[0].shape[3:]
    x_up, x_dn = zip(*[faces(c, s, 0) for c, s in zip(cubes, signs)])
    xlo, xhi = halo_exchange(jnp.stack(x_up), jnp.stack(x_dn), "gx")
    both = jnp.stack(cubes)
    rows = jnp.concatenate([both[..., sy - 1 : sy, :], both[..., 0:1, :]], axis=5)
    cols = jnp.concatenate([both[..., sz - 1 : sz], both[..., 0:1]], axis=6)
    y_up, y_dn = [], []
    for k, s in enumerate(signs):
        top = shifted(rows[k][..., 0:1, :], xlo[k][:, :, :, sy - 1 : sy], xhi[k][:, :, :, sy - 1 : sy], 0, s)
        bot = shifted(rows[k][..., 1:2, :], xlo[k][:, :, :, 0:1], xhi[k][:, :, :, 0:1], 0, s)
        y_up.append(lax.index_in_dim(top, 1 + s, axis=1, keepdims=False))
        y_dn.append(lax.index_in_dim(bot, 1 - s, axis=1, keepdims=False))
    ylo, yhi = halo_exchange(jnp.stack(y_up), jnp.stack(y_dn), "gy")
    z_up, z_dn = [], []
    for k, s in enumerate(signs):
        picked = []
        for at, z0 in ((0, sz - 1), (1, 0)):
            col = cols[k][..., at : at + 1]
            col = shifted(col, xlo[k][..., z0 : z0 + 1], xhi[k][..., z0 : z0 + 1], 0, s)
            col = shifted(col, ylo[k][..., z0 : z0 + 1], yhi[k][..., z0 : z0 + 1], 1, s)
            picked.append(col)
        z_up.append(jnp.swapaxes(lax.index_in_dim(picked[0], 1 + s, axis=2, keepdims=False)[..., 0], -1, -2))
        z_dn.append(jnp.swapaxes(lax.index_in_dim(picked[1], 1 - s, axis=2, keepdims=False)[..., 0], -1, -2))
    zlo, zhi = halo_exchange(jnp.stack(z_up), jnp.stack(z_dn), "gz")
    nf = len(cubes)
    return (
        xlo.reshape(nf * 9, sy, sz),
        xhi.reshape(nf * 9, sy, sz),
        ylo.reshape(nf * 9, sx, sz),
        yhi.reshape(nf * 9, sx, sz),
        zlo.reshape(nf * 9, sy, sx),
        zhi.reshape(nf * 9, sy, sx),
    )


def move_into(dst, src, hal, sign, base):
    xlo, xhi, ylo, yhi, zlo, zhi = hal
    _, sx, sy, sz = src.shape
    rows = lax.broadcasted_iota(jnp.int32, (sy, sz), 0)
    lanes = lax.broadcasted_iota(jnp.int32, (sy, sz), 1)
    for q in range(27):
        cx, cy, cz = (int(v) for v in STEPS[q])
        vx, vy, vz = sign * cx, sign * cy, sign * cz
        if vz == 1:
            zcol = zlo[base + (cx + 1) * 3 + cy + 1]
        elif vz == -1:
            zcol = zhi[base + (cx + 1) * 3 + cy + 1]
        for i in range(sx):
            j = i - vx
            if j < 0:
                t = xlo[base + (cy + 1) * 3 + cz + 1]
            elif j >= sx:
                t = xhi[base + (cy + 1) * 3 + cz + 1]
            else:
                t = src[q, j]
            if vy == 1:
                t = jnp.where(rows == 0, ylo[base + (cx + 1) * 3 + cz + 1, pl.ds(i, 1), :], pltpu.roll(t, 1, 0))
            elif vy == -1:
                t = jnp.where(rows == sy - 1, yhi[base + (cx + 1) * 3 + cz + 1, pl.ds(i, 1), :], pltpu.roll(t, sy - 1, 0))
            if vz == 1:
                t = jnp.where(lanes == 0, zcol[:, i : i + 1], pltpu.roll(t, 1, 1))
            elif vz == -1:
                t = jnp.where(lanes == sz - 1, zcol[:, i : i + 1], pltpu.roll(t, sz - 1, 1))
            dst[q, i] = t


def adjoint_rows(F, A, om, ga):
    rho = sum(F)
    mom = []
    for axis in range(3):
        pos = [F[q] for q in range(27) if STEPS[q, axis] == 1]
        neg = [F[q] for q in range(27) if STEPS[q, axis] == -1]
        mom.append(sum(pos) - sum(neg))
    vel = (mom[0] / rho, mom[1] / rho, mom[2] / rho)
    uu = vel[0] * vel[0] + vel[1] * vel[1] + vel[2] * vel[2]
    sens = 0.0
    e_rho = 0.0
    s0 = 0.0
    sm = [0.0, 0.0, 0.0]
    for q in range(27):
        c = STEPS[q]
        w = float(WEIGHTS[q])
        cu = None
        for axis in range(3):
            if c[axis] == 1:
                cu = vel[axis] if cu is None else cu + vel[axis]
            elif c[axis] == -1:
                cu = -vel[axis] if cu is None else cu - vel[axis]
        if cu is None:
            eq = w * rho * (1.0 - 1.5 * uu)
        else:
            eq = w * rho * (1.0 + 3.0 * cu + 4.5 * cu * cu - 1.5 * uu)
        bgk = F[q] - om * (F[q] - eq)
        sens = sens + A[q] * (F[26 - q] - bgk)
        aw = A[q] * w
        s0 = s0 + aw
        if cu is None:
            e_rho = e_rho + aw * (1.0 + 1.5 * uu)
        else:
            e_rho = e_rho + aw * (1.0 - 4.5 * cu * cu + 1.5 * uu)
            t = aw * (1.0 + 3.0 * cu)
            for axis in range(3):
                if c[axis] == 1:
                    sm[axis] = sm[axis] + t
                elif c[axis] == -1:
                    sm[axis] = sm[axis] - t
    em = [3.0 * sm[axis] - 3.0 * vel[axis] * s0 for axis in range(3)]
    keep = 1.0 - ga
    out = []
    for p in range(27):
        c = STEPS[p]
        g = e_rho
        for axis in range(3):
            if c[axis] == 1:
                g = g + em[axis]
            elif c[axis] == -1:
                g = g - em[axis]
        out.append(keep * ((1.0 - om) * A[p] + om * g) + ga * A[26 - p])
    return out, sens


def chunked_adjoint(f_ref, a_ref, rate_ref, gamma_ref, out_ref, sens_ref):
    _, sx, sy, sz = out_ref.shape
    halves = sy // 8

    def body(step, carry):
        i = step // halves
        h = pl.multiple_of((step % halves) * 8, 8)
        F = [f_ref[q, i, pl.ds(h, 8), :] for q in range(27)]
        A = [a_ref[q, i, pl.ds(h, 8), :] for q in range(27)]
        om = rate_ref[i, pl.ds(h, 8), :]
        ga = gamma_ref[i, pl.ds(h, 8), :]
        adj, sens = adjoint_rows(F, A, om, ga)
        for q in range(27):
            out_ref[q, i, pl.ds(h, 8), :] = adj[q]
        sens_ref[i, pl.ds(h, 8), :] = sens
        return carry

    lax.fori_loop(0, sx * halves, body, 0)


def next_kernel(cf_ref, ae_ref, *refs):
    hal = refs[0:6]
    rate_ref, gamma_ref, out_ref, sens_ref, fs, as_ = refs[6:]
    move_into(fs, cf_ref, hal, 1, 0)
    move_into(as_, ae_ref, hal, -1, 9)
    chunked_adjoint(fs, as_, rate_ref, gamma_ref, out_ref, sens_ref)


def now_kernel(an_ref, f_ref, *refs):
    hal = refs[0:6]
    rate_ref, gamma_ref, out_ref, sens_ref, as_ = refs[6:]
    move_into(as_, an_ref, hal, -1, 0)
    chunked_adjoint(f_ref, as_, rate_ref, gamma_ref, out_ref, sens_ref)


def run_stage(kernel, args, shape, scratch):
    _, sx, sy, sz = shape
    return pl.pallas_call(
        kernel,
        out_shape=(
            jax.ShapeDtypeStruct(shape, jnp.float32),
            jax.ShapeDtypeStruct((sx, sy, sz), jnp.float32),
        ),
        scratch_shapes=[pltpu.VMEM(shape, jnp.float32) for _ in range(scratch)],
    )(*args)


def shards(check_pops, adjoint_end, relax_rate, wall_flag, patch_of_cell, porosity, patch_slot):
    sx, sy, sz = relax_rate.shape
    ids = patch_of_cell[:, :: sy // 2, :: sz // 2]
    table = jnp.stack([porosity, patch_slot.astype(jnp.float32)], axis=1)
    looked = table[ids]
    solid = jnp.broadcast_to(looked[:, :, None, :, None, 0], (sx, 2, sy // 2, 2, sz // 2)).reshape(sx, sy, sz)
    walls = wall_flag.astype(jnp.float32)
    gamma = walls * solid
    post_now, _ = collide(check_pops, relax_rate, gamma)
    hal = halos([post_now, adjoint_end], [1, -1])
    shape = check_pops.shape
    adj_next, sens_next = run_stage(
        next_kernel, (post_now, adjoint_end) + hal + (relax_rate, gamma), shape, 2
    )
    hal_n = halos([adj_next], [-1])
    adjoint_start, sens_now = run_stage(now_kernel, (adj_next, check_pops) + hal_n + (relax_rate, gamma), shape, 1)
    density = walls * (sens_next + sens_now)
    boxes = density.reshape(sx, 2, sy // 2, 2, sz // 2).sum(axis=(2, 4))
    parts = jnp.stack([boxes[0], boxes[1 : sx - 1].sum(axis=0), boxes[sx - 1]])
    count = porosity.shape[0]
    devices = lax.axis_size(("gx", "gy", "gz"))
    slots = jnp.stack([looked[0, :, :, 1], looked[1, :, :, 1], looked[sx - 1, :, :, 1]]).reshape(-1)
    hits = (slots[:, None] == jnp.arange(count, dtype=jnp.float32)[None, :]).astype(jnp.float32)
    placed = jnp.sum(parts.reshape(-1)[:, None] * hits, axis=0)
    got = lax.all_to_all(placed.reshape(devices, count // devices), ("gx", "gy", "gz"), 0, 0, tiled=True)
    patch_sens = jnp.sum(got, axis=0)
    return (adjoint_start, patch_sens)


def solution(mesh):
    in_specs = (
        P(None, "gx", "gy", "gz"),
        P(None, "gx", "gy", "gz"),
        P("gx", "gy", "gz"),
        P("gx", "gy", "gz"),
        P("gx", "gy", "gz"),
        P(),
        P(),
    )
    out_specs = (P(None, "gx", "gy", "gz"), P(("gx", "gy", "gz")))
    return jax.shard_map(shards, mesh=mesh, in_specs=in_specs, out_specs=out_specs, check_vma=False)
```

```python
import jax
import jax.numpy as jnp
import numpy as np
from jax import lax
from jax.experimental import pallas as pl
from jax.experimental.pallas import tpu as pltpu
from jax.sharding import PartitionSpec as P


def lattice_table():
    steps = np.array(
        [
            [first, second, third]
            for first in (-1, 0, 1)
            for second in (-1, 0, 1)
            for third in (-1, 0, 1)
        ],
        dtype=np.int64,
    )
    moved = np.abs(steps).sum(axis=1)
    weights = np.array([8.0 / 27.0, 2.0 / 27.0, 1.0 / 54.0, 1.0 / 216.0])[moved]
    return (steps, weights)


STEPS, WEIGHTS = lattice_table()


def collide(pops, rate, gamma):
    steps, weights = lattice_table()
    cube = pops.reshape((3, 3, 3) + pops.shape[1:])
    density = jnp.sum(pops, axis=0)
    mom_x = jnp.sum(cube[2], axis=(0, 1)) - jnp.sum(cube[0], axis=(0, 1))
    mom_y = jnp.sum(cube[:, 2], axis=(0, 1)) - jnp.sum(cube[:, 0], axis=(0, 1))
    mom_z = jnp.sum(cube[:, :, 2], axis=(0, 1)) - jnp.sum(cube[:, :, 0], axis=(0, 1))
    vel_x = mom_x / density
    vel_y = mom_y / density
    vel_z = mom_z / density
    cx = jnp.asarray(steps[:, 0], jnp.float32)[:, None, None, None]
    cy = jnp.asarray(steps[:, 1], jnp.float32)[:, None, None, None]
    cz = jnp.asarray(steps[:, 2], jnp.float32)[:, None, None, None]
    wts = jnp.asarray(weights, jnp.float32)[:, None, None, None]
    along = cx * vel_x + cy * vel_y + cz * vel_z
    speed = vel_x * vel_x + vel_y * vel_y + vel_z * vel_z
    equil = wts * density * (1.0 + 3.0 * along + 4.5 * along * along - 1.5 * speed)
    relaxed = pops - rate * (pops - equil)
    flipped = pops[::-1]
    return ((1.0 - gamma) * relaxed + gamma * flipped, flipped - relaxed)


def halo_exchange(up, down, axis):
    size = lax.axis_size(axis)
    if size == 1:
        return up, down
    if size == 2:
        both = lax.ppermute(jnp.stack([up, down]), axis, [(0, 1), (1, 0)])
        return both[0], both[1]
    lo = lax.ppermute(up, axis, [(i, (i + 1) % size) for i in range(size)])
    hi = lax.ppermute(down, axis, [(i, (i - 1) % size) for i in range(size)])
    return lo, hi


def shifted(cube, lo, hi, d, sign):
    n = cube.shape[3 + d]
    plus = lax.index_in_dim(cube, 1 + sign, axis=d, keepdims=False)
    minus = lax.index_in_dim(cube, 1 - sign, axis=d, keepdims=False)
    still = lax.index_in_dim(cube, 1, axis=d, keepdims=False)
    plus = jnp.concatenate([lo, lax.slice_in_dim(plus, 0, n - 1, axis=2 + d)], axis=2 + d)
    minus = jnp.concatenate([lax.slice_in_dim(minus, 1, n, axis=2 + d), hi], axis=2 + d)
    groups = [None, still, None]
    groups[1 + sign] = plus
    groups[1 - sign] = minus
    return jnp.stack(groups, axis=d)


def faces(cube, sign, d):
    n = cube.shape[3 + d]
    plus = lax.index_in_dim(cube, 1 + sign, axis=d, keepdims=False)
    minus = lax.index_in_dim(cube, 1 - sign, axis=d, keepdims=False)
    return lax.slice_in_dim(plus, n - 1, n, axis=2 + d), lax.slice_in_dim(minus, 0, 1, axis=2 + d)


def halos(fields, signs):
    cubes = [f.reshape((3, 3, 3) + f.shape[1:]) for f in fields]
    sx, sy, sz = cubes[0].shape[3:]
    x_up, x_dn = zip(*[faces(c, s, 0) for c, s in zip(cubes, signs)])
    xlo, xhi = halo_exchange(jnp.stack(x_up), jnp.stack(x_dn), "gx")
    both = jnp.stack(cubes)
    rows = jnp.concatenate([both[..., sy - 1 : sy, :], both[..., 0:1, :]], axis=5)
    lane = lax.broadcasted_iota(jnp.int32, both.shape, both.ndim - 1)
    cols = [jnp.sum(jnp.where(lane == z0, both, 0.0), axis=-1) for z0 in (sz - 1, 0)]
    y_up, y_dn = [], []
    for k, s in enumerate(signs):
        top = shifted(rows[k][..., 0:1, :], xlo[k][:, :, :, sy - 1 : sy], xhi[k][:, :, :, sy - 1 : sy], 0, s)
        bot = shifted(rows[k][..., 1:2, :], xlo[k][:, :, :, 0:1], xhi[k][:, :, :, 0:1], 0, s)
        y_up.append(lax.index_in_dim(top, 1 + s, axis=1, keepdims=False))
        y_dn.append(lax.index_in_dim(bot, 1 - s, axis=1, keepdims=False))
    ylo, yhi = halo_exchange(jnp.stack(y_up), jnp.stack(y_dn), "gy")
    z_up, z_dn = [], []
    for k, s in enumerate(signs):
        picked = []
        for at, z0 in ((0, sz - 1), (1, 0)):
            col = shifted(cols[at][k], xlo[k][..., z0], xhi[k][..., z0], 0, s)
            col = shifted(col, ylo[k][..., z0], yhi[k][..., z0], 1, s)
            picked.append(col)
        z_up.append(jnp.swapaxes(lax.index_in_dim(picked[0], 1 + s, axis=2, keepdims=False), -1, -2))
        z_dn.append(jnp.swapaxes(lax.index_in_dim(picked[1], 1 - s, axis=2, keepdims=False), -1, -2))
    zlo, zhi = halo_exchange(jnp.stack(z_up), jnp.stack(z_dn), "gz")
    nf = len(cubes)
    return (
        xlo.reshape(nf * 9, sy, sz),
        xhi.reshape(nf * 9, sy, sz),
        ylo.reshape(nf * 9, sx, sz),
        yhi.reshape(nf * 9, sx, sz),
        zlo.reshape(nf * 9, sy, sx),
        zhi.reshape(nf * 9, sy, sx),
    )


def move_into(dst, src, hal, sign, base):
    xlo, xhi, ylo, yhi, zlo, zhi = hal
    _, sx, sy, sz = src.shape
    rows = lax.broadcasted_iota(jnp.int32, (sy, sz), 0)
    lanes = lax.broadcasted_iota(jnp.int32, (sy, sz), 1)
    for q in range(27):
        cx, cy, cz = (int(v) for v in STEPS[q])
        vx, vy, vz = sign * cx, sign * cy, sign * cz
        if vz == 1:
            zcol = zlo[base + (cx + 1) * 3 + cy + 1]
        elif vz == -1:
            zcol = zhi[base + (cx + 1) * 3 + cy + 1]
        for i in range(sx):
            j = i - vx
            if j < 0:
                t = xlo[base + (cy + 1) * 3 + cz + 1]
            elif j >= sx:
                t = xhi[base + (cy + 1) * 3 + cz + 1]
            else:
                t = src[q, j]
            if vy == 1:
                t = jnp.where(rows == 0, ylo[base + (cx + 1) * 3 + cz + 1, pl.ds(i, 1), :], pltpu.roll(t, 1, 0))
            elif vy == -1:
                t = jnp.where(rows == sy - 1, yhi[base + (cx + 1) * 3 + cz + 1, pl.ds(i, 1), :], pltpu.roll(t, sy - 1, 0))
            if vz == 1:
                t = jnp.where(lanes == 0, zcol[:, i : i + 1], pltpu.roll(t, 1, 1))
            elif vz == -1:
                t = jnp.where(lanes == sz - 1, zcol[:, i : i + 1], pltpu.roll(t, sz - 1, 1))
            dst[q, i] = t


def adjoint_rows(F, A, om, ga):
    rho = sum(F)
    mom = []
    for axis in range(3):
        pos = [F[q] for q in range(27) if STEPS[q, axis] == 1]
        neg = [F[q] for q in range(27) if STEPS[q, axis] == -1]
        mom.append(sum(pos) - sum(neg))
    vel = (mom[0] / rho, mom[1] / rho, mom[2] / rho)
    uu = vel[0] * vel[0] + vel[1] * vel[1] + vel[2] * vel[2]
    sens = 0.0
    e_rho = 0.0
    s0 = 0.0
    sm = [0.0, 0.0, 0.0]
    for q in range(27):
        c = STEPS[q]
        w = float(WEIGHTS[q])
        cu = None
        for axis in range(3):
            if c[axis] == 1:
                cu = vel[axis] if cu is None else cu + vel[axis]
            elif c[axis] == -1:
                cu = -vel[axis] if cu is None else cu - vel[axis]
        if cu is None:
            eq = w * rho * (1.0 - 1.5 * uu)
        else:
            eq = w * rho * (1.0 + 3.0 * cu + 4.5 * cu * cu - 1.5 * uu)
        bgk = F[q] - om * (F[q] - eq)
        sens = sens + A[q] * (F[26 - q] - bgk)
        aw = A[q] * w
        s0 = s0 + aw
        if cu is None:
            e_rho = e_rho + aw * (1.0 + 1.5 * uu)
        else:
            e_rho = e_rho + aw * (1.0 - 4.5 * cu * cu + 1.5 * uu)
            t = aw * (1.0 + 3.0 * cu)
            for axis in range(3):
                if c[axis] == 1:
                    sm[axis] = sm[axis] + t
                elif c[axis] == -1:
                    sm[axis] = sm[axis] - t
    em = [3.0 * sm[axis] - 3.0 * vel[axis] * s0 for axis in range(3)]
    keep = 1.0 - ga
    out = []
    for p in range(27):
        c = STEPS[p]
        g = e_rho
        for axis in range(3):
            if c[axis] == 1:
                g = g + em[axis]
            elif c[axis] == -1:
                g = g - em[axis]
        out.append(keep * ((1.0 - om) * A[p] + om * g) + ga * A[26 - p])
    return out, sens


def chunked_adjoint(f_ref, a_ref, rate_ref, gamma_ref, out_ref, sens_ref):
    _, sx, sy, sz = out_ref.shape
    halves = sy // 8

    def body(step, carry):
        i = step // halves
        h = pl.multiple_of((step % halves) * 8, 8)
        F = [f_ref[q, i, pl.ds(h, 8), :] for q in range(27)]
        A = [a_ref[q, i, pl.ds(h, 8), :] for q in range(27)]
        om = rate_ref[i, pl.ds(h, 8), :]
        ga = gamma_ref[i, pl.ds(h, 8), :]
        adj, sens = adjoint_rows(F, A, om, ga)
        for q in range(27):
            out_ref[q, i, pl.ds(h, 8), :] = adj[q]
        sens_ref[i, pl.ds(h, 8), :] = sens
        return carry

    lax.fori_loop(0, sx * halves, body, 0)


def next_kernel(cf_ref, ae_ref, *refs):
    hal = refs[0:6]
    rate_ref, gamma_ref, out_ref, sens_ref, fs, as_ = refs[6:]
    move_into(fs, cf_ref, hal, 1, 0)
    move_into(as_, ae_ref, hal, -1, 9)
    chunked_adjoint(fs, as_, rate_ref, gamma_ref, out_ref, sens_ref)


def now_kernel(an_ref, f_ref, *refs):
    hal = refs[0:6]
    rate_ref, gamma_ref, out_ref, sens_ref, as_ = refs[6:]
    move_into(as_, an_ref, hal, -1, 0)
    chunked_adjoint(f_ref, as_, rate_ref, gamma_ref, out_ref, sens_ref)


def run_stage(kernel, args, shape, scratch):
    _, sx, sy, sz = shape
    return pl.pallas_call(
        kernel,
        out_shape=(
            jax.ShapeDtypeStruct(shape, jnp.float32),
            jax.ShapeDtypeStruct((sx, sy, sz), jnp.float32),
        ),
        scratch_shapes=[pltpu.VMEM(shape, jnp.float32) for _ in range(scratch)],
    )(*args)


def shards(check_pops, adjoint_end, relax_rate, wall_flag, patch_of_cell, porosity, patch_slot):
    sx, sy, sz = relax_rate.shape
    ids = patch_of_cell[:, :: sy // 2, :: sz // 2]
    table = jnp.stack([porosity, patch_slot.astype(jnp.float32)], axis=1)
    looked = table[ids]
    solid = jnp.broadcast_to(looked[:, :, None, :, None, 0], (sx, 2, sy // 2, 2, sz // 2)).reshape(sx, sy, sz)
    walls = wall_flag.astype(jnp.float32)
    gamma = walls * solid
    post_now, _ = collide(check_pops, relax_rate, gamma)
    hal = halos([post_now, adjoint_end], [1, -1])
    shape = check_pops.shape
    adj_next, sens_next = run_stage(
        next_kernel, (post_now, adjoint_end) + hal + (relax_rate, gamma), shape, 2
    )
    hal_n = halos([adj_next], [-1])
    adjoint_start, sens_now = run_stage(now_kernel, (adj_next, check_pops) + hal_n + (relax_rate, gamma), shape, 1)
    density = walls * (sens_next + sens_now)
    boxes = density.reshape(sx, 2, sy // 2, 2, sz // 2).sum(axis=(2, 4))
    parts = jnp.stack([boxes[0], boxes[1 : sx - 1].sum(axis=0), boxes[sx - 1]])
    count = porosity.shape[0]
    devices = lax.axis_size(("gx", "gy", "gz"))
    slots = jnp.stack([looked[0, :, :, 1], looked[1, :, :, 1], looked[sx - 1, :, :, 1]]).reshape(-1)
    hits = (slots[:, None] == jnp.arange(count, dtype=jnp.float32)[None, :]).astype(jnp.float32)
    placed = jnp.sum(parts.reshape(-1)[:, None] * hits, axis=0)
    got = lax.all_to_all(placed.reshape(devices, count // devices), ("gx", "gy", "gz"), 0, 0, tiled=True)
    patch_sens = jnp.sum(got, axis=0)
    return (adjoint_start, patch_sens)


def solution(mesh):
    in_specs = (
        P(None, "gx", "gy", "gz"),
        P(None, "gx", "gy", "gz"),
        P("gx", "gy", "gz"),
        P("gx", "gy", "gz"),
        P("gx", "gy", "gz"),
        P(),
        P(),
    )
    out_specs = (P(None, "gx", "gy", "gz"), P(("gx", "gy", "gz")))
    return jax.shard_map(shards, mesh=mesh, in_specs=in_specs, out_specs=out_specs, check_vma=False)
```

```python
import jax
import jax.numpy as jnp
import numpy as np
from jax import lax
from jax.experimental import pallas as pl
from jax.experimental.pallas import tpu as pltpu
from jax.sharding import PartitionSpec as P


def lattice_table():
    steps = np.array(
        [
            [first, second, third]
            for first in (-1, 0, 1)
            for second in (-1, 0, 1)
            for third in (-1, 0, 1)
        ],
        dtype=np.int64,
    )
    moved = np.abs(steps).sum(axis=1)
    weights = np.array([8.0 / 27.0, 2.0 / 27.0, 1.0 / 54.0, 1.0 / 216.0])[moved]
    return (steps, weights)


STEPS, WEIGHTS = lattice_table()


def collide(pops, rate, gamma):
    steps, weights = lattice_table()
    cube = pops.reshape((3, 3, 3) + pops.shape[1:])
    density = jnp.sum(pops, axis=0)
    mom_x = jnp.sum(cube[2], axis=(0, 1)) - jnp.sum(cube[0], axis=(0, 1))
    mom_y = jnp.sum(cube[:, 2], axis=(0, 1)) - jnp.sum(cube[:, 0], axis=(0, 1))
    mom_z = jnp.sum(cube[:, :, 2], axis=(0, 1)) - jnp.sum(cube[:, :, 0], axis=(0, 1))
    vel_x = mom_x / density
    vel_y = mom_y / density
    vel_z = mom_z / density
    cx = jnp.asarray(steps[:, 0], jnp.float32)[:, None, None, None]
    cy = jnp.asarray(steps[:, 1], jnp.float32)[:, None, None, None]
    cz = jnp.asarray(steps[:, 2], jnp.float32)[:, None, None, None]
    wts = jnp.asarray(weights, jnp.float32)[:, None, None, None]
    along = cx * vel_x + cy * vel_y + cz * vel_z
    speed = vel_x * vel_x + vel_y * vel_y + vel_z * vel_z
    equil = wts * density * (1.0 + 3.0 * along + 4.5 * along * along - 1.5 * speed)
    relaxed = pops - rate * (pops - equil)
    flipped = pops[::-1]
    return ((1.0 - gamma) * relaxed + gamma * flipped, flipped - relaxed)


def halo_exchange(up, down, axis):
    size = lax.axis_size(axis)
    if size == 1:
        return up, down
    if size == 2:
        both = lax.ppermute(jnp.stack([up, down]), axis, [(0, 1), (1, 0)])
        return both[0], both[1]
    lo = lax.ppermute(up, axis, [(i, (i + 1) % size) for i in range(size)])
    hi = lax.ppermute(down, axis, [(i, (i - 1) % size) for i in range(size)])
    return lo, hi


def shifted(cube, lo, hi, d, sign):
    n = cube.shape[3 + d]
    plus = lax.index_in_dim(cube, 1 + sign, axis=d, keepdims=False)
    minus = lax.index_in_dim(cube, 1 - sign, axis=d, keepdims=False)
    still = lax.index_in_dim(cube, 1, axis=d, keepdims=False)
    plus = jnp.concatenate([lo, lax.slice_in_dim(plus, 0, n - 1, axis=2 + d)], axis=2 + d)
    minus = jnp.concatenate([lax.slice_in_dim(minus, 1, n, axis=2 + d), hi], axis=2 + d)
    groups = [None, still, None]
    groups[1 + sign] = plus
    groups[1 - sign] = minus
    return jnp.stack(groups, axis=d)


def faces(cube, sign, d):
    n = cube.shape[3 + d]
    plus = lax.index_in_dim(cube, 1 + sign, axis=d, keepdims=False)
    minus = lax.index_in_dim(cube, 1 - sign, axis=d, keepdims=False)
    return lax.slice_in_dim(plus, n - 1, n, axis=2 + d), lax.slice_in_dim(minus, 0, 1, axis=2 + d)


def halos(fields, signs):
    cubes = [f.reshape((3, 3, 3) + f.shape[1:]) for f in fields]
    sx, sy, sz = cubes[0].shape[3:]
    x_up, x_dn = zip(*[faces(c, s, 0) for c, s in zip(cubes, signs)])
    xlo, xhi = halo_exchange(jnp.stack(x_up), jnp.stack(x_dn), "gx")
    both = jnp.stack(cubes)
    rows = jnp.concatenate([both[..., sy - 1 : sy, :], both[..., 0:1, :]], axis=5)
    cols = jnp.concatenate([both[..., sz - 1 : sz], both[..., 0:1]], axis=6)
    y_up, y_dn = [], []
    for k, s in enumerate(signs):
        top = shifted(rows[k][..., 0:1, :], xlo[k][:, :, :, sy - 1 : sy], xhi[k][:, :, :, sy - 1 : sy], 0, s)
        bot = shifted(rows[k][..., 1:2, :], xlo[k][:, :, :, 0:1], xhi[k][:, :, :, 0:1], 0, s)
        y_up.append(lax.index_in_dim(top, 1 + s, axis=1, keepdims=False))
        y_dn.append(lax.index_in_dim(bot, 1 - s, axis=1, keepdims=False))
    ylo, yhi = halo_exchange(jnp.stack(y_up), jnp.stack(y_dn), "gy")
    z_up, z_dn = [], []
    for k, s in enumerate(signs):
        picked = []
        for at, z0 in ((0, sz - 1), (1, 0)):
            col = cols[k][..., at : at + 1]
            col = shifted(col, xlo[k][..., z0 : z0 + 1], xhi[k][..., z0 : z0 + 1], 0, s)
            col = shifted(col, ylo[k][..., z0 : z0 + 1], yhi[k][..., z0 : z0 + 1], 1, s)
            picked.append(col)
        z_up.append(jnp.swapaxes(lax.index_in_dim(picked[0], 1 + s, axis=2, keepdims=False)[..., 0], -1, -2))
        z_dn.append(jnp.swapaxes(lax.index_in_dim(picked[1], 1 - s, axis=2, keepdims=False)[..., 0], -1, -2))
    zlo, zhi = halo_exchange(jnp.stack(z_up), jnp.stack(z_dn), "gz")
    nf = len(cubes)
    return (
        xlo.reshape(nf * 9, sy, sz),
        xhi.reshape(nf * 9, sy, sz),
        ylo.reshape(nf * 9, sx, sz),
        yhi.reshape(nf * 9, sx, sz),
        zlo.reshape(nf * 9, sy, sx),
        zhi.reshape(nf * 9, sy, sx),
    )


def move_into(dst, src, hal, sign, base):
    xlo, xhi, ylo, yhi, zlo, zhi = hal
    _, sx, sy, sz = src.shape
    rows = lax.broadcasted_iota(jnp.int32, (sy, sz), 0)
    lanes = lax.broadcasted_iota(jnp.int32, (sy, sz), 1)
    for q in range(27):
        cx, cy, cz = (int(v) for v in STEPS[q])
        vx, vy, vz = sign * cx, sign * cy, sign * cz
        if vz == 1:
            zcol = zlo[base + (cx + 1) * 3 + cy + 1]
        elif vz == -1:
            zcol = zhi[base + (cx + 1) * 3 + cy + 1]
        for i in range(sx):
            j = i - vx
            if j < 0:
                t = xlo[base + (cy + 1) * 3 + cz + 1]
            elif j >= sx:
                t = xhi[base + (cy + 1) * 3 + cz + 1]
            else:
                t = src[q, j]
            if vy == 1:
                t = jnp.where(rows == 0, ylo[base + (cx + 1) * 3 + cz + 1, pl.ds(i, 1), :], pltpu.roll(t, 1, 0))
            elif vy == -1:
                t = jnp.where(rows == sy - 1, yhi[base + (cx + 1) * 3 + cz + 1, pl.ds(i, 1), :], pltpu.roll(t, sy - 1, 0))
            if vz == 1:
                t = jnp.where(lanes == 0, zcol[:, i : i + 1], pltpu.roll(t, 1, 1))
            elif vz == -1:
                t = jnp.where(lanes == sz - 1, zcol[:, i : i + 1], pltpu.roll(t, sz - 1, 1))
            dst[q, i] = t


def adjoint_rows(F, A, om, ga):
    rho = sum(F)
    mom = []
    for axis in range(3):
        pos = [F[q] for q in range(27) if STEPS[q, axis] == 1]
        neg = [F[q] for q in range(27) if STEPS[q, axis] == -1]
        mom.append(sum(pos) - sum(neg))
    vel = (mom[0] / rho, mom[1] / rho, mom[2] / rho)
    uu = vel[0] * vel[0] + vel[1] * vel[1] + vel[2] * vel[2]
    sens = 0.0
    e_rho = 0.0
    s0 = 0.0
    sm = [0.0, 0.0, 0.0]
    for q in range(27):
        c = STEPS[q]
        w = float(WEIGHTS[q])
        cu = None
        for axis in range(3):
            if c[axis] == 1:
                cu = vel[axis] if cu is None else cu + vel[axis]
            elif c[axis] == -1:
                cu = -vel[axis] if cu is None else cu - vel[axis]
        if cu is None:
            eq = w * rho * (1.0 - 1.5 * uu)
        else:
            eq = w * rho * (1.0 + 3.0 * cu + 4.5 * cu * cu - 1.5 * uu)
        bgk = F[q] - om * (F[q] - eq)
        sens = sens + A[q] * (F[26 - q] - bgk)
        aw = A[q] * w
        s0 = s0 + aw
        if cu is None:
            e_rho = e_rho + aw * (1.0 + 1.5 * uu)
        else:
            e_rho = e_rho + aw * (1.0 - 4.5 * cu * cu + 1.5 * uu)
            t = aw * (1.0 + 3.0 * cu)
            for axis in range(3):
                if c[axis] == 1:
                    sm[axis] = sm[axis] + t
                elif c[axis] == -1:
                    sm[axis] = sm[axis] - t
    em = [3.0 * sm[axis] - 3.0 * vel[axis] * s0 for axis in range(3)]
    keep = 1.0 - ga
    out = []
    for p in range(27):
        c = STEPS[p]
        g = e_rho
        for axis in range(3):
            if c[axis] == 1:
                g = g + em[axis]
            elif c[axis] == -1:
                g = g - em[axis]
        out.append(keep * ((1.0 - om) * A[p] + om * g) + ga * A[26 - p])
    return out, sens


def chunked_adjoint(f_ref, a_ref, rate_ref, gamma_ref, out_ref, sens_ref):
    _, sx, sy, sz = out_ref.shape
    halves = sy // 8

    def body(step, carry):
        i = step // halves
        h = pl.multiple_of((step % halves) * 8, 8)
        F = [f_ref[q, i, pl.ds(h, 8), :] for q in range(27)]
        A = [a_ref[q, i, pl.ds(h, 8), :] for q in range(27)]
        om = rate_ref[i, pl.ds(h, 8), :]
        ga = gamma_ref[i, pl.ds(h, 8), :]
        adj, sens = adjoint_rows(F, A, om, ga)
        for q in range(27):
            out_ref[q, i, pl.ds(h, 8), :] = adj[q]
        sens_ref[i, pl.ds(h, 8), :] = sens
        return carry

    lax.fori_loop(0, sx * halves, body, 0)


def next_kernel(cf_ref, ae_ref, *refs):
    hal = refs[0:6]
    rate_ref, gamma_ref, out_ref, sens_ref, fs, as_ = refs[6:]
    move_into(fs, cf_ref, hal, 1, 0)
    move_into(as_, ae_ref, hal, -1, 9)
    chunked_adjoint(fs, as_, rate_ref, gamma_ref, out_ref, sens_ref)


def now_kernel(an_ref, f_ref, *refs):
    hal = refs[0:6]
    rate_ref, gamma_ref, moved_ref, sens_ref = refs[6:]
    move_into(moved_ref, an_ref, hal, -1, 0)
    _, sx, sy, sz = f_ref.shape
    halves = sy // 8

    def body(step, carry):
        i = step // halves
        h = pl.multiple_of((step % halves) * 8, 8)
        F = [f_ref[q, i, pl.ds(h, 8), :] for q in range(27)]
        A = [moved_ref[q, i, pl.ds(h, 8), :] for q in range(27)]
        _, sens = adjoint_rows(F, A, rate_ref[i, pl.ds(h, 8), :], gamma_ref[i, pl.ds(h, 8), :])
        sens_ref[i, pl.ds(h, 8), :] = sens
        return carry

    lax.fori_loop(0, sx * halves, body, 0)


def start_kernel(f_ref, moved_ref, rate_ref, gamma_ref, out_ref, sens_ref):
    chunked_adjoint(f_ref, moved_ref, rate_ref, gamma_ref, out_ref, sens_ref)


def run_stage(kernel, args, shape, scratch):
    _, sx, sy, sz = shape
    return pl.pallas_call(
        kernel,
        out_shape=(
            jax.ShapeDtypeStruct(shape, jnp.float32),
            jax.ShapeDtypeStruct((sx, sy, sz), jnp.float32),
        ),
        scratch_shapes=[pltpu.VMEM(shape, jnp.float32) for _ in range(scratch)],
    )(*args)


def shards(check_pops, adjoint_end, relax_rate, wall_flag, patch_of_cell, porosity, patch_slot):
    sx, sy, sz = relax_rate.shape
    ids = patch_of_cell[:, :: sy // 2, :: sz // 2]
    table = jnp.stack([porosity, patch_slot.astype(jnp.float32)], axis=1)
    looked = table[ids]
    solid = jnp.broadcast_to(looked[:, :, None, :, None, 0], (sx, 2, sy // 2, 2, sz // 2)).reshape(sx, sy, sz)
    walls = wall_flag.astype(jnp.float32)
    gamma = walls * solid
    post_now, _ = collide(check_pops, relax_rate, gamma)
    hal = halos([post_now, adjoint_end], [1, -1])
    shape = check_pops.shape
    adj_next, sens_next = run_stage(
        next_kernel, (post_now, adjoint_end) + hal + (relax_rate, gamma), shape, 2
    )
    hal_n = halos([adj_next], [-1])
    post_adj, sens_now = run_stage(now_kernel, (adj_next, check_pops) + hal_n + (relax_rate, gamma), shape, 0)
    adjoint_start, _ = run_stage(start_kernel, (check_pops, post_adj, relax_rate, gamma), shape, 0)
    density = walls * (sens_next + sens_now)
    boxes = density.reshape(sx, 2, sy // 2, 2, sz // 2).sum(axis=(2, 4))
    parts = jnp.stack([boxes[0], boxes[1 : sx - 1].sum(axis=0), boxes[sx - 1]])
    count = porosity.shape[0]
    devices = lax.axis_size(("gx", "gy", "gz"))
    slots = jnp.stack([looked[0, :, :, 1], looked[1, :, :, 1], looked[sx - 1, :, :, 1]]).reshape(-1)
    hits = (slots[:, None] == jnp.arange(count, dtype=jnp.float32)[None, :]).astype(jnp.float32)
    placed = jnp.sum(parts.reshape(-1)[:, None] * hits, axis=0)
    got = lax.all_to_all(placed.reshape(devices, count // devices), ("gx", "gy", "gz"), 0, 0, tiled=True)
    patch_sens = jnp.sum(got, axis=0)
    return (adjoint_start, patch_sens)


def solution(mesh):
    in_specs = (
        P(None, "gx", "gy", "gz"),
        P(None, "gx", "gy", "gz"),
        P("gx", "gy", "gz"),
        P("gx", "gy", "gz"),
        P("gx", "gy", "gz"),
        P(),
        P(),
    )
    out_specs = (P(None, "gx", "gy", "gz"), P(("gx", "gy", "gz")))
    return jax.shard_map(shards, mesh=mesh, in_specs=in_specs, out_specs=out_specs, check_vma=False)
```

```python
import jax
import jax.numpy as jnp
import numpy as np
from jax import lax
from jax.experimental import pallas as pl
from jax.experimental.pallas import tpu as pltpu
from jax.sharding import PartitionSpec as P


def lattice_table():
    steps = np.array(
        [
            [first, second, third]
            for first in (-1, 0, 1)
            for second in (-1, 0, 1)
            for third in (-1, 0, 1)
        ],
        dtype=np.int64,
    )
    moved = np.abs(steps).sum(axis=1)
    weights = np.array([8.0 / 27.0, 2.0 / 27.0, 1.0 / 54.0, 1.0 / 216.0])[moved]
    return (steps, weights)


STEPS, WEIGHTS = lattice_table()


def collide(pops, rate, gamma):
    steps, weights = lattice_table()
    cube = pops.reshape((3, 3, 3) + pops.shape[1:])
    density = jnp.sum(pops, axis=0)
    mom_x = jnp.sum(cube[2], axis=(0, 1)) - jnp.sum(cube[0], axis=(0, 1))
    mom_y = jnp.sum(cube[:, 2], axis=(0, 1)) - jnp.sum(cube[:, 0], axis=(0, 1))
    mom_z = jnp.sum(cube[:, :, 2], axis=(0, 1)) - jnp.sum(cube[:, :, 0], axis=(0, 1))
    vel_x = mom_x / density
    vel_y = mom_y / density
    vel_z = mom_z / density
    cx = jnp.asarray(steps[:, 0], jnp.float32)[:, None, None, None]
    cy = jnp.asarray(steps[:, 1], jnp.float32)[:, None, None, None]
    cz = jnp.asarray(steps[:, 2], jnp.float32)[:, None, None, None]
    wts = jnp.asarray(weights, jnp.float32)[:, None, None, None]
    along = cx * vel_x + cy * vel_y + cz * vel_z
    speed = vel_x * vel_x + vel_y * vel_y + vel_z * vel_z
    equil = wts * density * (1.0 + 3.0 * along + 4.5 * along * along - 1.5 * speed)
    relaxed = pops - rate * (pops - equil)
    flipped = pops[::-1]
    return ((1.0 - gamma) * relaxed + gamma * flipped, flipped - relaxed)


def halo_exchange(up, down, axis):
    size = lax.axis_size(axis)
    if size == 1:
        return up, down
    if size == 2:
        both = lax.ppermute(jnp.stack([up, down]), axis, [(0, 1), (1, 0)])
        return both[0], both[1]
    lo = lax.ppermute(up, axis, [(i, (i + 1) % size) for i in range(size)])
    hi = lax.ppermute(down, axis, [(i, (i - 1) % size) for i in range(size)])
    return lo, hi


def shifted(cube, lo, hi, d, sign):
    n = cube.shape[3 + d]
    plus = lax.index_in_dim(cube, 1 + sign, axis=d, keepdims=False)
    minus = lax.index_in_dim(cube, 1 - sign, axis=d, keepdims=False)
    still = lax.index_in_dim(cube, 1, axis=d, keepdims=False)
    plus = jnp.concatenate([lo, lax.slice_in_dim(plus, 0, n - 1, axis=2 + d)], axis=2 + d)
    minus = jnp.concatenate([lax.slice_in_dim(minus, 1, n, axis=2 + d), hi], axis=2 + d)
    groups = [None, still, None]
    groups[1 + sign] = plus
    groups[1 - sign] = minus
    return jnp.stack(groups, axis=d)


def faces(cube, sign, d):
    n = cube.shape[3 + d]
    plus = lax.index_in_dim(cube, 1 + sign, axis=d, keepdims=False)
    minus = lax.index_in_dim(cube, 1 - sign, axis=d, keepdims=False)
    return lax.slice_in_dim(plus, n - 1, n, axis=2 + d), lax.slice_in_dim(minus, 0, 1, axis=2 + d)


def halos(fields, signs):
    cubes = [f.reshape((3, 3, 3) + f.shape[1:]) for f in fields]
    sx, sy, sz = cubes[0].shape[3:]
    x_up, x_dn = zip(*[faces(c, s, 0) for c, s in zip(cubes, signs)])
    xlo, xhi = halo_exchange(jnp.stack(x_up), jnp.stack(x_dn), "gx")
    both = jnp.stack(cubes)
    rows = jnp.concatenate([both[..., sy - 1 : sy, :], both[..., 0:1, :]], axis=5)
    pick = (jnp.arange(sz)[:, None] == jnp.array([sz - 1, 0])[None, :]).astype(jnp.float32)
    cols = jnp.einsum("nabcxyz,zk->knabcxy", both, pick, precision=lax.Precision.HIGHEST)
    y_up, y_dn = [], []
    for k, s in enumerate(signs):
        top = shifted(rows[k][..., 0:1, :], xlo[k][:, :, :, sy - 1 : sy], xhi[k][:, :, :, sy - 1 : sy], 0, s)
        bot = shifted(rows[k][..., 1:2, :], xlo[k][:, :, :, 0:1], xhi[k][:, :, :, 0:1], 0, s)
        y_up.append(lax.index_in_dim(top, 1 + s, axis=1, keepdims=False))
        y_dn.append(lax.index_in_dim(bot, 1 - s, axis=1, keepdims=False))
    ylo, yhi = halo_exchange(jnp.stack(y_up), jnp.stack(y_dn), "gy")
    z_up, z_dn = [], []
    for k, s in enumerate(signs):
        picked = []
        for at, z0 in ((0, sz - 1), (1, 0)):
            col = shifted(cols[at, k], xlo[k][..., z0], xhi[k][..., z0], 0, s)
            col = shifted(col, ylo[k][..., z0], yhi[k][..., z0], 1, s)
            picked.append(col)
        z_up.append(jnp.swapaxes(lax.index_in_dim(picked[0], 1 + s, axis=2, keepdims=False), -1, -2))
        z_dn.append(jnp.swapaxes(lax.index_in_dim(picked[1], 1 - s, axis=2, keepdims=False), -1, -2))
    zlo, zhi = halo_exchange(jnp.stack(z_up), jnp.stack(z_dn), "gz")
    nf = len(cubes)
    return (
        xlo.reshape(nf * 9, sy, sz),
        xhi.reshape(nf * 9, sy, sz),
        ylo.reshape(nf * 9, sx, sz),
        yhi.reshape(nf * 9, sx, sz),
        zlo.reshape(nf * 9, sy, sx),
        zhi.reshape(nf * 9, sy, sx),
    )


def move_into(dst, src, hal, sign, base):
    xlo, xhi, ylo, yhi, zlo, zhi = hal
    _, sx, sy, sz = src.shape
    rows = lax.broadcasted_iota(jnp.int32, (sy, sz), 0)
    lanes = lax.broadcasted_iota(jnp.int32, (sy, sz), 1)
    for q in range(27):
        cx, cy, cz = (int(v) for v in STEPS[q])
        vx, vy, vz = sign * cx, sign * cy, sign * cz
        if vz == 1:
            zcol = zlo[base + (cx + 1) * 3 + cy + 1]
        elif vz == -1:
            zcol = zhi[base + (cx + 1) * 3 + cy + 1]
        for i in range(sx):
            j = i - vx
            if j < 0:
                t = xlo[base + (cy + 1) * 3 + cz + 1]
            elif j >= sx:
                t = xhi[base + (cy + 1) * 3 + cz + 1]
            else:
                t = src[q, j]
            if vy == 1:
                t = jnp.where(rows == 0, ylo[base + (cx + 1) * 3 + cz + 1, pl.ds(i, 1), :], pltpu.roll(t, 1, 0))
            elif vy == -1:
                t = jnp.where(rows == sy - 1, yhi[base + (cx + 1) * 3 + cz + 1, pl.ds(i, 1), :], pltpu.roll(t, sy - 1, 0))
            if vz == 1:
                t = jnp.where(lanes == 0, zcol[:, i : i + 1], pltpu.roll(t, 1, 1))
            elif vz == -1:
                t = jnp.where(lanes == sz - 1, zcol[:, i : i + 1], pltpu.roll(t, sz - 1, 1))
            dst[q, i] = t


def adjoint_rows(F, A, om, ga):
    rho = sum(F)
    mom = []
    for axis in range(3):
        pos = [F[q] for q in range(27) if STEPS[q, axis] == 1]
        neg = [F[q] for q in range(27) if STEPS[q, axis] == -1]
        mom.append(sum(pos) - sum(neg))
    vel = (mom[0] / rho, mom[1] / rho, mom[2] / rho)
    uu = vel[0] * vel[0] + vel[1] * vel[1] + vel[2] * vel[2]
    sens = 0.0
    e_rho = 0.0
    s0 = 0.0
    sm = [0.0, 0.0, 0.0]
    for q in range(27):
        c = STEPS[q]
        w = float(WEIGHTS[q])
        cu = None
        for axis in range(3):
            if c[axis] == 1:
                cu = vel[axis] if cu is None else cu + vel[axis]
            elif c[axis] == -1:
                cu = -vel[axis] if cu is None else cu - vel[axis]
        if cu is None:
            eq = w * rho * (1.0 - 1.5 * uu)
        else:
            eq = w * rho * (1.0 + 3.0 * cu + 4.5 * cu * cu - 1.5 * uu)
        bgk = F[q] - om * (F[q] - eq)
        sens = sens + A[q] * (F[26 - q] - bgk)
        aw = A[q] * w
        s0 = s0 + aw
        if cu is None:
            e_rho = e_rho + aw * (1.0 + 1.5 * uu)
        else:
            e_rho = e_rho + aw * (1.0 - 4.5 * cu * cu + 1.5 * uu)
            t = aw * (1.0 + 3.0 * cu)
            for axis in range(3):
                if c[axis] == 1:
                    sm[axis] = sm[axis] + t
                elif c[axis] == -1:
                    sm[axis] = sm[axis] - t
    em = [3.0 * sm[axis] - 3.0 * vel[axis] * s0 for axis in range(3)]
    keep = 1.0 - ga
    out = []
    for p in range(27):
        c = STEPS[p]
        g = e_rho
        for axis in range(3):
            if c[axis] == 1:
                g = g + em[axis]
            elif c[axis] == -1:
                g = g - em[axis]
        out.append(keep * ((1.0 - om) * A[p] + om * g) + ga * A[26 - p])
    return out, sens


def chunked_adjoint(f_ref, a_ref, rate_ref, gamma_ref, out_ref, sens_ref):
    _, sx, sy, sz = out_ref.shape
    halves = sy // 8

    def body(step, carry):
        i = step // halves
        h = pl.multiple_of((step % halves) * 8, 8)
        F = [f_ref[q, i, pl.ds(h, 8), :] for q in range(27)]
        A = [a_ref[q, i, pl.ds(h, 8), :] for q in range(27)]
        om = rate_ref[i, pl.ds(h, 8), :]
        ga = gamma_ref[i, pl.ds(h, 8), :]
        adj, sens = adjoint_rows(F, A, om, ga)
        for q in range(27):
            out_ref[q, i, pl.ds(h, 8), :] = adj[q]
        sens_ref[i, pl.ds(h, 8), :] = sens
        return carry

    lax.fori_loop(0, sx * halves, body, 0)


def next_kernel(cf_ref, ae_ref, *refs):
    hal = refs[0:6]
    rate_ref, gamma_ref, out_ref, sens_ref, fs, as_ = refs[6:]
    move_into(fs, cf_ref, hal, 1, 0)
    move_into(as_, ae_ref, hal, -1, 9)
    chunked_adjoint(fs, as_, rate_ref, gamma_ref, out_ref, sens_ref)


def now_kernel(an_ref, f_ref, *refs):
    hal = refs[0:6]
    rate_ref, gamma_ref, out_ref, sens_ref, as_ = refs[6:]
    move_into(as_, an_ref, hal, -1, 0)
    chunked_adjoint(f_ref, as_, rate_ref, gamma_ref, out_ref, sens_ref)


def run_stage(kernel, args, shape, scratch):
    _, sx, sy, sz = shape
    return pl.pallas_call(
        kernel,
        out_shape=(
            jax.ShapeDtypeStruct(shape, jnp.float32),
            jax.ShapeDtypeStruct((sx, sy, sz), jnp.float32),
        ),
        scratch_shapes=[pltpu.VMEM(shape, jnp.float32) for _ in range(scratch)],
    )(*args)


def shards(check_pops, adjoint_end, relax_rate, wall_flag, patch_of_cell, porosity, patch_slot):
    sx, sy, sz = relax_rate.shape
    ids = patch_of_cell[:, :: sy // 2, :: sz // 2]
    table = jnp.stack([porosity, patch_slot.astype(jnp.float32)], axis=1)
    looked = table[ids]
    solid = jnp.broadcast_to(looked[:, :, None, :, None, 0], (sx, 2, sy // 2, 2, sz // 2)).reshape(sx, sy, sz)
    walls = wall_flag.astype(jnp.float32)
    gamma = walls * solid
    post_now, _ = collide(check_pops, relax_rate, gamma)
    hal = halos([post_now, adjoint_end], [1, -1])
    shape = check_pops.shape
    adj_next, sens_next = run_stage(
        next_kernel, (post_now, adjoint_end) + hal + (relax_rate, gamma), shape, 2
    )
    hal_n = halos([adj_next], [-1])
    adjoint_start, sens_now = run_stage(now_kernel, (adj_next, check_pops) + hal_n + (relax_rate, gamma), shape, 1)
    density = walls * (sens_next + sens_now)
    boxes = density.reshape(sx, 2, sy // 2, 2, sz // 2).sum(axis=(2, 4))
    parts = jnp.stack([boxes[0], boxes[1 : sx - 1].sum(axis=0), boxes[sx - 1]])
    count = porosity.shape[0]
    devices = lax.axis_size(("gx", "gy", "gz"))
    slots = jnp.stack([looked[0, :, :, 1], looked[1, :, :, 1], looked[sx - 1, :, :, 1]]).reshape(-1)
    hits = (slots[:, None] == jnp.arange(count, dtype=jnp.float32)[None, :]).astype(jnp.float32)
    placed = jnp.sum(parts.reshape(-1)[:, None] * hits, axis=0)
    got = lax.all_to_all(placed.reshape(devices, count // devices), ("gx", "gy", "gz"), 0, 0, tiled=True)
    patch_sens = jnp.sum(got, axis=0)
    return (adjoint_start, patch_sens)


def solution(mesh):
    in_specs = (
        P(None, "gx", "gy", "gz"),
        P(None, "gx", "gy", "gz"),
        P("gx", "gy", "gz"),
        P("gx", "gy", "gz"),
        P("gx", "gy", "gz"),
        P(),
        P(),
    )
    out_specs = (P(None, "gx", "gy", "gz"), P(("gx", "gy", "gz")))
    return jax.shard_map(shards, mesh=mesh, in_specs=in_specs, out_specs=out_specs, check_vma=False)
```

```python
import jax
import jax.numpy as jnp
import numpy as np
from jax import lax
from jax.experimental import pallas as pl
from jax.experimental.pallas import tpu as pltpu
from jax.sharding import PartitionSpec as P


def lattice_table():
    steps = np.array(
        [
            [first, second, third]
            for first in (-1, 0, 1)
            for second in (-1, 0, 1)
            for third in (-1, 0, 1)
        ],
        dtype=np.int64,
    )
    moved = np.abs(steps).sum(axis=1)
    weights = np.array([8.0 / 27.0, 2.0 / 27.0, 1.0 / 54.0, 1.0 / 216.0])[moved]
    return (steps, weights)


STEPS, WEIGHTS = lattice_table()


def collide(pops, rate, gamma):
    steps, weights = lattice_table()
    cube = pops.reshape((3, 3, 3) + pops.shape[1:])
    density = jnp.sum(pops, axis=0)
    mom_x = jnp.sum(cube[2], axis=(0, 1)) - jnp.sum(cube[0], axis=(0, 1))
    mom_y = jnp.sum(cube[:, 2], axis=(0, 1)) - jnp.sum(cube[:, 0], axis=(0, 1))
    mom_z = jnp.sum(cube[:, :, 2], axis=(0, 1)) - jnp.sum(cube[:, :, 0], axis=(0, 1))
    vel_x = mom_x / density
    vel_y = mom_y / density
    vel_z = mom_z / density
    cx = jnp.asarray(steps[:, 0], jnp.float32)[:, None, None, None]
    cy = jnp.asarray(steps[:, 1], jnp.float32)[:, None, None, None]
    cz = jnp.asarray(steps[:, 2], jnp.float32)[:, None, None, None]
    wts = jnp.asarray(weights, jnp.float32)[:, None, None, None]
    along = cx * vel_x + cy * vel_y + cz * vel_z
    speed = vel_x * vel_x + vel_y * vel_y + vel_z * vel_z
    equil = wts * density * (1.0 + 3.0 * along + 4.5 * along * along - 1.5 * speed)
    relaxed = pops - rate * (pops - equil)
    flipped = pops[::-1]
    return ((1.0 - gamma) * relaxed + gamma * flipped, flipped - relaxed)


def halo_exchange(up, down, axis):
    size = lax.axis_size(axis)
    if size == 1:
        return up, down
    if size == 2:
        both = lax.ppermute(jnp.stack([up, down]), axis, [(0, 1), (1, 0)])
        return both[0], both[1]
    lo = lax.ppermute(up, axis, [(i, (i + 1) % size) for i in range(size)])
    hi = lax.ppermute(down, axis, [(i, (i - 1) % size) for i in range(size)])
    return lo, hi


def shifted(cube, lo, hi, d, sign):
    n = cube.shape[3 + d]
    plus = lax.index_in_dim(cube, 1 + sign, axis=d, keepdims=False)
    minus = lax.index_in_dim(cube, 1 - sign, axis=d, keepdims=False)
    still = lax.index_in_dim(cube, 1, axis=d, keepdims=False)
    plus = jnp.concatenate([lo, lax.slice_in_dim(plus, 0, n - 1, axis=2 + d)], axis=2 + d)
    minus = jnp.concatenate([lax.slice_in_dim(minus, 1, n, axis=2 + d), hi], axis=2 + d)
    groups = [None, still, None]
    groups[1 + sign] = plus
    groups[1 - sign] = minus
    return jnp.stack(groups, axis=d)


def faces(cube, sign, d):
    n = cube.shape[3 + d]
    plus = lax.index_in_dim(cube, 1 + sign, axis=d, keepdims=False)
    minus = lax.index_in_dim(cube, 1 - sign, axis=d, keepdims=False)
    return lax.slice_in_dim(plus, n - 1, n, axis=2 + d), lax.slice_in_dim(minus, 0, 1, axis=2 + d)


def halos(fields, signs, given=None):
    cubes = [f.reshape((3, 3, 3) + f.shape[1:]) for f in fields]
    sx, sy, sz = cubes[0].shape[3:]
    if given is None:
        x_up, x_dn = zip(*[faces(c, s, 0) for c, s in zip(cubes, signs)])
        given = (jnp.stack(x_up), jnp.stack(x_dn))
    xlo, xhi = halo_exchange(given[0], given[1], "gx")
    both = jnp.stack(cubes)
    rows = jnp.concatenate([both[..., sy - 1 : sy, :], both[..., 0:1, :]], axis=5)
    cols = jnp.concatenate([both[..., sz - 1 : sz], both[..., 0:1]], axis=6)
    y_up, y_dn = [], []
    for k, s in enumerate(signs):
        top = shifted(rows[k][..., 0:1, :], xlo[k][:, :, :, sy - 1 : sy], xhi[k][:, :, :, sy - 1 : sy], 0, s)
        bot = shifted(rows[k][..., 1:2, :], xlo[k][:, :, :, 0:1], xhi[k][:, :, :, 0:1], 0, s)
        y_up.append(lax.index_in_dim(top, 1 + s, axis=1, keepdims=False))
        y_dn.append(lax.index_in_dim(bot, 1 - s, axis=1, keepdims=False))
    ylo, yhi = halo_exchange(jnp.stack(y_up), jnp.stack(y_dn), "gy")
    z_up, z_dn = [], []
    for k, s in enumerate(signs):
        picked = []
        for at, z0 in ((0, sz - 1), (1, 0)):
            col = cols[k][..., at : at + 1]
            col = shifted(col, xlo[k][..., z0 : z0 + 1], xhi[k][..., z0 : z0 + 1], 0, s)
            col = shifted(col, ylo[k][..., z0 : z0 + 1], yhi[k][..., z0 : z0 + 1], 1, s)
            picked.append(col)
        z_up.append(jnp.swapaxes(lax.index_in_dim(picked[0], 1 + s, axis=2, keepdims=False)[..., 0], -1, -2))
        z_dn.append(jnp.swapaxes(lax.index_in_dim(picked[1], 1 - s, axis=2, keepdims=False)[..., 0], -1, -2))
    zlo, zhi = halo_exchange(jnp.stack(z_up), jnp.stack(z_dn), "gz")
    nf = len(cubes)
    return (
        xlo.reshape(nf * 9, sy, sz),
        xhi.reshape(nf * 9, sy, sz),
        ylo.reshape(nf * 9, sx, sz),
        yhi.reshape(nf * 9, sx, sz),
        zlo.reshape(nf * 9, sy, sx),
        zhi.reshape(nf * 9, sy, sx),
    )


def move_into(dst, src, hal, sign, base):
    xlo, xhi, ylo, yhi, zlo, zhi = hal
    _, sx, sy, sz = src.shape
    rows = lax.broadcasted_iota(jnp.int32, (sy, sz), 0)
    lanes = lax.broadcasted_iota(jnp.int32, (sy, sz), 1)
    for q in range(27):
        cx, cy, cz = (int(v) for v in STEPS[q])
        vx, vy, vz = sign * cx, sign * cy, sign * cz
        if vz == 1:
            zcol = zlo[base + (cx + 1) * 3 + cy + 1]
        elif vz == -1:
            zcol = zhi[base + (cx + 1) * 3 + cy + 1]
        for i in range(sx):
            j = i - vx
            if j < 0:
                t = xlo[base + (cy + 1) * 3 + cz + 1]
            elif j >= sx:
                t = xhi[base + (cy + 1) * 3 + cz + 1]
            else:
                t = src[q, j]
            if vy == 1:
                t = jnp.where(rows == 0, ylo[base + (cx + 1) * 3 + cz + 1, pl.ds(i, 1), :], pltpu.roll(t, 1, 0))
            elif vy == -1:
                t = jnp.where(rows == sy - 1, yhi[base + (cx + 1) * 3 + cz + 1, pl.ds(i, 1), :], pltpu.roll(t, sy - 1, 0))
            if vz == 1:
                t = jnp.where(lanes == 0, zcol[:, i : i + 1], pltpu.roll(t, 1, 1))
            elif vz == -1:
                t = jnp.where(lanes == sz - 1, zcol[:, i : i + 1], pltpu.roll(t, sz - 1, 1))
            dst[q, i] = t


def adjoint_rows(F, A, om, ga):
    rho = sum(F)
    mom = []
    for axis in range(3):
        pos = [F[q] for q in range(27) if STEPS[q, axis] == 1]
        neg = [F[q] for q in range(27) if STEPS[q, axis] == -1]
        mom.append(sum(pos) - sum(neg))
    vel = (mom[0] / rho, mom[1] / rho, mom[2] / rho)
    uu = vel[0] * vel[0] + vel[1] * vel[1] + vel[2] * vel[2]
    sens = 0.0
    e_rho = 0.0
    s0 = 0.0
    sm = [0.0, 0.0, 0.0]
    for q in range(27):
        c = STEPS[q]
        w = float(WEIGHTS[q])
        cu = None
        for axis in range(3):
            if c[axis] == 1:
                cu = vel[axis] if cu is None else cu + vel[axis]
            elif c[axis] == -1:
                cu = -vel[axis] if cu is None else cu - vel[axis]
        if cu is None:
            eq = w * rho * (1.0 - 1.5 * uu)
        else:
            eq = w * rho * (1.0 + 3.0 * cu + 4.5 * cu * cu - 1.5 * uu)
        bgk = F[q] - om * (F[q] - eq)
        sens = sens + A[q] * (F[26 - q] - bgk)
        aw = A[q] * w
        s0 = s0 + aw
        if cu is None:
            e_rho = e_rho + aw * (1.0 + 1.5 * uu)
        else:
            e_rho = e_rho + aw * (1.0 - 4.5 * cu * cu + 1.5 * uu)
            t = aw * (1.0 + 3.0 * cu)
            for axis in range(3):
                if c[axis] == 1:
                    sm[axis] = sm[axis] + t
                elif c[axis] == -1:
                    sm[axis] = sm[axis] - t
    em = [3.0 * sm[axis] - 3.0 * vel[axis] * s0 for axis in range(3)]
    keep = 1.0 - ga
    out = []
    for p in range(27):
        c = STEPS[p]
        g = e_rho
        for axis in range(3):
            if c[axis] == 1:
                g = g + em[axis]
            elif c[axis] == -1:
                g = g - em[axis]
        out.append(keep * ((1.0 - om) * A[p] + om * g) + ga * A[26 - p])
    return out, sens


def chunked_adjoint(f_ref, a_ref, rate_ref, gamma_ref, out_ref, sens_ref):
    _, sx, sy, sz = out_ref.shape
    halves = sy // 8

    def body(step, carry):
        i = step // halves
        h = pl.multiple_of((step % halves) * 8, 8)
        F = [f_ref[q, i, pl.ds(h, 8), :] for q in range(27)]
        A = [a_ref[q, i, pl.ds(h, 8), :] for q in range(27)]
        om = rate_ref[i, pl.ds(h, 8), :]
        ga = gamma_ref[i, pl.ds(h, 8), :]
        adj, sens = adjoint_rows(F, A, om, ga)
        for q in range(27):
            out_ref[q, i, pl.ds(h, 8), :] = adj[q]
        sens_ref[i, pl.ds(h, 8), :] = sens
        return carry

    lax.fori_loop(0, sx * halves, body, 0)


def next_kernel(cf_ref, ae_ref, *refs):
    hal = refs[0:6]
    rate_ref, gamma_ref, out_ref, sens_ref, up_ref, down_ref, fs, as_ = refs[6:]
    move_into(fs, cf_ref, hal, 1, 0)
    move_into(as_, ae_ref, hal, -1, 9)
    chunked_adjoint(fs, as_, rate_ref, gamma_ref, out_ref, sens_ref)
    sx = out_ref.shape[1]
    for q in range(9):
        up_ref[q] = out_ref[q, sx - 1]
        down_ref[q] = out_ref[18 + q, 0]


def now_kernel(an_ref, f_ref, *refs):
    hal = refs[0:6]
    rate_ref, gamma_ref, out_ref, sens_ref, as_ = refs[6:]
    move_into(as_, an_ref, hal, -1, 0)
    chunked_adjoint(f_ref, as_, rate_ref, gamma_ref, out_ref, sens_ref)


def run_stage(kernel, args, shape, scratch):
    _, sx, sy, sz = shape
    return pl.pallas_call(
        kernel,
        out_shape=(
            jax.ShapeDtypeStruct(shape, jnp.float32),
            jax.ShapeDtypeStruct((sx, sy, sz), jnp.float32),
        ),
        scratch_shapes=[pltpu.VMEM(shape, jnp.float32) for _ in range(scratch)],
    )(*args)


def shards(check_pops, adjoint_end, relax_rate, wall_flag, patch_of_cell, porosity, patch_slot):
    sx, sy, sz = relax_rate.shape
    ids = patch_of_cell[:, :: sy // 2, :: sz // 2]
    table = jnp.stack([porosity, patch_slot.astype(jnp.float32)], axis=1)
    looked = table[ids]
    solid = jnp.broadcast_to(looked[:, :, None, :, None, 0], (sx, 2, sy // 2, 2, sz // 2)).reshape(sx, sy, sz)
    walls = wall_flag.astype(jnp.float32)
    gamma = walls * solid
    post_now, _ = collide(check_pops, relax_rate, gamma)
    hal = halos([post_now, adjoint_end], [1, -1])
    shape = check_pops.shape
    _, sx, sy, sz = shape
    adj_next, sens_next, x_up, x_dn = pl.pallas_call(
        next_kernel,
        out_shape=(
            jax.ShapeDtypeStruct(shape, jnp.float32),
            jax.ShapeDtypeStruct((sx, sy, sz), jnp.float32),
            jax.ShapeDtypeStruct((9, sy, sz), jnp.float32),
            jax.ShapeDtypeStruct((9, sy, sz), jnp.float32),
        ),
        scratch_shapes=[pltpu.VMEM(shape, jnp.float32) for _ in range(2)],
    )(post_now, adjoint_end, *hal, relax_rate, gamma)
    hal_n = halos([adj_next], [-1], (x_up.reshape(1, 3, 3, 1, sy, sz), x_dn.reshape(1, 3, 3, 1, sy, sz)))
    adjoint_start, sens_now = run_stage(now_kernel, (adj_next, check_pops) + hal_n + (relax_rate, gamma), shape, 1)
    density = walls * (sens_next + sens_now)
    boxes = density.reshape(sx, 2, sy // 2, 2, sz // 2).sum(axis=(2, 4))
    parts = jnp.stack([boxes[0], boxes[1 : sx - 1].sum(axis=0), boxes[sx - 1]])
    count = porosity.shape[0]
    devices = lax.axis_size(("gx", "gy", "gz"))
    slots = jnp.stack([looked[0, :, :, 1], looked[1, :, :, 1], looked[sx - 1, :, :, 1]]).reshape(-1)
    hits = (slots[:, None] == jnp.arange(count, dtype=jnp.float32)[None, :]).astype(jnp.float32)
    placed = jnp.sum(parts.reshape(-1)[:, None] * hits, axis=0)
    got = lax.all_to_all(placed.reshape(devices, count // devices), ("gx", "gy", "gz"), 0, 0, tiled=True)
    patch_sens = jnp.sum(got, axis=0)
    return (adjoint_start, patch_sens)


def solution(mesh):
    in_specs = (
        P(None, "gx", "gy", "gz"),
        P(None, "gx", "gy", "gz"),
        P("gx", "gy", "gz"),
        P("gx", "gy", "gz"),
        P("gx", "gy", "gz"),
        P(),
        P(),
    )
    out_specs = (P(None, "gx", "gy", "gz"), P(("gx", "gy", "gz")))
    return jax.shard_map(shards, mesh=mesh, in_specs=in_specs, out_specs=out_specs, check_vma=False)
```

```python
import jax
import jax.numpy as jnp
import numpy as np
from jax import lax
from jax.experimental import pallas as pl
from jax.experimental.pallas import tpu as pltpu
from jax.sharding import PartitionSpec as P


def lattice_table():
    steps = np.array(
        [
            [first, second, third]
            for first in (-1, 0, 1)
            for second in (-1, 0, 1)
            for third in (-1, 0, 1)
        ],
        dtype=np.int64,
    )
    moved = np.abs(steps).sum(axis=1)
    weights = np.array([8.0 / 27.0, 2.0 / 27.0, 1.0 / 54.0, 1.0 / 216.0])[moved]
    return (steps, weights)


STEPS, WEIGHTS = lattice_table()


def collide(pops, rate, gamma):
    steps, weights = lattice_table()
    cube = pops.reshape((3, 3, 3) + pops.shape[1:])
    density = jnp.sum(pops, axis=0)
    mom_x = jnp.sum(cube[2], axis=(0, 1)) - jnp.sum(cube[0], axis=(0, 1))
    mom_y = jnp.sum(cube[:, 2], axis=(0, 1)) - jnp.sum(cube[:, 0], axis=(0, 1))
    mom_z = jnp.sum(cube[:, :, 2], axis=(0, 1)) - jnp.sum(cube[:, :, 0], axis=(0, 1))
    vel_x = mom_x / density
    vel_y = mom_y / density
    vel_z = mom_z / density
    cx = jnp.asarray(steps[:, 0], jnp.float32)[:, None, None, None]
    cy = jnp.asarray(steps[:, 1], jnp.float32)[:, None, None, None]
    cz = jnp.asarray(steps[:, 2], jnp.float32)[:, None, None, None]
    wts = jnp.asarray(weights, jnp.float32)[:, None, None, None]
    along = cx * vel_x + cy * vel_y + cz * vel_z
    speed = vel_x * vel_x + vel_y * vel_y + vel_z * vel_z
    equil = wts * density * (1.0 + 3.0 * along + 4.5 * along * along - 1.5 * speed)
    relaxed = pops - rate * (pops - equil)
    flipped = pops[::-1]
    return ((1.0 - gamma) * relaxed + gamma * flipped, flipped - relaxed)


def halo_exchange(up, down, axis):
    size = lax.axis_size(axis)
    if size == 1:
        return up, down
    if size == 2:
        both = lax.ppermute(jnp.stack([up, down]), axis, [(0, 1), (1, 0)])
        return both[0], both[1]
    lo = lax.ppermute(up, axis, [(i, (i + 1) % size) for i in range(size)])
    hi = lax.ppermute(down, axis, [(i, (i - 1) % size) for i in range(size)])
    return lo, hi


def shifted(cube, lo, hi, d, sign):
    n = cube.shape[3 + d]
    plus = lax.index_in_dim(cube, 1 + sign, axis=d, keepdims=False)
    minus = lax.index_in_dim(cube, 1 - sign, axis=d, keepdims=False)
    still = lax.index_in_dim(cube, 1, axis=d, keepdims=False)
    plus = jnp.concatenate([lo, lax.slice_in_dim(plus, 0, n - 1, axis=2 + d)], axis=2 + d)
    minus = jnp.concatenate([lax.slice_in_dim(minus, 1, n, axis=2 + d), hi], axis=2 + d)
    groups = [None, still, None]
    groups[1 + sign] = plus
    groups[1 - sign] = minus
    return jnp.stack(groups, axis=d)


def faces(cube, sign, d):
    n = cube.shape[3 + d]
    plus = lax.index_in_dim(cube, 1 + sign, axis=d, keepdims=False)
    minus = lax.index_in_dim(cube, 1 - sign, axis=d, keepdims=False)
    return lax.slice_in_dim(plus, n - 1, n, axis=2 + d), lax.slice_in_dim(minus, 0, 1, axis=2 + d)


def columns_kernel(a_ref, b_ref, out_ref):
    _, sx, sy, sz = a_ref.shape
    pairs = [(r, q, i) for r in (a_ref, b_ref) for q in range(27) for i in range(sx)]
    per = 128 // sy
    for g in range(len(pairs) // per):
        block = jnp.concatenate([r[q, i] for r, q, i in pairs[g * per : (g + 1) * per]], axis=0)
        flipped = block.T
        out_ref[0, pl.ds(g, 1), :] = flipped[sz - 1 : sz, :]
        out_ref[1, pl.ds(g, 1), :] = flipped[0:1, :]


def halos(fields, signs):
    cubes = [f.reshape((3, 3, 3) + f.shape[1:]) for f in fields]
    sx, sy, sz = cubes[0].shape[3:]
    x_up, x_dn = zip(*[faces(c, s, 0) for c, s in zip(cubes, signs)])
    xlo, xhi = halo_exchange(jnp.stack(x_up), jnp.stack(x_dn), "gx")
    both = jnp.stack(cubes)
    rows = jnp.concatenate([both[..., sy - 1 : sy, :], both[..., 0:1, :]], axis=5)
    if len(fields) == 2 and sy * 8 == 128 and sz == 128:
        flat = pl.pallas_call(
            columns_kernel, out_shape=jax.ShapeDtypeStruct((2, 2 * 27 * sx * sy // 128, 128), jnp.float32)
        )(fields[0], fields[1])
        cols = flat.reshape((2, 2, 3, 3, 3, sx, sy))
    else:
        cols = None
        edges = jnp.concatenate([both[..., sz - 1 : sz], both[..., 0:1]], axis=6)
    y_up, y_dn = [], []
    for k, s in enumerate(signs):
        top = shifted(rows[k][..., 0:1, :], xlo[k][:, :, :, sy - 1 : sy], xhi[k][:, :, :, sy - 1 : sy], 0, s)
        bot = shifted(rows[k][..., 1:2, :], xlo[k][:, :, :, 0:1], xhi[k][:, :, :, 0:1], 0, s)
        y_up.append(lax.index_in_dim(top, 1 + s, axis=1, keepdims=False))
        y_dn.append(lax.index_in_dim(bot, 1 - s, axis=1, keepdims=False))
    ylo, yhi = halo_exchange(jnp.stack(y_up), jnp.stack(y_dn), "gy")
    z_up, z_dn = [], []
    for k, s in enumerate(signs):
        picked = []
        for at, z0 in ((0, sz - 1), (1, 0)):
            if cols is None:
                col = edges[k][..., at : at + 1]
                col = shifted(col, xlo[k][..., z0 : z0 + 1], xhi[k][..., z0 : z0 + 1], 0, s)
                col = shifted(col, ylo[k][..., z0 : z0 + 1], yhi[k][..., z0 : z0 + 1], 1, s)[..., 0]
            else:
                col = shifted(cols[at, k], xlo[k][..., z0], xhi[k][..., z0], 0, s)
                col = shifted(col, ylo[k][..., z0], yhi[k][..., z0], 1, s)
            picked.append(col)
        z_up.append(jnp.swapaxes(lax.index_in_dim(picked[0], 1 + s, axis=2, keepdims=False), -1, -2))
        z_dn.append(jnp.swapaxes(lax.index_in_dim(picked[1], 1 - s, axis=2, keepdims=False), -1, -2))
    zlo, zhi = halo_exchange(jnp.stack(z_up), jnp.stack(z_dn), "gz")
    nf = len(cubes)
    return (
        xlo.reshape(nf * 9, sy, sz),
        xhi.reshape(nf * 9, sy, sz),
        ylo.reshape(nf * 9, sx, sz),
        yhi.reshape(nf * 9, sx, sz),
        zlo.reshape(nf * 9, sy, sx),
        zhi.reshape(nf * 9, sy, sx),
    )


def move_into(dst, src, hal, sign, base):
    xlo, xhi, ylo, yhi, zlo, zhi = hal
    _, sx, sy, sz = src.shape
    rows = lax.broadcasted_iota(jnp.int32, (sy, sz), 0)
    lanes = lax.broadcasted_iota(jnp.int32, (sy, sz), 1)
    for q in range(27):
        cx, cy, cz = (int(v) for v in STEPS[q])
        vx, vy, vz = sign * cx, sign * cy, sign * cz
        if vz == 1:
            zcol = zlo[base + (cx + 1) * 3 + cy + 1]
        elif vz == -1:
            zcol = zhi[base + (cx + 1) * 3 + cy + 1]
        for i in range(sx):
            j = i - vx
            if j < 0:
                t = xlo[base + (cy + 1) * 3 + cz + 1]
            elif j >= sx:
                t = xhi[base + (cy + 1) * 3 + cz + 1]
            else:
                t = src[q, j]
            if vy == 1:
                t = jnp.where(rows == 0, ylo[base + (cx + 1) * 3 + cz + 1, pl.ds(i, 1), :], pltpu.roll(t, 1, 0))
            elif vy == -1:
                t = jnp.where(rows == sy - 1, yhi[base + (cx + 1) * 3 + cz + 1, pl.ds(i, 1), :], pltpu.roll(t, sy - 1, 0))
            if vz == 1:
                t = jnp.where(lanes == 0, zcol[:, i : i + 1], pltpu.roll(t, 1, 1))
            elif vz == -1:
                t = jnp.where(lanes == sz - 1, zcol[:, i : i + 1], pltpu.roll(t, sz - 1, 1))
            dst[q, i] = t


def adjoint_rows(F, A, om, ga):
    rho = sum(F)
    mom = []
    for axis in range(3):
        pos = [F[q] for q in range(27) if STEPS[q, axis] == 1]
        neg = [F[q] for q in range(27) if STEPS[q, axis] == -1]
        mom.append(sum(pos) - sum(neg))
    vel = (mom[0] / rho, mom[1] / rho, mom[2] / rho)
    uu = vel[0] * vel[0] + vel[1] * vel[1] + vel[2] * vel[2]
    sens = 0.0
    e_rho = 0.0
    s0 = 0.0
    sm = [0.0, 0.0, 0.0]
    for q in range(27):
        c = STEPS[q]
        w = float(WEIGHTS[q])
        cu = None
        for axis in range(3):
            if c[axis] == 1:
                cu = vel[axis] if cu is None else cu + vel[axis]
            elif c[axis] == -1:
                cu = -vel[axis] if cu is None else cu - vel[axis]
        if cu is None:
            eq = w * rho * (1.0 - 1.5 * uu)
        else:
            eq = w * rho * (1.0 + 3.0 * cu + 4.5 * cu * cu - 1.5 * uu)
        bgk = F[q] - om * (F[q] - eq)
        sens = sens + A[q] * (F[26 - q] - bgk)
        aw = A[q] * w
        s0 = s0 + aw
        if cu is None:
            e_rho = e_rho + aw * (1.0 + 1.5 * uu)
        else:
            e_rho = e_rho + aw * (1.0 - 4.5 * cu * cu + 1.5 * uu)
            t = aw * (1.0 + 3.0 * cu)
            for axis in range(3):
                if c[axis] == 1:
                    sm[axis] = sm[axis] + t
                elif c[axis] == -1:
                    sm[axis] = sm[axis] - t
    em = [3.0 * sm[axis] - 3.0 * vel[axis] * s0 for axis in range(3)]
    keep = 1.0 - ga
    out = []
    for p in range(27):
        c = STEPS[p]
        g = e_rho
        for axis in range(3):
            if c[axis] == 1:
                g = g + em[axis]
            elif c[axis] == -1:
                g = g - em[axis]
        out.append(keep * ((1.0 - om) * A[p] + om * g) + ga * A[26 - p])
    return out, sens


def chunked_adjoint(f_ref, a_ref, rate_ref, gamma_ref, out_ref, sens_ref):
    _, sx, sy, sz = out_ref.shape
    halves = sy // 8

    def body(step, carry):
        i = step // halves
        h = pl.multiple_of((step % halves) * 8, 8)
        F = [f_ref[q, i, pl.ds(h, 8), :] for q in range(27)]
        A = [a_ref[q, i, pl.ds(h, 8), :] for q in range(27)]
        om = rate_ref[i, pl.ds(h, 8), :]
        ga = gamma_ref[i, pl.ds(h, 8), :]
        adj, sens = adjoint_rows(F, A, om, ga)
        for q in range(27):
            out_ref[q, i, pl.ds(h, 8), :] = adj[q]
        sens_ref[i, pl.ds(h, 8), :] = sens
        return carry

    lax.fori_loop(0, sx * halves, body, 0)


def next_kernel(cf_ref, ae_ref, *refs):
    hal = refs[0:6]
    rate_ref, gamma_ref, out_ref, sens_ref, fs, as_ = refs[6:]
    move_into(fs, cf_ref, hal, 1, 0)
    move_into(as_, ae_ref, hal, -1, 9)
    chunked_adjoint(fs, as_, rate_ref, gamma_ref, out_ref, sens_ref)


def now_kernel(an_ref, f_ref, *refs):
    hal = refs[0:6]
    rate_ref, gamma_ref, out_ref, sens_ref, as_ = refs[6:]
    move_into(as_, an_ref, hal, -1, 0)
    chunked_adjoint(f_ref, as_, rate_ref, gamma_ref, out_ref, sens_ref)


def run_stage(kernel, args, shape, scratch):
    _, sx, sy, sz = shape
    return pl.pallas_call(
        kernel,
        out_shape=(
            jax.ShapeDtypeStruct(shape, jnp.float32),
            jax.ShapeDtypeStruct((sx, sy, sz), jnp.float32),
        ),
        scratch_shapes=[pltpu.VMEM(shape, jnp.float32) for _ in range(scratch)],
    )(*args)


def shards(check_pops, adjoint_end, relax_rate, wall_flag, patch_of_cell, porosity, patch_slot):
    sx, sy, sz = relax_rate.shape
    ids = patch_of_cell[:, :: sy // 2, :: sz // 2]
    table = jnp.stack([porosity, patch_slot.astype(jnp.float32)], axis=1)
    looked = table[ids]
    solid = jnp.broadcast_to(looked[:, :, None, :, None, 0], (sx, 2, sy // 2, 2, sz // 2)).reshape(sx, sy, sz)
    walls = wall_flag.astype(jnp.float32)
    gamma = walls * solid
    post_now, _ = collide(check_pops, relax_rate, gamma)
    hal = halos([post_now, adjoint_end], [1, -1])
    shape = check_pops.shape
    adj_next, sens_next = run_stage(
        next_kernel, (post_now, adjoint_end) + hal + (relax_rate, gamma), shape, 2
    )
    hal_n = halos([adj_next], [-1])
    adjoint_start, sens_now = run_stage(now_kernel, (adj_next, check_pops) + hal_n + (relax_rate, gamma), shape, 1)
    density = walls * (sens_next + sens_now)
    boxes = density.reshape(sx, 2, sy // 2, 2, sz // 2).sum(axis=(2, 4))
    parts = jnp.stack([boxes[0], boxes[1 : sx - 1].sum(axis=0), boxes[sx - 1]])
    count = porosity.shape[0]
    devices = lax.axis_size(("gx", "gy", "gz"))
    slots = jnp.stack([looked[0, :, :, 1], looked[1, :, :, 1], looked[sx - 1, :, :, 1]]).reshape(-1)
    hits = (slots[:, None] == jnp.arange(count, dtype=jnp.float32)[None, :]).astype(jnp.float32)
    placed = jnp.sum(parts.reshape(-1)[:, None] * hits, axis=0)
    got = lax.all_to_all(placed.reshape(devices, count // devices), ("gx", "gy", "gz"), 0, 0, tiled=True)
    patch_sens = jnp.sum(got, axis=0)
    return (adjoint_start, patch_sens)


def solution(mesh):
    in_specs = (
        P(None, "gx", "gy", "gz"),
        P(None, "gx", "gy", "gz"),
        P("gx", "gy", "gz"),
        P("gx", "gy", "gz"),
        P("gx", "gy", "gz"),
        P(),
        P(),
    )
    out_specs = (P(None, "gx", "gy", "gz"), P(("gx", "gy", "gz")))
    return jax.shard_map(shards, mesh=mesh, in_specs=in_specs, out_specs=out_specs, check_vma=False)
```

```python
import jax
import jax.numpy as jnp
import numpy as np
from jax import lax
from jax.experimental import pallas as pl
from jax.experimental.pallas import tpu as pltpu
from jax.sharding import PartitionSpec as P


def lattice_table():
    steps = np.array(
        [
            [first, second, third]
            for first in (-1, 0, 1)
            for second in (-1, 0, 1)
            for third in (-1, 0, 1)
        ],
        dtype=np.int64,
    )
    moved = np.abs(steps).sum(axis=1)
    weights = np.array([8.0 / 27.0, 2.0 / 27.0, 1.0 / 54.0, 1.0 / 216.0])[moved]
    return (steps, weights)


STEPS, WEIGHTS = lattice_table()


def collide(pops, rate, gamma):
    steps, weights = lattice_table()
    cube = pops.reshape((3, 3, 3) + pops.shape[1:])
    density = jnp.sum(pops, axis=0)
    mom_x = jnp.sum(cube[2], axis=(0, 1)) - jnp.sum(cube[0], axis=(0, 1))
    mom_y = jnp.sum(cube[:, 2], axis=(0, 1)) - jnp.sum(cube[:, 0], axis=(0, 1))
    mom_z = jnp.sum(cube[:, :, 2], axis=(0, 1)) - jnp.sum(cube[:, :, 0], axis=(0, 1))
    vel_x = mom_x / density
    vel_y = mom_y / density
    vel_z = mom_z / density
    cx = jnp.asarray(steps[:, 0], jnp.float32)[:, None, None, None]
    cy = jnp.asarray(steps[:, 1], jnp.float32)[:, None, None, None]
    cz = jnp.asarray(steps[:, 2], jnp.float32)[:, None, None, None]
    wts = jnp.asarray(weights, jnp.float32)[:, None, None, None]
    along = cx * vel_x + cy * vel_y + cz * vel_z
    speed = vel_x * vel_x + vel_y * vel_y + vel_z * vel_z
    equil = wts * density * (1.0 + 3.0 * along + 4.5 * along * along - 1.5 * speed)
    relaxed = pops - rate * (pops - equil)
    flipped = pops[::-1]
    return ((1.0 - gamma) * relaxed + gamma * flipped, flipped - relaxed)


def halo_exchange(up, down, axis):
    size = lax.axis_size(axis)
    if size == 1:
        return up, down
    if size == 2:
        both = lax.ppermute(jnp.stack([up, down]), axis, [(0, 1), (1, 0)])
        return both[0], both[1]
    lo = lax.ppermute(up, axis, [(i, (i + 1) % size) for i in range(size)])
    hi = lax.ppermute(down, axis, [(i, (i - 1) % size) for i in range(size)])
    return lo, hi


def shifted(cube, lo, hi, d, sign):
    n = cube.shape[3 + d]
    plus = lax.index_in_dim(cube, 1 + sign, axis=d, keepdims=False)
    minus = lax.index_in_dim(cube, 1 - sign, axis=d, keepdims=False)
    still = lax.index_in_dim(cube, 1, axis=d, keepdims=False)
    plus = jnp.concatenate([lo, lax.slice_in_dim(plus, 0, n - 1, axis=2 + d)], axis=2 + d)
    minus = jnp.concatenate([lax.slice_in_dim(minus, 1, n, axis=2 + d), hi], axis=2 + d)
    groups = [None, still, None]
    groups[1 + sign] = plus
    groups[1 - sign] = minus
    return jnp.stack(groups, axis=d)


def faces(cube, sign, d):
    n = cube.shape[3 + d]
    plus = lax.index_in_dim(cube, 1 + sign, axis=d, keepdims=False)
    minus = lax.index_in_dim(cube, 1 - sign, axis=d, keepdims=False)
    return lax.slice_in_dim(plus, n - 1, n, axis=2 + d), lax.slice_in_dim(minus, 0, 1, axis=2 + d)


def columns_kernel(*refs):
    fields, out_ref = refs[:-1], refs[-1]
    _, sx, sy, sz = fields[0].shape
    pairs = [(r, q, i) for r in fields for q in range(27) for i in range(sx)]
    per = 128 // sy
    for g in range(out_ref.shape[1]):
        tiles = [r[q, i] for r, q, i in pairs[g * per : (g + 1) * per]]
        tiles += [jnp.zeros((sy, sz), jnp.float32)] * (per - len(tiles))
        flipped = jnp.concatenate(tiles, axis=0).T
        out_ref[0, pl.ds(g, 1), :] = flipped[sz - 1 : sz, :]
        out_ref[1, pl.ds(g, 1), :] = flipped[0:1, :]

def halos(fields, signs):
    cubes = [f.reshape((3, 3, 3) + f.shape[1:]) for f in fields]
    sx, sy, sz = cubes[0].shape[3:]
    x_up, x_dn = zip(*[faces(c, s, 0) for c, s in zip(cubes, signs)])
    xlo, xhi = halo_exchange(jnp.stack(x_up), jnp.stack(x_dn), "gx")
    both = jnp.stack(cubes)
    rows = jnp.concatenate([both[..., sy - 1 : sy, :], both[..., 0:1, :]], axis=5)
    if sy * 8 == 128 and sz == 128:
        count = len(fields) * 27 * sx
        flat = pl.pallas_call(
            columns_kernel, out_shape=jax.ShapeDtypeStruct((2, -(-count // 8), 128), jnp.float32)
        )(*fields)
        cols = flat.reshape(2, -1)[:, : count * sy].reshape((2, len(fields), 3, 3, 3, sx, sy))
    else:
        cols = None
        edges = jnp.concatenate([both[..., sz - 1 : sz], both[..., 0:1]], axis=6)
    y_up, y_dn = [], []
    for k, s in enumerate(signs):
        top = shifted(rows[k][..., 0:1, :], xlo[k][:, :, :, sy - 1 : sy], xhi[k][:, :, :, sy - 1 : sy], 0, s)
        bot = shifted(rows[k][..., 1:2, :], xlo[k][:, :, :, 0:1], xhi[k][:, :, :, 0:1], 0, s)
        y_up.append(lax.index_in_dim(top, 1 + s, axis=1, keepdims=False))
        y_dn.append(lax.index_in_dim(bot, 1 - s, axis=1, keepdims=False))
    ylo, yhi = halo_exchange(jnp.stack(y_up), jnp.stack(y_dn), "gy")
    z_up, z_dn = [], []
    for k, s in enumerate(signs):
        picked = []
        for at, z0 in ((0, sz - 1), (1, 0)):
            if cols is None:
                col = edges[k][..., at : at + 1]
                col = shifted(col, xlo[k][..., z0 : z0 + 1], xhi[k][..., z0 : z0 + 1], 0, s)
                col = shifted(col, ylo[k][..., z0 : z0 + 1], yhi[k][..., z0 : z0 + 1], 1, s)[..., 0]
            else:
                col = shifted(cols[at, k], xlo[k][..., z0], xhi[k][..., z0], 0, s)
                col = shifted(col, ylo[k][..., z0], yhi[k][..., z0], 1, s)
            picked.append(col)
        z_up.append(jnp.swapaxes(lax.index_in_dim(picked[0], 1 + s, axis=2, keepdims=False), -1, -2))
        z_dn.append(jnp.swapaxes(lax.index_in_dim(picked[1], 1 - s, axis=2, keepdims=False), -1, -2))
    zlo, zhi = halo_exchange(jnp.stack(z_up), jnp.stack(z_dn), "gz")
    nf = len(cubes)
    return (
        xlo.reshape(nf * 9, sy, sz),
        xhi.reshape(nf * 9, sy, sz),
        ylo.reshape(nf * 9, sx, sz),
        yhi.reshape(nf * 9, sx, sz),
        zlo.reshape(nf * 9, sy, sx),
        zhi.reshape(nf * 9, sy, sx),
    )


def move_into(dst, src, hal, sign, base):
    xlo, xhi, ylo, yhi, zlo, zhi = hal
    _, sx, sy, sz = src.shape
    rows = lax.broadcasted_iota(jnp.int32, (sy, sz), 0)
    lanes = lax.broadcasted_iota(jnp.int32, (sy, sz), 1)
    for q in range(27):
        cx, cy, cz = (int(v) for v in STEPS[q])
        vx, vy, vz = sign * cx, sign * cy, sign * cz
        if vz == 1:
            zcol = zlo[base + (cx + 1) * 3 + cy + 1]
        elif vz == -1:
            zcol = zhi[base + (cx + 1) * 3 + cy + 1]
        for i in range(sx):
            j = i - vx
            if j < 0:
                t = xlo[base + (cy + 1) * 3 + cz + 1]
            elif j >= sx:
                t = xhi[base + (cy + 1) * 3 + cz + 1]
            else:
                t = src[q, j]
            if vy == 1:
                t = jnp.where(rows == 0, ylo[base + (cx + 1) * 3 + cz + 1, pl.ds(i, 1), :], pltpu.roll(t, 1, 0))
            elif vy == -1:
                t = jnp.where(rows == sy - 1, yhi[base + (cx + 1) * 3 + cz + 1, pl.ds(i, 1), :], pltpu.roll(t, sy - 1, 0))
            if vz == 1:
                t = jnp.where(lanes == 0, zcol[:, i : i + 1], pltpu.roll(t, 1, 1))
            elif vz == -1:
                t = jnp.where(lanes == sz - 1, zcol[:, i : i + 1], pltpu.roll(t, sz - 1, 1))
            dst[q, i] = t


def adjoint_rows(F, A, om, ga):
    rho = sum(F)
    mom = []
    for axis in range(3):
        pos = [F[q] for q in range(27) if STEPS[q, axis] == 1]
        neg = [F[q] for q in range(27) if STEPS[q, axis] == -1]
        mom.append(sum(pos) - sum(neg))
    vel = (mom[0] / rho, mom[1] / rho, mom[2] / rho)
    uu = vel[0] * vel[0] + vel[1] * vel[1] + vel[2] * vel[2]
    sens = 0.0
    e_rho = 0.0
    s0 = 0.0
    sm = [0.0, 0.0, 0.0]
    for q in range(27):
        c = STEPS[q]
        w = float(WEIGHTS[q])
        cu = None
        for axis in range(3):
            if c[axis] == 1:
                cu = vel[axis] if cu is None else cu + vel[axis]
            elif c[axis] == -1:
                cu = -vel[axis] if cu is None else cu - vel[axis]
        if cu is None:
            eq = w * rho * (1.0 - 1.5 * uu)
        else:
            eq = w * rho * (1.0 + 3.0 * cu + 4.5 * cu * cu - 1.5 * uu)
        bgk = F[q] - om * (F[q] - eq)
        sens = sens + A[q] * (F[26 - q] - bgk)
        aw = A[q] * w
        s0 = s0 + aw
        if cu is None:
            e_rho = e_rho + aw * (1.0 + 1.5 * uu)
        else:
            e_rho = e_rho + aw * (1.0 - 4.5 * cu * cu + 1.5 * uu)
            t = aw * (1.0 + 3.0 * cu)
            for axis in range(3):
                if c[axis] == 1:
                    sm[axis] = sm[axis] + t
                elif c[axis] == -1:
                    sm[axis] = sm[axis] - t
    em = [3.0 * sm[axis] - 3.0 * vel[axis] * s0 for axis in range(3)]
    keep = 1.0 - ga
    out = []
    for p in range(27):
        c = STEPS[p]
        g = e_rho
        for axis in range(3):
            if c[axis] == 1:
                g = g + em[axis]
            elif c[axis] == -1:
                g = g - em[axis]
        out.append(keep * ((1.0 - om) * A[p] + om * g) + ga * A[26 - p])
    return out, sens


def chunked_adjoint(f_ref, a_ref, rate_ref, gamma_ref, out_ref, sens_ref):
    _, sx, sy, sz = out_ref.shape
    halves = sy // 8

    def body(step, carry):
        i = step // halves
        h = pl.multiple_of((step % halves) * 8, 8)
        F = [f_ref[q, i, pl.ds(h, 8), :] for q in range(27)]
        A = [a_ref[q, i, pl.ds(h, 8), :] for q in range(27)]
        om = rate_ref[i, pl.ds(h, 8), :]
        ga = gamma_ref[i, pl.ds(h, 8), :]
        adj, sens = adjoint_rows(F, A, om, ga)
        for q in range(27):
            out_ref[q, i, pl.ds(h, 8), :] = adj[q]
        sens_ref[i, pl.ds(h, 8), :] = sens
        return carry

    lax.fori_loop(0, sx * halves, body, 0)


def next_kernel(cf_ref, ae_ref, *refs):
    hal = refs[0:6]
    rate_ref, gamma_ref, out_ref, sens_ref, fs, as_ = refs[6:]
    move_into(fs, cf_ref, hal, 1, 0)
    move_into(as_, ae_ref, hal, -1, 9)
    chunked_adjoint(fs, as_, rate_ref, gamma_ref, out_ref, sens_ref)


def now_kernel(an_ref, f_ref, *refs):
    hal = refs[0:6]
    rate_ref, gamma_ref, out_ref, sens_ref, as_ = refs[6:]
    move_into(as_, an_ref, hal, -1, 0)
    chunked_adjoint(f_ref, as_, rate_ref, gamma_ref, out_ref, sens_ref)


def run_stage(kernel, args, shape, scratch):
    _, sx, sy, sz = shape
    return pl.pallas_call(
        kernel,
        out_shape=(
            jax.ShapeDtypeStruct(shape, jnp.float32),
            jax.ShapeDtypeStruct((sx, sy, sz), jnp.float32),
        ),
        scratch_shapes=[pltpu.VMEM(shape, jnp.float32) for _ in range(scratch)],
    )(*args)


def shards(check_pops, adjoint_end, relax_rate, wall_flag, patch_of_cell, porosity, patch_slot):
    sx, sy, sz = relax_rate.shape
    ids = patch_of_cell[:, :: sy // 2, :: sz // 2]
    table = jnp.stack([porosity, patch_slot.astype(jnp.float32)], axis=1)
    looked = table[ids]
    solid = jnp.broadcast_to(looked[:, :, None, :, None, 0], (sx, 2, sy // 2, 2, sz // 2)).reshape(sx, sy, sz)
    walls = wall_flag.astype(jnp.float32)
    gamma = walls * solid
    post_now, _ = collide(check_pops, relax_rate, gamma)
    hal = halos([post_now, adjoint_end], [1, -1])
    shape = check_pops.shape
    adj_next, sens_next = run_stage(
        next_kernel, (post_now, adjoint_end) + hal + (relax_rate, gamma), shape, 2
    )
    hal_n = halos([adj_next], [-1])
    adjoint_start, sens_now = run_stage(now_kernel, (adj_next, check_pops) + hal_n + (relax_rate, gamma), shape, 1)
    density = walls * (sens_next + sens_now)
    boxes = density.reshape(sx, 2, sy // 2, 2, sz // 2).sum(axis=(2, 4))
    parts = jnp.stack([boxes[0], boxes[1 : sx - 1].sum(axis=0), boxes[sx - 1]])
    count = porosity.shape[0]
    devices = lax.axis_size(("gx", "gy", "gz"))
    slots = jnp.stack([looked[0, :, :, 1], looked[1, :, :, 1], looked[sx - 1, :, :, 1]]).reshape(-1)
    hits = (slots[:, None] == jnp.arange(count, dtype=jnp.float32)[None, :]).astype(jnp.float32)
    placed = jnp.sum(parts.reshape(-1)[:, None] * hits, axis=0)
    got = lax.all_to_all(placed.reshape(devices, count // devices), ("gx", "gy", "gz"), 0, 0, tiled=True)
    patch_sens = jnp.sum(got, axis=0)
    return (adjoint_start, patch_sens)


def solution(mesh):
    in_specs = (
        P(None, "gx", "gy", "gz"),
        P(None, "gx", "gy", "gz"),
        P("gx", "gy", "gz"),
        P("gx", "gy", "gz"),
        P("gx", "gy", "gz"),
        P(),
        P(),
    )
    out_specs = (P(None, "gx", "gy", "gz"), P(("gx", "gy", "gz")))
    return jax.shard_map(shards, mesh=mesh, in_specs=in_specs, out_specs=out_specs, check_vma=False)
```

```python
import jax
import jax.numpy as jnp
import numpy as np
from jax import lax
from jax.experimental import pallas as pl
from jax.experimental.pallas import tpu as pltpu
from jax.sharding import PartitionSpec as P


def lattice_table():
    steps = np.array(
        [
            [first, second, third]
            for first in (-1, 0, 1)
            for second in (-1, 0, 1)
            for third in (-1, 0, 1)
        ],
        dtype=np.int64,
    )
    moved = np.abs(steps).sum(axis=1)
    weights = np.array([8.0 / 27.0, 2.0 / 27.0, 1.0 / 54.0, 1.0 / 216.0])[moved]
    return (steps, weights)


STEPS, WEIGHTS = lattice_table()


def collide(pops, rate, gamma):
    steps, weights = lattice_table()
    cube = pops.reshape((3, 3, 3) + pops.shape[1:])
    density = jnp.sum(pops, axis=0)
    mom_x = jnp.sum(cube[2], axis=(0, 1)) - jnp.sum(cube[0], axis=(0, 1))
    mom_y = jnp.sum(cube[:, 2], axis=(0, 1)) - jnp.sum(cube[:, 0], axis=(0, 1))
    mom_z = jnp.sum(cube[:, :, 2], axis=(0, 1)) - jnp.sum(cube[:, :, 0], axis=(0, 1))
    vel_x = mom_x / density
    vel_y = mom_y / density
    vel_z = mom_z / density
    cx = jnp.asarray(steps[:, 0], jnp.float32)[:, None, None, None]
    cy = jnp.asarray(steps[:, 1], jnp.float32)[:, None, None, None]
    cz = jnp.asarray(steps[:, 2], jnp.float32)[:, None, None, None]
    wts = jnp.asarray(weights, jnp.float32)[:, None, None, None]
    along = cx * vel_x + cy * vel_y + cz * vel_z
    speed = vel_x * vel_x + vel_y * vel_y + vel_z * vel_z
    equil = wts * density * (1.0 + 3.0 * along + 4.5 * along * along - 1.5 * speed)
    relaxed = pops - rate * (pops - equil)
    flipped = pops[::-1]
    return ((1.0 - gamma) * relaxed + gamma * flipped, flipped - relaxed)


def halo_exchange(up, down, axis):
    size = lax.axis_size(axis)
    if size == 1:
        return up, down
    if size == 2:
        both = lax.ppermute(jnp.stack([up, down]), axis, [(0, 1), (1, 0)])
        return both[0], both[1]
    lo = lax.ppermute(up, axis, [(i, (i + 1) % size) for i in range(size)])
    hi = lax.ppermute(down, axis, [(i, (i - 1) % size) for i in range(size)])
    return lo, hi


def shifted(cube, lo, hi, d, sign):
    n = cube.shape[3 + d]
    plus = lax.index_in_dim(cube, 1 + sign, axis=d, keepdims=False)
    minus = lax.index_in_dim(cube, 1 - sign, axis=d, keepdims=False)
    still = lax.index_in_dim(cube, 1, axis=d, keepdims=False)
    plus = jnp.concatenate([lo, lax.slice_in_dim(plus, 0, n - 1, axis=2 + d)], axis=2 + d)
    minus = jnp.concatenate([lax.slice_in_dim(minus, 1, n, axis=2 + d), hi], axis=2 + d)
    groups = [None, still, None]
    groups[1 + sign] = plus
    groups[1 - sign] = minus
    return jnp.stack(groups, axis=d)


def faces(cube, sign, d):
    n = cube.shape[3 + d]
    plus = lax.index_in_dim(cube, 1 + sign, axis=d, keepdims=False)
    minus = lax.index_in_dim(cube, 1 - sign, axis=d, keepdims=False)
    return lax.slice_in_dim(plus, n - 1, n, axis=2 + d), lax.slice_in_dim(minus, 0, 1, axis=2 + d)


def columns_kernel(a_ref, b_ref, out_ref):
    _, sx, sy, sz = a_ref.shape
    pairs = [(r, q, i) for r in (a_ref, b_ref) for q in range(27) for i in range(sx)]
    per = 128 // sy
    for g in range(len(pairs) // per):
        block = jnp.concatenate([r[q, i] for r, q, i in pairs[g * per : (g + 1) * per]], axis=0)
        flipped = block.T
        out_ref[0, pl.ds(g, 1), :] = flipped[sz - 1 : sz, :]
        out_ref[1, pl.ds(g, 1), :] = flipped[0:1, :]


def halos(fields, signs):
    cubes = [f.reshape((3, 3, 3) + f.shape[1:]) for f in fields]
    sx, sy, sz = cubes[0].shape[3:]
    x_up, x_dn = zip(*[faces(c, s, 0) for c, s in zip(cubes, signs)])
    xlo, xhi = halo_exchange(jnp.stack(x_up), jnp.stack(x_dn), "gx")
    both = jnp.stack(cubes)
    rows = jnp.concatenate([both[..., sy - 1 : sy, :], both[..., 0:1, :]], axis=5)
    if len(fields) == 2 and sy * 8 == 128 and sz == 128:
        flat = pl.pallas_call(
            columns_kernel, out_shape=jax.ShapeDtypeStruct((2, 2 * 27 * sx * sy // 128, 128), jnp.float32)
        )(fields[0], fields[1])
        cols = flat.reshape((2, 2, 3, 3, 3, sx, sy))
    else:
        cols = None
        edges = jnp.concatenate([both[..., sz - 1 : sz], both[..., 0:1]], axis=6)
    y_up, y_dn = [], []
    for k, s in enumerate(signs):
        top = shifted(rows[k][..., 0:1, :], xlo[k][:, :, :, sy - 1 : sy], xhi[k][:, :, :, sy - 1 : sy], 0, s)
        bot = shifted(rows[k][..., 1:2, :], xlo[k][:, :, :, 0:1], xhi[k][:, :, :, 0:1], 0, s)
        y_up.append(lax.index_in_dim(top, 1 + s, axis=1, keepdims=False))
        y_dn.append(lax.index_in_dim(bot, 1 - s, axis=1, keepdims=False))
    ylo, yhi = halo_exchange(jnp.stack(y_up), jnp.stack(y_dn), "gy")
    z_up, z_dn = [], []
    for k, s in enumerate(signs):
        picked = []
        for at, z0 in ((0, sz - 1), (1, 0)):
            if cols is None:
                col = edges[k][..., at : at + 1]
                col = shifted(col, xlo[k][..., z0 : z0 + 1], xhi[k][..., z0 : z0 + 1], 0, s)
                col = shifted(col, ylo[k][..., z0 : z0 + 1], yhi[k][..., z0 : z0 + 1], 1, s)[..., 0]
            else:
                col = shifted(cols[at, k], xlo[k][..., z0], xhi[k][..., z0], 0, s)
                col = shifted(col, ylo[k][..., z0], yhi[k][..., z0], 1, s)
            picked.append(col)
        z_up.append(jnp.swapaxes(lax.index_in_dim(picked[0], 1 + s, axis=2, keepdims=False), -1, -2))
        z_dn.append(jnp.swapaxes(lax.index_in_dim(picked[1], 1 - s, axis=2, keepdims=False), -1, -2))
    zlo, zhi = halo_exchange(jnp.stack(z_up), jnp.stack(z_dn), "gz")
    nf = len(cubes)
    return (
        xlo.reshape(nf * 9, sy, sz),
        xhi.reshape(nf * 9, sy, sz),
        ylo.reshape(nf * 9, sx, sz),
        yhi.reshape(nf * 9, sx, sz),
        zlo.reshape(nf * 9, sy, sx),
        zhi.reshape(nf * 9, sy, sx),
    )


def move_into(dst, src, hal, sign, base):
    xlo, xhi, ylo, yhi, zlo, zhi = hal
    _, sx, sy, sz = src.shape
    rows = lax.broadcasted_iota(jnp.int32, (sy, sz), 0)
    lanes = lax.broadcasted_iota(jnp.int32, (sy, sz), 1)
    for q in range(27):
        cx, cy, cz = (int(v) for v in STEPS[q])
        vx, vy, vz = sign * cx, sign * cy, sign * cz
        if vz == 1:
            zcol = zlo[base + (cx + 1) * 3 + cy + 1]
        elif vz == -1:
            zcol = zhi[base + (cx + 1) * 3 + cy + 1]
        for i in range(sx):
            j = i - vx
            if j < 0:
                t = xlo[base + (cy + 1) * 3 + cz + 1]
            elif j >= sx:
                t = xhi[base + (cy + 1) * 3 + cz + 1]
            else:
                t = src[q, j]
            if vy == 1:
                t = jnp.where(rows == 0, ylo[base + (cx + 1) * 3 + cz + 1, pl.ds(i, 1), :], pltpu.roll(t, 1, 0))
            elif vy == -1:
                t = jnp.where(rows == sy - 1, yhi[base + (cx + 1) * 3 + cz + 1, pl.ds(i, 1), :], pltpu.roll(t, sy - 1, 0))
            if vz == 1:
                t = jnp.where(lanes == 0, zcol[:, i : i + 1], pltpu.roll(t, 1, 1))
            elif vz == -1:
                t = jnp.where(lanes == sz - 1, zcol[:, i : i + 1], pltpu.roll(t, sz - 1, 1))
            dst[q, i] = t


def adjoint_rows(F, A, om, ga):
    rho = sum(F)
    mom = []
    for axis in range(3):
        pos = [F[q] for q in range(27) if STEPS[q, axis] == 1]
        neg = [F[q] for q in range(27) if STEPS[q, axis] == -1]
        mom.append(sum(pos) - sum(neg))
    vel = (mom[0] / rho, mom[1] / rho, mom[2] / rho)
    uu = vel[0] * vel[0] + vel[1] * vel[1] + vel[2] * vel[2]
    sens = 0.0
    e_rho = 0.0
    s0 = 0.0
    sm = [0.0, 0.0, 0.0]
    for q in range(27):
        c = STEPS[q]
        w = float(WEIGHTS[q])
        cu = None
        for axis in range(3):
            if c[axis] == 1:
                cu = vel[axis] if cu is None else cu + vel[axis]
            elif c[axis] == -1:
                cu = -vel[axis] if cu is None else cu - vel[axis]
        if cu is None:
            eq = w * rho * (1.0 - 1.5 * uu)
        else:
            eq = w * rho * (1.0 + 3.0 * cu + 4.5 * cu * cu - 1.5 * uu)
        bgk = F[q] - om * (F[q] - eq)
        sens = sens + A[q] * (F[26 - q] - bgk)
        aw = A[q] * w
        s0 = s0 + aw
        if cu is None:
            e_rho = e_rho + aw * (1.0 + 1.5 * uu)
        else:
            e_rho = e_rho + aw * (1.0 - 4.5 * cu * cu + 1.5 * uu)
            t = aw * (1.0 + 3.0 * cu)
            for axis in range(3):
                if c[axis] == 1:
                    sm[axis] = sm[axis] + t
                elif c[axis] == -1:
                    sm[axis] = sm[axis] - t
    em = [3.0 * sm[axis] - 3.0 * vel[axis] * s0 for axis in range(3)]
    keep = 1.0 - ga
    out = []
    for p in range(27):
        c = STEPS[p]
        g = e_rho
        for axis in range(3):
            if c[axis] == 1:
                g = g + em[axis]
            elif c[axis] == -1:
                g = g - em[axis]
        out.append(keep * ((1.0 - om) * A[p] + om * g) + ga * A[26 - p])
    return out, sens


def chunked_adjoint(f_ref, a_ref, rate_ref, gamma_ref, out_ref, sens_ref):
    _, sx, sy, sz = out_ref.shape
    halves = sy // 8

    def body(step, carry):
        i = step // halves
        h = pl.multiple_of((step % halves) * 8, 8)
        F = [f_ref[q, i, pl.ds(h, 8), :] for q in range(27)]
        A = [a_ref[q, i, pl.ds(h, 8), :] for q in range(27)]
        om = rate_ref[i, pl.ds(h, 8), :]
        ga = gamma_ref[i, pl.ds(h, 8), :]
        adj, sens = adjoint_rows(F, A, om, ga)
        for q in range(27):
            out_ref[q, i, pl.ds(h, 8), :] = adj[q]
        sens_ref[i, pl.ds(h, 8), :] = sens
        return carry

    lax.fori_loop(0, sx * halves, body, 0)


def next_kernel(cf_ref, ae_ref, *refs):
    hal = refs[0:6]
    rate_ref, gamma_ref, out_ref, sens_ref, fs, as_ = refs[6:]
    move_into(fs, cf_ref, hal, 1, 0)
    move_into(as_, ae_ref, hal, -1, 9)
    chunked_adjoint(fs, as_, rate_ref, gamma_ref, out_ref, sens_ref)


def now_kernel(an_ref, f_ref, *refs):
    hal = refs[0:6]
    rate_ref, gamma_ref, moved_ref, sens_ref = refs[6:]
    move_into(moved_ref, an_ref, hal, -1, 0)
    _, sx, sy, sz = f_ref.shape
    halves = sy // 8

    def body(step, carry):
        i = step // halves
        h = pl.multiple_of((step % halves) * 8, 8)
        F = [f_ref[q, i, pl.ds(h, 8), :] for q in range(27)]
        A = [moved_ref[q, i, pl.ds(h, 8), :] for q in range(27)]
        _, sens = adjoint_rows(F, A, rate_ref[i, pl.ds(h, 8), :], gamma_ref[i, pl.ds(h, 8), :])
        sens_ref[i, pl.ds(h, 8), :] = sens
        return carry

    lax.fori_loop(0, sx * halves, body, 0)


def start_kernel(f_ref, moved_ref, rate_ref, gamma_ref, out_ref, sens_ref):
    chunked_adjoint(f_ref, moved_ref, rate_ref, gamma_ref, out_ref, sens_ref)


def run_stage(kernel, args, shape, scratch):
    _, sx, sy, sz = shape
    return pl.pallas_call(
        kernel,
        out_shape=(
            jax.ShapeDtypeStruct(shape, jnp.float32),
            jax.ShapeDtypeStruct((sx, sy, sz), jnp.float32),
        ),
        scratch_shapes=[pltpu.VMEM(shape, jnp.float32) for _ in range(scratch)],
    )(*args)


def shards(check_pops, adjoint_end, relax_rate, wall_flag, patch_of_cell, porosity, patch_slot):
    sx, sy, sz = relax_rate.shape
    ids = patch_of_cell[:, :: sy // 2, :: sz // 2]
    table = jnp.stack([porosity, patch_slot.astype(jnp.float32)], axis=1)
    looked = table[ids]
    solid = jnp.broadcast_to(looked[:, :, None, :, None, 0], (sx, 2, sy // 2, 2, sz // 2)).reshape(sx, sy, sz)
    walls = wall_flag.astype(jnp.float32)
    gamma = walls * solid
    post_now, _ = collide(check_pops, relax_rate, gamma)
    hal = halos([post_now, adjoint_end], [1, -1])
    shape = check_pops.shape
    adj_next, sens_next = run_stage(
        next_kernel, (post_now, adjoint_end) + hal + (relax_rate, gamma), shape, 2
    )
    hal_n = halos([adj_next], [-1])
    post_adj, sens_now = run_stage(now_kernel, (adj_next, check_pops) + hal_n + (relax_rate, gamma), shape, 0)
    adjoint_start, _ = run_stage(start_kernel, (check_pops, post_adj, relax_rate, gamma), shape, 0)
    density = walls * (sens_next + sens_now)
    boxes = density.reshape(sx, 2, sy // 2, 2, sz // 2).sum(axis=(2, 4))
    parts = jnp.stack([boxes[0], boxes[1 : sx - 1].sum(axis=0), boxes[sx - 1]])
    count = porosity.shape[0]
    devices = lax.axis_size(("gx", "gy", "gz"))
    slots = jnp.stack([looked[0, :, :, 1], looked[1, :, :, 1], looked[sx - 1, :, :, 1]]).reshape(-1)
    hits = (slots[:, None] == jnp.arange(count, dtype=jnp.float32)[None, :]).astype(jnp.float32)
    placed = jnp.sum(parts.reshape(-1)[:, None] * hits, axis=0)
    got = lax.all_to_all(placed.reshape(devices, count // devices), ("gx", "gy", "gz"), 0, 0, tiled=True)
    patch_sens = jnp.sum(got, axis=0)
    return (adjoint_start, patch_sens)


def solution(mesh):
    in_specs = (
        P(None, "gx", "gy", "gz"),
        P(None, "gx", "gy", "gz"),
        P("gx", "gy", "gz"),
        P("gx", "gy", "gz"),
        P("gx", "gy", "gz"),
        P(),
        P(),
    )
    out_specs = (P(None, "gx", "gy", "gz"), P(("gx", "gy", "gz")))
    return jax.shard_map(shards, mesh=mesh, in_specs=in_specs, out_specs=out_specs, check_vma=False)
```

```python
import jax
import jax.numpy as jnp
import numpy as np
from jax import lax
from jax.experimental import pallas as pl
from jax.experimental.pallas import tpu as pltpu
from jax.sharding import PartitionSpec as P


def lattice_table():
    steps = np.array(
        [
            [first, second, third]
            for first in (-1, 0, 1)
            for second in (-1, 0, 1)
            for third in (-1, 0, 1)
        ],
        dtype=np.int64,
    )
    moved = np.abs(steps).sum(axis=1)
    weights = np.array([8.0 / 27.0, 2.0 / 27.0, 1.0 / 54.0, 1.0 / 216.0])[moved]
    return (steps, weights)


STEPS, WEIGHTS = lattice_table()


def collide(pops, rate, gamma):
    steps, weights = lattice_table()
    cube = pops.reshape((3, 3, 3) + pops.shape[1:])
    density = jnp.sum(pops, axis=0)
    mom_x = jnp.sum(cube[2], axis=(0, 1)) - jnp.sum(cube[0], axis=(0, 1))
    mom_y = jnp.sum(cube[:, 2], axis=(0, 1)) - jnp.sum(cube[:, 0], axis=(0, 1))
    mom_z = jnp.sum(cube[:, :, 2], axis=(0, 1)) - jnp.sum(cube[:, :, 0], axis=(0, 1))
    vel_x = mom_x / density
    vel_y = mom_y / density
    vel_z = mom_z / density
    cx = jnp.asarray(steps[:, 0], jnp.float32)[:, None, None, None]
    cy = jnp.asarray(steps[:, 1], jnp.float32)[:, None, None, None]
    cz = jnp.asarray(steps[:, 2], jnp.float32)[:, None, None, None]
    wts = jnp.asarray(weights, jnp.float32)[:, None, None, None]
    along = cx * vel_x + cy * vel_y + cz * vel_z
    speed = vel_x * vel_x + vel_y * vel_y + vel_z * vel_z
    equil = wts * density * (1.0 + 3.0 * along + 4.5 * along * along - 1.5 * speed)
    relaxed = pops - rate * (pops - equil)
    flipped = pops[::-1]
    return ((1.0 - gamma) * relaxed + gamma * flipped, flipped - relaxed)


def halo_exchange(up, down, axis):
    size = lax.axis_size(axis)
    if size == 1:
        return up, down
    if size == 2:
        both = lax.ppermute(jnp.stack([up, down]), axis, [(0, 1), (1, 0)])
        return both[0], both[1]
    lo = lax.ppermute(up, axis, [(i, (i + 1) % size) for i in range(size)])
    hi = lax.ppermute(down, axis, [(i, (i - 1) % size) for i in range(size)])
    return lo, hi


def shifted(cube, lo, hi, d, sign):
    n = cube.shape[3 + d]
    plus = lax.index_in_dim(cube, 1 + sign, axis=d, keepdims=False)
    minus = lax.index_in_dim(cube, 1 - sign, axis=d, keepdims=False)
    still = lax.index_in_dim(cube, 1, axis=d, keepdims=False)
    plus = jnp.concatenate([lo, lax.slice_in_dim(plus, 0, n - 1, axis=2 + d)], axis=2 + d)
    minus = jnp.concatenate([lax.slice_in_dim(minus, 1, n, axis=2 + d), hi], axis=2 + d)
    groups = [None, still, None]
    groups[1 + sign] = plus
    groups[1 - sign] = minus
    return jnp.stack(groups, axis=d)


def faces(cube, sign, d):
    n = cube.shape[3 + d]
    plus = lax.index_in_dim(cube, 1 + sign, axis=d, keepdims=False)
    minus = lax.index_in_dim(cube, 1 - sign, axis=d, keepdims=False)
    return lax.slice_in_dim(plus, n - 1, n, axis=2 + d), lax.slice_in_dim(minus, 0, 1, axis=2 + d)


def columns_kernel(a_ref, b_ref, out_ref, rows_ref):
    _, sx, sy, sz = a_ref.shape
    pairs = [(r, q, i) for r in (a_ref, b_ref) for q in range(27) for i in range(sx)]
    per = 128 // sy
    for p, (r, q, i) in enumerate(pairs):
        rows_ref[0, pl.ds(p, 1), :] = r[q, i, pl.ds(sy - 1, 1), :]
        rows_ref[1, pl.ds(p, 1), :] = r[q, i, pl.ds(0, 1), :]
    for g in range(len(pairs) // per):
        block = jnp.concatenate([r[q, i] for r, q, i in pairs[g * per : (g + 1) * per]], axis=0)
        flipped = block.T
        out_ref[0, pl.ds(g, 1), :] = flipped[sz - 1 : sz, :]
        out_ref[1, pl.ds(g, 1), :] = flipped[0:1, :]


def halos(fields, signs):
    cubes = [f.reshape((3, 3, 3) + f.shape[1:]) for f in fields]
    sx, sy, sz = cubes[0].shape[3:]
    x_up, x_dn = zip(*[faces(c, s, 0) for c, s in zip(cubes, signs)])
    xlo, xhi = halo_exchange(jnp.stack(x_up), jnp.stack(x_dn), "gx")
    both = jnp.stack(cubes)
    rows = jnp.concatenate([both[..., sy - 1 : sy, :], both[..., 0:1, :]], axis=5)
    if len(fields) == 2 and sy * 8 == 128 and sz == 128:
        flat, edge_rows = pl.pallas_call(
            columns_kernel,
            out_shape=(
                jax.ShapeDtypeStruct((2, 2 * 27 * sx * sy // 128, 128), jnp.float32),
                jax.ShapeDtypeStruct((2, 2 * 27 * sx, sz), jnp.float32),
            ),
        )(fields[0], fields[1])
        cols = flat.reshape((2, 2, 3, 3, 3, sx, sy))
        edge_rows = edge_rows.reshape((2, 2, 3, 3, 3, sx, 1, sz))
        rows = jnp.concatenate([edge_rows[0], edge_rows[1]], axis=5)
    else:
        cols = None
        edges = jnp.concatenate([both[..., sz - 1 : sz], both[..., 0:1]], axis=6)
    y_up, y_dn = [], []
    for k, s in enumerate(signs):
        top = shifted(rows[k][..., 0:1, :], xlo[k][:, :, :, sy - 1 : sy], xhi[k][:, :, :, sy - 1 : sy], 0, s)
        bot = shifted(rows[k][..., 1:2, :], xlo[k][:, :, :, 0:1], xhi[k][:, :, :, 0:1], 0, s)
        y_up.append(lax.index_in_dim(top, 1 + s, axis=1, keepdims=False))
        y_dn.append(lax.index_in_dim(bot, 1 - s, axis=1, keepdims=False))
    ylo, yhi = halo_exchange(jnp.stack(y_up), jnp.stack(y_dn), "gy")
    z_up, z_dn = [], []
    for k, s in enumerate(signs):
        picked = []
        for at, z0 in ((0, sz - 1), (1, 0)):
            if cols is None:
                col = edges[k][..., at : at + 1]
                col = shifted(col, xlo[k][..., z0 : z0 + 1], xhi[k][..., z0 : z0 + 1], 0, s)
                col = shifted(col, ylo[k][..., z0 : z0 + 1], yhi[k][..., z0 : z0 + 1], 1, s)[..., 0]
            else:
                col = shifted(cols[at, k], xlo[k][..., z0], xhi[k][..., z0], 0, s)
                col = shifted(col, ylo[k][..., z0], yhi[k][..., z0], 1, s)
            picked.append(col)
        z_up.append(jnp.swapaxes(lax.index_in_dim(picked[0], 1 + s, axis=2, keepdims=False), -1, -2))
        z_dn.append(jnp.swapaxes(lax.index_in_dim(picked[1], 1 - s, axis=2, keepdims=False), -1, -2))
    zlo, zhi = halo_exchange(jnp.stack(z_up), jnp.stack(z_dn), "gz")
    nf = len(cubes)
    return (
        xlo.reshape(nf * 9, sy, sz),
        xhi.reshape(nf * 9, sy, sz),
        ylo.reshape(nf * 9, sx, sz),
        yhi.reshape(nf * 9, sx, sz),
        zlo.reshape(nf * 9, sy, sx),
        zhi.reshape(nf * 9, sy, sx),
    )


def move_into(dst, src, hal, sign, base):
    xlo, xhi, ylo, yhi, zlo, zhi = hal
    _, sx, sy, sz = src.shape
    rows = lax.broadcasted_iota(jnp.int32, (sy, sz), 0)
    lanes = lax.broadcasted_iota(jnp.int32, (sy, sz), 1)
    for q in range(27):
        cx, cy, cz = (int(v) for v in STEPS[q])
        vx, vy, vz = sign * cx, sign * cy, sign * cz
        if vz == 1:
            zcol = zlo[base + (cx + 1) * 3 + cy + 1]
        elif vz == -1:
            zcol = zhi[base + (cx + 1) * 3 + cy + 1]
        for i in range(sx):
            j = i - vx
            if j < 0:
                t = xlo[base + (cy + 1) * 3 + cz + 1]
            elif j >= sx:
                t = xhi[base + (cy + 1) * 3 + cz + 1]
            else:
                t = src[q, j]
            if vy == 1:
                t = jnp.where(rows == 0, ylo[base + (cx + 1) * 3 + cz + 1, pl.ds(i, 1), :], pltpu.roll(t, 1, 0))
            elif vy == -1:
                t = jnp.where(rows == sy - 1, yhi[base + (cx + 1) * 3 + cz + 1, pl.ds(i, 1), :], pltpu.roll(t, sy - 1, 0))
            if vz == 1:
                t = jnp.where(lanes == 0, zcol[:, i : i + 1], pltpu.roll(t, 1, 1))
            elif vz == -1:
                t = jnp.where(lanes == sz - 1, zcol[:, i : i + 1], pltpu.roll(t, sz - 1, 1))
            dst[q, i] = t


def adjoint_rows(F, A, om, ga):
    rho = sum(F)
    mom = []
    for axis in range(3):
        pos = [F[q] for q in range(27) if STEPS[q, axis] == 1]
        neg = [F[q] for q in range(27) if STEPS[q, axis] == -1]
        mom.append(sum(pos) - sum(neg))
    vel = (mom[0] / rho, mom[1] / rho, mom[2] / rho)
    uu = vel[0] * vel[0] + vel[1] * vel[1] + vel[2] * vel[2]
    sens = 0.0
    e_rho = 0.0
    s0 = 0.0
    sm = [0.0, 0.0, 0.0]
    for q in range(27):
        c = STEPS[q]
        w = float(WEIGHTS[q])
        cu = None
        for axis in range(3):
            if c[axis] == 1:
                cu = vel[axis] if cu is None else cu + vel[axis]
            elif c[axis] == -1:
                cu = -vel[axis] if cu is None else cu - vel[axis]
        if cu is None:
            eq = w * rho * (1.0 - 1.5 * uu)
        else:
            eq = w * rho * (1.0 + 3.0 * cu + 4.5 * cu * cu - 1.5 * uu)
        bgk = F[q] - om * (F[q] - eq)
        sens = sens + A[q] * (F[26 - q] - bgk)
        aw = A[q] * w
        s0 = s0 + aw
        if cu is None:
            e_rho = e_rho + aw * (1.0 + 1.5 * uu)
        else:
            e_rho = e_rho + aw * (1.0 - 4.5 * cu * cu + 1.5 * uu)
            t = aw * (1.0 + 3.0 * cu)
            for axis in range(3):
                if c[axis] == 1:
                    sm[axis] = sm[axis] + t
                elif c[axis] == -1:
                    sm[axis] = sm[axis] - t
    em = [3.0 * sm[axis] - 3.0 * vel[axis] * s0 for axis in range(3)]
    keep = 1.0 - ga
    out = []
    for p in range(27):
        c = STEPS[p]
        g = e_rho
        for axis in range(3):
            if c[axis] == 1:
                g = g + em[axis]
            elif c[axis] == -1:
                g = g - em[axis]
        out.append(keep * ((1.0 - om) * A[p] + om * g) + ga * A[26 - p])
    return out, sens


def chunked_adjoint(f_ref, a_ref, rate_ref, gamma_ref, out_ref, sens_ref):
    _, sx, sy, sz = out_ref.shape
    halves = sy // 8

    def body(step, carry):
        i = step // halves
        h = pl.multiple_of((step % halves) * 8, 8)
        F = [f_ref[q, i, pl.ds(h, 8), :] for q in range(27)]
        A = [a_ref[q, i, pl.ds(h, 8), :] for q in range(27)]
        om = rate_ref[i, pl.ds(h, 8), :]
        ga = gamma_ref[i, pl.ds(h, 8), :]
        adj, sens = adjoint_rows(F, A, om, ga)
        for q in range(27):
            out_ref[q, i, pl.ds(h, 8), :] = adj[q]
        sens_ref[i, pl.ds(h, 8), :] = sens
        return carry

    lax.fori_loop(0, sx * halves, body, 0)


def next_kernel(cf_ref, ae_ref, *refs):
    hal = refs[0:6]
    rate_ref, gamma_ref, out_ref, sens_ref, fs, as_ = refs[6:]
    move_into(fs, cf_ref, hal, 1, 0)
    move_into(as_, ae_ref, hal, -1, 9)
    chunked_adjoint(fs, as_, rate_ref, gamma_ref, out_ref, sens_ref)


def now_kernel(an_ref, f_ref, *refs):
    hal = refs[0:6]
    rate_ref, gamma_ref, out_ref, sens_ref, as_ = refs[6:]
    move_into(as_, an_ref, hal, -1, 0)
    chunked_adjoint(f_ref, as_, rate_ref, gamma_ref, out_ref, sens_ref)


def run_stage(kernel, args, shape, scratch):
    _, sx, sy, sz = shape
    return pl.pallas_call(
        kernel,
        out_shape=(
            jax.ShapeDtypeStruct(shape, jnp.float32),
            jax.ShapeDtypeStruct((sx, sy, sz), jnp.float32),
        ),
        scratch_shapes=[pltpu.VMEM(shape, jnp.float32) for _ in range(scratch)],
    )(*args)


def shards(check_pops, adjoint_end, relax_rate, wall_flag, patch_of_cell, porosity, patch_slot):
    sx, sy, sz = relax_rate.shape
    ids = patch_of_cell[:, :: sy // 2, :: sz // 2]
    table = jnp.stack([porosity, patch_slot.astype(jnp.float32)], axis=1)
    looked = table[ids]
    solid = jnp.broadcast_to(looked[:, :, None, :, None, 0], (sx, 2, sy // 2, 2, sz // 2)).reshape(sx, sy, sz)
    walls = wall_flag.astype(jnp.float32)
    gamma = walls * solid
    post_now, _ = collide(check_pops, relax_rate, gamma)
    hal = halos([post_now, adjoint_end], [1, -1])
    shape = check_pops.shape
    adj_next, sens_next = run_stage(
        next_kernel, (post_now, adjoint_end) + hal + (relax_rate, gamma), shape, 2
    )
    hal_n = halos([adj_next], [-1])
    adjoint_start, sens_now = run_stage(now_kernel, (adj_next, check_pops) + hal_n + (relax_rate, gamma), shape, 1)
    density = walls * (sens_next + sens_now)
    boxes = density.reshape(sx, 2, sy // 2, 2, sz // 2).sum(axis=(2, 4))
    parts = jnp.stack([boxes[0], boxes[1 : sx - 1].sum(axis=0), boxes[sx - 1]])
    count = porosity.shape[0]
    devices = lax.axis_size(("gx", "gy", "gz"))
    slots = jnp.stack([looked[0, :, :, 1], looked[1, :, :, 1], looked[sx - 1, :, :, 1]]).reshape(-1)
    hits = (slots[:, None] == jnp.arange(count, dtype=jnp.float32)[None, :]).astype(jnp.float32)
    placed = jnp.sum(parts.reshape(-1)[:, None] * hits, axis=0)
    got = lax.all_to_all(placed.reshape(devices, count // devices), ("gx", "gy", "gz"), 0, 0, tiled=True)
    patch_sens = jnp.sum(got, axis=0)
    return (adjoint_start, patch_sens)


def solution(mesh):
    in_specs = (
        P(None, "gx", "gy", "gz"),
        P(None, "gx", "gy", "gz"),
        P("gx", "gy", "gz"),
        P("gx", "gy", "gz"),
        P("gx", "gy", "gz"),
        P(),
        P(),
    )
    out_specs = (P(None, "gx", "gy", "gz"), P(("gx", "gy", "gz")))
    return jax.shard_map(shards, mesh=mesh, in_specs=in_specs, out_specs=out_specs, check_vma=False)
```
